32 devices in a mesh: src: 8 (over z, core), dst: 4 (over y, x).
Axes of the slice: x: 2, y: 2, z: 4, core: 2. Of those that a mesh axis runs over, the one named last changes fastest.
Arguments:
- teleport: float32 [16, 4, 8192], P(None, 'dst', 'src'), may hold values from 0.1 to 10
- tiles: bfloat16 [4, 8, 128, 256, 256], P('dst', 'src')
- tile_rows: int32 [4, 8, 128], P('dst', 'src'), may hold values from 0 to 31
- tile_cols: int32 [4, 8, 128], P('dst', 'src'), may hold values from 0 to 15
- tile_counts: int32 [4, 8], P('dst', 'src'), may hold values from 32 to 128, as said below
- dangling: int32 [128], replicated, may hold values 0 or 1
- agg_of_block: int32 [128], replicated, may hold values from 0 to 63, as said below
- owner_list: int32 [64], replicated, may hold values from 0 to 63, each once
Outputs:
- fine_out: float32 [16, 4, 8192], P(None, 'dst', 'src')
- coarse_out: float32 [16, 64], P(None, ('src', 'dst'))
The draws below stay inside these ranges and needn't reach their ends.
Inputs may be any that keep to these rules, and one draw needn't show every extreme that they name: `tile_counts`: slots 0 to count - 1 of a group pair's list hold its tiles, later slots are unused; some group pair fills all 128 slots. `agg_of_block`: every aggregate holds at least one block. `owner_list`: each aggregate appears once.
All inputs are finite; a program needn't handle non-finite values.
Results may differ from the reference program's by a relative error of at most 0.0003.
Values may be sent and summed in bfloat16 or wider, within the bound.
No kernel may reach another device: no remote copies, remote signals or barrier semaphores. Data moves between devices by JAX's collectives and lax.ppermute only.
A program may use at most 192 MiB of HBM per device.

```python
import math
import jax
import jax.numpy as jnp
from jax import lax

K = 16
TB = 256
M = 4
TILES_DEV = 128
ROWGRP = 4
COLGRP = 8
NB = 128
RBG = 32
CBG = 16
RANGE = 8192
PAGES = 32768
AGG = 64


def draw_tiles(key, part):
    shape = (ROWGRP, COLGRP, TILES_DEV, TB, TB)
    base = jax.random.uniform(key, shape, jnp.float32)
    values = base * base * base * (8.0 * M / (TB * TILES_DEV))
    return values.astype(jnp.bfloat16)


def draw_tile_counts(key, part):
    first_key, second_key, third_key = jax.random.split(key, 3)
    base = jax.random.randint(first_key, (ROWGRP, COLGRP), TILES_DEV // 4, TILES_DEV // 2 + 1)
    full_mask = jax.random.randint(second_key, (ROWGRP, COLGRP), 0, 8) == 0
    picked = jax.random.randint(third_key, (), 0, ROWGRP * COLGRP)
    forced = jnp.arange(ROWGRP * COLGRP, dtype=jnp.int32).reshape(ROWGRP, COLGRP) == picked
    return jnp.where(full_mask | forced, TILES_DEV, base).astype(jnp.int32)


def draw_agg_of_block(key, part):
    first_key, second_key = jax.random.split(key, 2)
    order = jax.random.permutation(first_key, NB)
    extra = jax.random.randint(second_key, (NB,), 0, AGG)
    placing = jnp.zeros((NB,), jnp.int32).at[order].set(jnp.arange(NB, dtype=jnp.int32))
    return jnp.where(placing < AGG, placing, extra).astype(jnp.int32)


def plant(drawn, rng, smallest, largest):
    shape = drawn.shape
    spot = [jax.random.randint(jax.random.fold_in(rng, axis), (), 0, shape[axis]) for axis in range(len(shape))]
    drawn = drawn.at[tuple(spot)].set(smallest)
    longest = shape.index(max(shape))
    spot[longest] = (spot[longest] + 1) % shape[longest]
    return drawn.at[tuple(spot)].set(largest)


def shard_levels(own_key, shape, shards, smallest, largest):
    loudness = 1.0
    for position, blocks in shards:
        draws = jax.random.uniform(jax.random.fold_in(jax.random.fold_in(own_key, 6), position), (blocks,), jnp.float32, smallest / len(shards), largest / len(shards))
        loudness = loudness * jnp.repeat(jnp.exp(draws), shape[position] // blocks).reshape((-1,) + (1,) * (len(shape) - 1 - position))
    return loudness


def setup_inputs(seed: int = 0) -> dict:
    seeds = jax.random.split(jax.random.key(seed), 9)
    return {
        "teleport": jnp.clip(jnp.exp(math.log(10.0) - 4.6051702 * jax.random.uniform(seeds[0], (K, ROWGRP, RANGE), jnp.float32) ** shard_levels(seeds[0], (K, ROWGRP, RANGE), ((1, 4), (2, 8)), -0.2, 0.2)), 0.1, 10.0),
        "tiles": draw_tiles(jax.random.fold_in(seeds[8], 71), 0),
        "tile_rows": plant(jax.random.randint(seeds[2], (ROWGRP, COLGRP, TILES_DEV), 0, RBG), jax.random.fold_in(seeds[2], 1), 0, RBG - 1).astype(jnp.int32),
        "tile_cols": plant(jax.random.randint(seeds[3], (ROWGRP, COLGRP, TILES_DEV), 0, CBG), jax.random.fold_in(seeds[3], 1), 0, CBG - 1).astype(jnp.int32),
        "tile_counts": draw_tile_counts(jax.random.fold_in(seeds[8], 71), 0),
        "dangling": plant((jax.random.randint(seeds[5], (NB,), 0, 8) < 1).astype(jnp.int32), jax.random.fold_in(seeds[5], 1), 0, 1),
        "agg_of_block": draw_agg_of_block(jax.random.fold_in(seeds[8], 71), 0),
        "owner_list": jax.random.permutation(seeds[7], AGG).astype(jnp.int32),
    }


damping = 0.85
highest = lax.Precision.HIGHEST


def tile_layout(tile_rows, tile_cols, tile_counts, dangling):
    dst_ids = jnp.arange(ROWGRP, dtype=jnp.int32)[:, None, None]
    src_ids = jnp.arange(COLGRP, dtype=jnp.int32)[None, :, None]
    row_global = dst_ids * RBG + tile_rows
    col_global = (tile_cols // M) * (M * COLGRP) + src_ids * M + tile_cols % M
    slot_ids = jnp.arange(TILES_DEV, dtype=jnp.int32)[None, None, :]
    live_mask = (slot_ids < tile_counts[:, :, None]) & (dangling[col_global] == 0)
    weights = jnp.where(live_mask, 1.0, 0.0).astype(jnp.float32)
    return row_global.reshape(-1).astype(jnp.int32), col_global.reshape(-1).astype(jnp.int32), weights.reshape(-1)


def block_major(field):
    return jnp.transpose(field.reshape(K, NB, TB), (1, 0, 2))


def apply_chain(field, tiles, row_global, col_global, weights):
    rounded = block_major(field).astype(jnp.bfloat16)
    flat_tiles = tiles.reshape(ROWGRP * COLGRP, TILES_DEV, TB, TB)

    def one_device(accumulated, device_item):
        tile_set, rows_here, cols_here, weights_here = device_item
        chosen = rounded[cols_here].astype(jnp.float32) * weights_here[:, None, None]
        product = jnp.einsum("tkj,tji->tki", chosen, tile_set.astype(jnp.float32))
        return accumulated.at[rows_here].add(product), None

    start_sum = jnp.zeros((NB, K, TB), jnp.float32)
    result, _ = lax.scan(one_device, start_sum, (flat_tiles, row_global.reshape(-1, TILES_DEV), col_global.reshape(-1, TILES_DEV), weights.reshape(-1, TILES_DEV)))
    return jnp.transpose(result, (1, 0, 2)).reshape(K, ROWGRP, RANGE)


def relaxation(field, teleport, tiles, layout, block_dangling):
    row_global, col_global, weights = layout
    image_field = apply_chain(field, tiles, row_global, col_global, weights)
    lost_sum = jnp.sum(field.reshape(K, NB, TB) * block_dangling[None, :, None], axis=(1, 2))
    return damping * (image_field + (lost_sum / PAGES)[:, None, None] * teleport) + (1.0 - damping) * teleport


def coarse_level(field, teleport, tiles, layout, block_dangling, agg_of_block, owner_list):
    row_global, col_global, weights = layout
    agg_hot = (agg_of_block[:, None] == jnp.arange(AGG, dtype=jnp.int32)[None, :]).astype(jnp.float32)
    block_sums = jnp.sum(field.reshape(K, NB, TB), axis=2)
    totals = jnp.dot(block_sums, agg_hot, precision=highest)
    lost_mass = jnp.dot(block_sums * block_dangling[None, :], agg_hot, precision=highest)
    weight = jnp.dot(jnp.sum(teleport.reshape(K, NB, TB), axis=2), agg_hot, precision=highest)
    rounded = lax.optimization_barrier(block_major(field).astype(jnp.bfloat16)).astype(jnp.float32)
    flat_tiles = tiles.reshape(ROWGRP * COLGRP, TILES_DEV, TB, TB)

    def device_entries(device_item):
        tile_set, cols_here, weights_here = device_item
        sums_here = jnp.sum(tile_set.astype(jnp.float32), axis=2)
        chosen = rounded[cols_here] * weights_here[:, None, None]
        return jnp.einsum("tkj,tj->tk", chosen, sums_here, precision=highest)

    entries = lax.map(device_entries, (flat_tiles, col_global.reshape(-1, TILES_DEV), weights.reshape(-1, TILES_DEV))).reshape(-1, K)
    flat_index = agg_of_block[row_global] * AGG + agg_of_block[col_global]
    coupling = jax.ops.segment_sum(entries, flat_index, num_segments=AGG * AGG).reshape(AGG, AGG, K)

    def coarse_sweep(ratios):
        inflow = jnp.einsum("abk,kb->ka", coupling, ratios, precision=highest)
        carried = jnp.sum(lost_mass * ratios, axis=1)
        return damping * (inflow + (carried / PAGES)[:, None] * weight) + (1.0 - damping) * weight

    level_one = coarse_sweep(jnp.ones((K, AGG), jnp.float32))
    level_two = coarse_sweep(level_one / totals)
    rescale = jnp.dot(level_two / totals, agg_hot.T, precision=highest)
    corrected = field.reshape(K, NB, TB) * rescale[:, :, None]
    return corrected.reshape(K, ROWGRP, RANGE), level_two[:, owner_list]


def reference(teleport, tiles, tile_rows, tile_cols, tile_counts, dangling, agg_of_block, owner_list):
    layout = tile_layout(tile_rows, tile_cols, tile_counts, dangling)
    block_dangling = dangling.astype(jnp.float32)
    relaxed_one = relaxation(teleport, teleport, tiles, layout, block_dangling)
    relaxed_two = relaxation(relaxed_one, teleport, tiles, layout, block_dangling)
    corrected, coarse_out = coarse_level(relaxed_two, teleport, tiles, layout, block_dangling, agg_of_block, owner_list)
    relaxed_three = relaxation(corrected, teleport, tiles, layout, block_dangling)
    return relaxation(relaxed_three, teleport, tiles, layout, block_dangling), coarse_out
```

```python
import functools

import jax
import jax.numpy as jnp
from jax import lax
from jax.experimental import pallas as pl
from jax.experimental.pallas import tpu as pltpu
from jax.sharding import PartitionSpec as P

damping = 0.85
group_size = 8
highest = lax.Precision.HIGHEST


def tile_kernel(mode, rows_ref, cols_ref, live_ref, nb_ref, x_ref, t_ref, o_ref):
    step = pl.program_id(0)
    if mode == "image":

        @pl.when(step == 0)
        def _():
            o_ref[...] = jnp.zeros_like(o_ref)

    for g in range(group_size):
        slot = step * group_size + g
        live = live_ref[slot] != 0

        @pl.when(live)
        def _():
            product = jnp.dot(
                x_ref[cols_ref[slot]], t_ref[g], preferred_element_type=jnp.float32
            )
            if mode == "image":
                row = rows_ref[slot]
                o_ref[row] = o_ref[row] + product
            else:
                row_sum = jnp.sum(product, axis=1, keepdims=True)
                o_ref[g] = jnp.broadcast_to(row_sum, o_ref.shape[1:])

        if mode == "entries":

            @pl.when(jnp.logical_not(live))
            def _():
                o_ref[g] = jnp.zeros(o_ref.shape[1:], o_ref.dtype)


def tile_pass(mode, x_cols, tiles, rows, cols, live, block_count, row_blocks):
    col_blocks, vectors, side = x_cols.shape
    slots = tiles.shape[2]
    steps = slots // group_size

    def tile_index(i, rows_ref, cols_ref, live_ref, nb_ref):
        return (0, 0, jnp.minimum(i, nb_ref[0] - 1), 0, 0)

    if mode == "image":
        out_shape = jax.ShapeDtypeStruct((row_blocks, vectors, side), jnp.float32)
        out_spec = pl.BlockSpec((row_blocks, vectors, side), lambda i, *_: (0, 0, 0))
    else:
        out_shape = jax.ShapeDtypeStruct((slots, vectors, 128), jnp.float32)
        out_spec = pl.BlockSpec((group_size, vectors, 128), lambda i, *_: (i, 0, 0))
    grid_spec = pltpu.PrefetchScalarGridSpec(
        num_scalar_prefetch=4,
        grid=(steps,),
        in_specs=[
            pl.BlockSpec((col_blocks, vectors, side), lambda i, *_: (0, 0, 0)),
            pl.BlockSpec((None, None, group_size, side, side), tile_index),
        ],
        out_specs=out_spec,
    )
    return pl.pallas_call(
        functools.partial(tile_kernel, mode),
        grid_spec=grid_spec,
        out_shape=out_shape,
        compiler_params=pltpu.CompilerParams(dimension_semantics=("arbitrary",)),
    )(rows, cols, live, block_count, x_cols, tiles)


def per_device(
    teleport, tiles, tile_rows, tile_cols, tile_counts, dangling, agg_of_block, owner_list
):
    vectors = teleport.shape[0]
    piece_width = teleport.shape[2]
    slots_total = tiles.shape[2]
    tile_side = tiles.shape[4]
    blocks_piece = piece_width // tile_side
    src_count = lax.axis_size("src")
    dst_count = lax.axis_size("dst")
    row_blocks = blocks_piece * src_count
    col_blocks = blocks_piece * dst_count
    page_total = row_blocks * dst_count * tile_side
    agg_count = owner_list.shape[0]
    src_index = lax.axis_index("src")
    dst_index = lax.axis_index("dst")
    own_rows = jnp.clip(tile_rows[0, 0], 0, row_blocks - 1)
    own_cols = jnp.clip(tile_cols[0, 0], 0, col_blocks - 1)
    own_count = tile_counts[0, 0]
    col_global = (
        own_cols // blocks_piece * (blocks_piece * src_count)
        + src_index * blocks_piece
        + own_cols % blocks_piece
    )
    row_global = dst_index * row_blocks + own_rows
    slot_range = jnp.arange(slots_total, dtype=jnp.int32)
    live_mask = ((slot_range < own_count) & (dangling[col_global] == 0)).astype(jnp.int32)
    steps = slots_total // group_size
    block_count = jnp.clip((own_count + group_size - 1) // group_size, 1, steps).reshape(1)
    block_count = block_count.astype(jnp.int32)
    piece_first = dst_index * row_blocks + src_index * blocks_piece
    piece_dangling = lax.dynamic_slice_in_dim(dangling, piece_first, blocks_piece).astype(
        jnp.float32
    )
    piece_agg = lax.dynamic_slice_in_dim(agg_of_block, piece_first, blocks_piece)
    agg_range = jnp.arange(agg_count, dtype=jnp.int32)
    piece_hot = (piece_agg[:, None] == agg_range[None, :]).astype(jnp.float32)
    tele = jnp.transpose(teleport.reshape(vectors, blocks_piece, tile_side), (1, 0, 2))

    def spread_columns(blocks):
        return lax.all_gather(blocks.astype(jnp.bfloat16), "dst", axis=0, tiled=True)

    def reduce_rows(accumulated):
        n = src_count
        if n % 2 == 0 and n > 1:
            half = n // 2
            chunks = accumulated.reshape(half, 2, blocks_piece, vectors, tile_side)
            core = src_index % 2
            keep = lax.dynamic_index_in_dim(chunks, core, 1, keepdims=False)
            give = lax.dynamic_index_in_dim(chunks, 1 - core, 1, keepdims=False)
            got = lax.ppermute(give, "src", [(i, i ^ 1) for i in range(n)])
            part = keep + got
            chip = src_index // 2
            total = lax.dynamic_index_in_dim(part, chip, 0, keepdims=False)
            for shift in range(1, half):
                send = lax.dynamic_index_in_dim(part, (chip + shift) % half, 0, keepdims=False)
                pairs = [(i, ((i // 2 + shift) % half) * 2 + i % 2) for i in range(n)]
                total = total + lax.ppermute(send, "src", pairs)
            return total
        chunks = accumulated.reshape(n, blocks_piece, vectors, tile_side)
        total = lax.dynamic_index_in_dim(chunks, src_index, 0, keepdims=False)
        for shift in range(1, n):
            send = lax.dynamic_index_in_dim(chunks, (src_index + shift) % n, 0, keepdims=False)
            total = total + lax.ppermute(send, "src", [(i, (i + shift) % n) for i in range(n)])
        return total

    def lost_partial(blocks):
        return jnp.sum(blocks * piece_dangling[:, None, None], axis=(0, 2))

    def relaxation(blocks, lost_sum):
        gathered = spread_columns(blocks)
        accumulated = tile_pass(
            "image", gathered, tiles, own_rows, own_cols, live_mask, block_count, row_blocks
        )
        image = reduce_rows(accumulated)
        return (
            damping * (image + (lost_sum / page_total)[None, :, None] * tele)
            + (1.0 - damping) * tele
        )

    tele_sums = jnp.sum(tele, axis=2)
    weight_partial = jnp.einsum("bk,ba->ka", tele_sums, piece_hot, precision=highest)
    start_sums = lax.psum(
        jnp.concatenate([lost_partial(tele)[:, None], weight_partial], axis=1), ("src", "dst")
    )
    lost_zero = start_sums[:, 0]
    weight = start_sums[:, 1:]

    relaxed_one = relaxation(tele, lost_zero)
    lost_one = lax.psum(lost_partial(relaxed_one), ("src", "dst"))
    relaxed_two = relaxation(relaxed_one, lost_one)

    gathered = spread_columns(relaxed_two)
    entries = tile_pass(
        "entries", gathered, tiles, own_rows, own_cols, live_mask, block_count, row_blocks
    )[:, :, 0]
    block_sums = jnp.sum(relaxed_two, axis=2)
    totals_partial = jnp.einsum("bk,ba->ka", block_sums, piece_hot, precision=highest)
    lost_mass_partial = jnp.einsum(
        "bk,ba->ka", block_sums * piece_dangling[:, None], piece_hot, precision=highest
    )
    row_agg = agg_of_block[row_global]
    col_agg = agg_of_block[col_global]
    row_hot = (row_agg[:, None] == agg_range[None, :]).astype(jnp.float32)
    col_hot = (col_agg[:, None] == agg_range[None, :]).astype(jnp.float32)
    inflow_partial = jnp.einsum("tk,ta->ka", entries, row_hot, precision=highest)
    inflow_one, totals, lost_mass = lax.psum(
        jnp.stack([inflow_partial, totals_partial, lost_mass_partial]), ("src", "dst")
    )

    def coarse_sweep(inflow, ratios):
        carried = jnp.sum(lost_mass * ratios, axis=1)
        return (
            damping * (inflow + (carried / page_total)[:, None] * weight)
            + (1.0 - damping) * weight
        )

    level_one = coarse_sweep(inflow_one, jnp.ones((vectors, agg_count), jnp.float32))
    ratios_one = level_one / totals
    ratio_at_tile = jnp.einsum("ka,ta->tk", ratios_one, col_hot, precision=highest)
    inflow_two = lax.psum(
        jnp.einsum("tk,ta->ka", entries * ratio_at_tile, row_hot, precision=highest),
        ("src", "dst"),
    )
    level_two = coarse_sweep(inflow_two, ratios_one)
    ratios_two = level_two / totals
    rescale = jnp.einsum("ka,ba->bk", ratios_two, piece_hot, precision=highest)
    corrected = relaxed_two * rescale[:, :, None]
    lost_two = jnp.sum(lost_mass * ratios_two, axis=1)

    position = lax.axis_index(("src", "dst"))
    owned_count = agg_count // (src_count * dst_count)
    owned = lax.dynamic_slice_in_dim(owner_list, position * owned_count, owned_count)
    owned_hot = (owned[:, None] == agg_range[None, :]).astype(jnp.float32)
    coarse_out = jnp.einsum("ka,qa->kq", level_two, owned_hot, precision=highest)

    relaxed_three = relaxation(corrected, lost_two)
    lost_three = lax.psum(lost_partial(relaxed_three), ("src", "dst"))
    relaxed_four = relaxation(relaxed_three, lost_three)
    fine_out = jnp.transpose(relaxed_four, (1, 0, 2)).reshape(teleport.shape)
    return fine_out, coarse_out


def solution(mesh):
    placed = (
        P(None, "dst", "src"),
        P("dst", "src", None, None, None),
        P("dst", "src", None),
        P("dst", "src", None),
        P("dst", "src"),
        P(),
        P(),
        P(),
    )
    return jax.shard_map(
        per_device,
        mesh=mesh,
        in_specs=placed,
        out_specs=(P(None, "dst", "src"), P(None, ("src", "dst"))),
        check_vma=False,
    )
```

```python
import functools

import jax
import jax.numpy as jnp
from jax import lax
from jax.experimental import pallas as pl
from jax.experimental.pallas import tpu as pltpu
from jax.sharding import PartitionSpec as P

damping = 0.85
group_size = 8
highest = lax.Precision.HIGHEST


def tile_kernel(mode, rows_ref, cols_ref, live_ref, nb_ref, x_ref, t_ref, o_ref):
    step = pl.program_id(0)
    if mode == "image":

        @pl.when(step == 0)
        def _():
            o_ref[...] = jnp.zeros_like(o_ref)

    for g in range(group_size):
        slot = step * group_size + g
        live = live_ref[slot] != 0

        @pl.when(live)
        def _():
            product = jnp.dot(
                x_ref[cols_ref[slot]], t_ref[g], preferred_element_type=jnp.float32
            )
            if mode == "image":
                row = rows_ref[slot]
                o_ref[row] = o_ref[row] + product
            else:
                row_sum = jnp.sum(product, axis=1, keepdims=True)
                o_ref[g] = jnp.broadcast_to(row_sum, o_ref.shape[1:])

        if mode == "entries":

            @pl.when(jnp.logical_not(live))
            def _():
                o_ref[g] = jnp.zeros(o_ref.shape[1:], o_ref.dtype)


def tile_pass(mode, x_cols, tiles, rows, cols, live, block_count, row_blocks):
    col_blocks, vectors, side = x_cols.shape
    slots = tiles.shape[2]
    steps = slots // group_size

    def tile_index(i, rows_ref, cols_ref, live_ref, nb_ref):
        return (0, 0, jnp.minimum(i, nb_ref[0] - 1), 0, 0)

    if mode == "image":
        out_shape = jax.ShapeDtypeStruct((row_blocks, vectors, side), jnp.float32)
        out_spec = pl.BlockSpec((row_blocks, vectors, side), lambda i, *_: (0, 0, 0))
    else:
        out_shape = jax.ShapeDtypeStruct((slots, vectors, 128), jnp.float32)
        out_spec = pl.BlockSpec((group_size, vectors, 128), lambda i, *_: (i, 0, 0))
    grid_spec = pltpu.PrefetchScalarGridSpec(
        num_scalar_prefetch=4,
        grid=(steps,),
        in_specs=[
            pl.BlockSpec((col_blocks, vectors, side), lambda i, *_: (0, 0, 0)),
            pl.BlockSpec((None, None, group_size, side, side), tile_index),
        ],
        out_specs=out_spec,
    )
    return pl.pallas_call(
        functools.partial(tile_kernel, mode),
        grid_spec=grid_spec,
        out_shape=out_shape,
        compiler_params=pltpu.CompilerParams(dimension_semantics=("arbitrary",)),
    )(rows, cols, live, block_count, x_cols, tiles)


def per_device(
    teleport, tiles, tile_rows, tile_cols, tile_counts, dangling, agg_of_block, owner_list
):
    vectors = teleport.shape[0]
    piece_width = teleport.shape[2]
    slots_total = tiles.shape[2]
    tile_side = tiles.shape[4]
    blocks_piece = piece_width // tile_side
    src_count = lax.axis_size("src")
    dst_count = lax.axis_size("dst")
    row_blocks = blocks_piece * src_count
    col_blocks = blocks_piece * dst_count
    page_total = row_blocks * dst_count * tile_side
    agg_count = owner_list.shape[0]
    src_index = lax.axis_index("src")
    dst_index = lax.axis_index("dst")
    own_rows = jnp.clip(tile_rows[0, 0], 0, row_blocks - 1)
    own_cols = jnp.clip(tile_cols[0, 0], 0, col_blocks - 1)
    own_count = tile_counts[0, 0]
    col_global = (
        own_cols // blocks_piece * (blocks_piece * src_count)
        + src_index * blocks_piece
        + own_cols % blocks_piece
    )
    row_global = dst_index * row_blocks + own_rows
    slot_range = jnp.arange(slots_total, dtype=jnp.int32)
    live_mask = ((slot_range < own_count) & (dangling[col_global] == 0)).astype(jnp.int32)
    steps = slots_total // group_size
    block_count = jnp.clip((own_count + group_size - 1) // group_size, 1, steps).reshape(1)
    block_count = block_count.astype(jnp.int32)
    piece_first = dst_index * row_blocks + src_index * blocks_piece
    piece_dangling = lax.dynamic_slice_in_dim(dangling, piece_first, blocks_piece).astype(
        jnp.float32
    )
    piece_agg = lax.dynamic_slice_in_dim(agg_of_block, piece_first, blocks_piece)
    agg_range = jnp.arange(agg_count, dtype=jnp.int32)
    piece_hot = (piece_agg[:, None] == agg_range[None, :]).astype(jnp.float32)
    tele = jnp.transpose(teleport.reshape(vectors, blocks_piece, tile_side), (1, 0, 2))

    all_axes = ("src", "dst")
    all_count = src_count * dst_count

    def tree_sum(value, axis, size):
        if size & (size - 1):
            return lax.psum(value, axis)
        shift = 1
        while shift < size:
            value = value + lax.ppermute(value, axis, [(i, i ^ shift) for i in range(size)])
            shift *= 2
        return value

    exchange = dst_count & (dst_count - 1) == 0
    if exchange:
        kernel_cols = (
            (own_cols // blocks_piece) ^ dst_index
        ) * blocks_piece + own_cols % blocks_piece
    else:
        kernel_cols = own_cols

    def spread_columns(blocks):
        rounded = blocks.astype(jnp.bfloat16)
        if not exchange:
            return lax.all_gather(rounded, "dst", axis=0, tiled=True)
        pieces = [rounded] + [
            lax.ppermute(rounded, "dst", [(i, i ^ v) for i in range(dst_count)])
            for v in range(1, dst_count)
        ]
        return jnp.concatenate(pieces, axis=0)

    def reduce_rows(accumulated, lost):
        n = src_count
        if n % 2 == 0 and n > 1:
            half = n // 2
            chunks = accumulated.reshape(half, 2, blocks_piece, vectors, tile_side)
            core = src_index % 2
            keep = lax.dynamic_index_in_dim(chunks, core, 1, keepdims=False)
            give = lax.dynamic_index_in_dim(chunks, 1 - core, 1, keepdims=False)
            got, got_lost = lax.ppermute((give, lost), "src", [(i, i ^ 1) for i in range(n)])
            part = keep + got
            lost_part = lost + got_lost
            chip = src_index // 2
            total = lax.dynamic_index_in_dim(part, chip, 0, keepdims=False)
            lost_total = lost_part
            for shift in range(1, half):
                send = lax.dynamic_index_in_dim(part, (chip + shift) % half, 0, keepdims=False)
                pairs = [(i, ((i // 2 + shift) % half) * 2 + i % 2) for i in range(n)]
                got, got_lost = lax.ppermute((send, lost_part), "src", pairs)
                total = total + got
                lost_total = lost_total + got_lost
            return total, lost_total
        chunks = accumulated.reshape(n, blocks_piece, vectors, tile_side)
        total = lax.dynamic_index_in_dim(chunks, src_index, 0, keepdims=False)
        lost_total = lost
        for shift in range(1, n):
            send = lax.dynamic_index_in_dim(chunks, (src_index + shift) % n, 0, keepdims=False)
            pairs = [(i, (i + shift) % n) for i in range(n)]
            got, got_lost = lax.ppermute((send, lost), "src", pairs)
            total = total + got
            lost_total = lost_total + got_lost
        return total, lost_total

    def lost_partial(blocks):
        return jnp.sum(blocks * piece_dangling[:, None, None], axis=(0, 2))

    def relaxation(blocks, lost_sum=None):
        if lost_sum is None:
            lost_dst = tree_sum(lost_partial(blocks), "dst", dst_count)
        gathered = spread_columns(blocks)
        accumulated = tile_pass(
            "image", gathered, tiles, own_rows, kernel_cols, live_mask, block_count, row_blocks
        )
        if lost_sum is None:
            image, lost_sum = reduce_rows(accumulated, lost_dst)
        else:
            image, _ = reduce_rows(accumulated, jnp.zeros((vectors,), jnp.float32))
        return (
            damping * (image + (lost_sum / page_total)[None, :, None] * tele)
            + (1.0 - damping) * tele
        )

    tele_sums = jnp.sum(tele, axis=2)
    weight_partial = jnp.einsum("bk,ba->ka", tele_sums, piece_hot, precision=highest)

    relaxed_one = relaxation(tele)
    relaxed_two = relaxation(relaxed_one)

    gathered = spread_columns(relaxed_two)
    entries = tile_pass(
        "entries", gathered, tiles, own_rows, kernel_cols, live_mask, block_count, row_blocks
    )[:, :, 0]
    block_sums = jnp.sum(relaxed_two, axis=2)
    totals_partial = jnp.einsum("bk,ba->ka", block_sums, piece_hot, precision=highest)
    lost_mass_partial = jnp.einsum(
        "bk,ba->ka", block_sums * piece_dangling[:, None], piece_hot, precision=highest
    )
    row_agg = agg_of_block[row_global]
    col_agg = agg_of_block[col_global]
    row_hot = (row_agg[:, None] == agg_range[None, :]).astype(jnp.float32)
    col_hot = (col_agg[:, None] == agg_range[None, :]).astype(jnp.float32)
    inflow_partial = jnp.einsum("tk,ta->ka", entries, row_hot, precision=highest)
    inflow_one, totals, lost_mass, weight = tree_sum(
        jnp.stack([inflow_partial, totals_partial, lost_mass_partial, weight_partial]),
        all_axes,
        all_count,
    )

    def coarse_sweep(inflow, ratios):
        carried = jnp.sum(lost_mass * ratios, axis=1)
        return (
            damping * (inflow + (carried / page_total)[:, None] * weight)
            + (1.0 - damping) * weight
        )

    level_one = coarse_sweep(inflow_one, jnp.ones((vectors, agg_count), jnp.float32))
    ratios_one = level_one / totals
    ratio_at_tile = jnp.einsum("ka,ta->tk", ratios_one, col_hot, precision=highest)
    inflow_two = tree_sum(
        jnp.einsum("tk,ta->ka", entries * ratio_at_tile, row_hot, precision=highest),
        all_axes,
        all_count,
    )
    level_two = coarse_sweep(inflow_two, ratios_one)
    ratios_two = level_two / totals
    rescale = jnp.einsum("ka,ba->bk", ratios_two, piece_hot, precision=highest)
    corrected = relaxed_two * rescale[:, :, None]
    lost_two = jnp.sum(lost_mass * ratios_two, axis=1)

    position = lax.axis_index(all_axes)
    owned_count = agg_count // (src_count * dst_count)
    owned = lax.dynamic_slice_in_dim(owner_list, position * owned_count, owned_count)
    owned_hot = (owned[:, None] == agg_range[None, :]).astype(jnp.float32)
    coarse_out = jnp.einsum("ka,qa->kq", level_two, owned_hot, precision=highest)

    relaxed_three = relaxation(corrected, lost_two)
    relaxed_four = relaxation(relaxed_three)
    fine_out = jnp.transpose(relaxed_four, (1, 0, 2)).reshape(teleport.shape)
    return fine_out, coarse_out


def solution(mesh):
    placed = (
        P(None, "dst", "src"),
        P("dst", "src", None, None, None),
        P("dst", "src", None),
        P("dst", "src", None),
        P("dst", "src"),
        P(),
        P(),
        P(),
    )
    return jax.shard_map(
        per_device,
        mesh=mesh,
        in_specs=placed,
        out_specs=(P(None, "dst", "src"), P(None, ("src", "dst"))),
        check_vma=False,
    )
```

```python
import functools

import jax
import jax.numpy as jnp
from jax import lax
from jax.experimental import pallas as pl
from jax.experimental.pallas import tpu as pltpu
from jax.sharding import PartitionSpec as P

damping = 0.85
group_size = 8
highest = lax.Precision.HIGHEST


def tile_kernel(mode, blocks_piece, rows_ref, cols_ref, live_ref, nb_ref, x_ref, t_ref, o_ref):
    step = pl.program_id(0)
    vectors = o_ref.shape[1]
    if mode == "image":

        @pl.when(step == 0)
        def _():
            o_ref[...] = jnp.zeros_like(o_ref)

    for g in range(group_size):
        slot = step * group_size + g
        live = live_ref[slot] != 0

        @pl.when(live)
        def _():
            col = cols_ref[slot]
            start = pl.multiple_of((col % blocks_piece) * vectors, vectors)
            picked = x_ref[col // blocks_piece, pl.ds(start, vectors), :]
            product = jnp.dot(
                picked.astype(jnp.bfloat16), t_ref[g], preferred_element_type=jnp.float32
            )
            if mode == "image":
                row = rows_ref[slot]
                o_ref[row] = o_ref[row] + product
            else:
                row_sum = jnp.sum(product, axis=1, keepdims=True)
                o_ref[g] = jnp.broadcast_to(row_sum, o_ref.shape[1:])

        if mode == "entries":

            @pl.when(jnp.logical_not(live))
            def _():
                o_ref[g] = jnp.zeros(o_ref.shape[1:], o_ref.dtype)


def tile_pass(mode, x_cols, tiles, rows, cols, live, block_count, row_blocks, vectors):
    groups, payload_rows, side = x_cols.shape
    slots = tiles.shape[2]
    steps = slots // group_size

    def tile_index(i, rows_ref, cols_ref, live_ref, nb_ref):
        return (0, 0, jnp.minimum(i, nb_ref[0] - 1), 0, 0)

    if mode == "image":
        out_shape = jax.ShapeDtypeStruct((row_blocks, vectors, side), jnp.float32)
        out_spec = pl.BlockSpec((row_blocks, vectors, side), lambda i, *_: (0, 0, 0))
    else:
        out_shape = jax.ShapeDtypeStruct((slots, vectors, 128), jnp.float32)
        out_spec = pl.BlockSpec((group_size, vectors, 128), lambda i, *_: (i, 0, 0))
    grid_spec = pltpu.PrefetchScalarGridSpec(
        num_scalar_prefetch=4,
        grid=(steps,),
        in_specs=[
            pl.BlockSpec((groups, payload_rows, side), lambda i, *_: (0, 0, 0)),
            pl.BlockSpec((None, None, group_size, side, side), tile_index),
        ],
        out_specs=out_spec,
    )
    return pl.pallas_call(
        functools.partial(tile_kernel, mode, payload_rows // vectors),
        grid_spec=grid_spec,
        out_shape=out_shape,
        compiler_params=pltpu.CompilerParams(dimension_semantics=("arbitrary",)),
    )(rows, cols, live, block_count, x_cols, tiles)


def per_device(
    teleport, tiles, tile_rows, tile_cols, tile_counts, dangling, agg_of_block, owner_list
):
    vectors = teleport.shape[0]
    piece_width = teleport.shape[2]
    slots_total = tiles.shape[2]
    tile_side = tiles.shape[4]
    blocks_piece = piece_width // tile_side
    src_count = lax.axis_size("src")
    dst_count = lax.axis_size("dst")
    row_blocks = blocks_piece * src_count
    col_blocks = blocks_piece * dst_count
    page_total = row_blocks * dst_count * tile_side
    agg_count = owner_list.shape[0]
    src_index = lax.axis_index("src")
    dst_index = lax.axis_index("dst")
    own_rows = jnp.clip(tile_rows[0, 0], 0, row_blocks - 1)
    own_cols = jnp.clip(tile_cols[0, 0], 0, col_blocks - 1)
    own_count = tile_counts[0, 0]
    col_global = (
        own_cols // blocks_piece * (blocks_piece * src_count)
        + src_index * blocks_piece
        + own_cols % blocks_piece
    )
    row_global = dst_index * row_blocks + own_rows
    slot_range = jnp.arange(slots_total, dtype=jnp.int32)
    live_mask = ((slot_range < own_count) & (dangling[col_global] == 0)).astype(jnp.int32)
    steps = slots_total // group_size
    block_count = jnp.clip((own_count + group_size - 1) // group_size, 1, steps).reshape(1)
    block_count = block_count.astype(jnp.int32)
    piece_first = dst_index * row_blocks + src_index * blocks_piece
    piece_dangling = lax.dynamic_slice_in_dim(dangling, piece_first, blocks_piece).astype(
        jnp.float32
    )
    piece_agg = lax.dynamic_slice_in_dim(agg_of_block, piece_first, blocks_piece)
    agg_range = jnp.arange(agg_count, dtype=jnp.int32)
    piece_hot = (piece_agg[:, None] == agg_range[None, :]).astype(jnp.float32)
    tele = jnp.transpose(teleport.reshape(vectors, blocks_piece, tile_side), (1, 0, 2))

    all_axes = ("src", "dst")
    all_count = src_count * dst_count

    def tree_sum(value, axis, size):
        if size & (size - 1):
            return lax.psum(value, axis)
        shift = 1
        while shift < size:
            value = value + lax.ppermute(value, axis, [(i, i ^ shift) for i in range(size)])
            shift *= 2
        return value

    exchange = dst_count & (dst_count - 1) == 0
    if exchange:
        kernel_cols = (
            (own_cols // blocks_piece) ^ dst_index
        ) * blocks_piece + own_cols % blocks_piece
    else:
        kernel_cols = own_cols

    payload_rows = blocks_piece * vectors
    pad_rows = 8

    def with_lost_row(body, lost):
        lead = body.shape[:-2]
        extra = jnp.zeros(lead + (pad_rows, tile_side), jnp.float32)
        extra = extra.at[..., 0, :vectors].set(jnp.broadcast_to(lost, lead + (vectors,)))
        return jnp.concatenate([body, extra], axis=-2)

    def spread_columns(blocks, lost):
        payload = with_lost_row(blocks.reshape(payload_rows, tile_side), lost)[None]
        if exchange:
            shift = 1
            while shift < dst_count:
                got = lax.ppermute(payload, "dst", [(i, i ^ shift) for i in range(dst_count)])
                payload = jnp.concatenate([payload, got], axis=0)
                shift *= 2
        else:
            payload = lax.all_gather(payload, "dst", axis=0, tiled=True)
        lost_dst = jnp.sum(payload[:, payload_rows, :vectors], axis=0)
        return payload, lost_dst

    def reduce_rows(accumulated, lost):
        n = src_count
        chunks = with_lost_row(accumulated.reshape(n, payload_rows, tile_side), lost)
        if n & (n - 1) == 0:
            bit = 0
            while chunks.shape[0] > 1:
                mine = (src_index >> bit) & 1
                paired = chunks.reshape(chunks.shape[0] // 2, 2, *chunks.shape[1:])
                keep = lax.dynamic_index_in_dim(paired, mine, 1, keepdims=False)
                give = lax.dynamic_index_in_dim(paired, 1 - mine, 1, keepdims=False)
                partner = [(i, i ^ (1 << bit)) for i in range(n)]
                chunks = keep + lax.ppermute(give, "src", partner)
                bit += 1
            total = chunks[0]
        else:
            total = lax.dynamic_index_in_dim(chunks, src_index, 0, keepdims=False)
            for shift in range(1, n):
                send = lax.dynamic_index_in_dim(chunks, (src_index + shift) % n, 0, keepdims=False)
                total = total + lax.ppermute(send, "src", [(i, (i + shift) % n) for i in range(n)])
        image = total[:payload_rows].reshape(blocks_piece, vectors, tile_side)
        return image, total[payload_rows, :vectors]

    def lost_partial(blocks):
        return jnp.sum(blocks * piece_dangling[:, None, None], axis=(0, 2))

    def relaxation(blocks, lost_sum=None):
        gathered, lost_dst = spread_columns(blocks, lost_partial(blocks))
        accumulated = tile_pass(
            "image", gathered, tiles, own_rows, kernel_cols, live_mask, block_count,
            row_blocks, vectors,
        )
        image, lost_total = reduce_rows(accumulated, lost_dst)
        if lost_sum is None:
            lost_sum = lost_total
        return (
            damping * (image + (lost_sum / page_total)[None, :, None] * tele)
            + (1.0 - damping) * tele
        )

    tele_sums = jnp.sum(tele, axis=2)
    weight_partial = jnp.einsum("bk,ba->ka", tele_sums, piece_hot, precision=highest)

    relaxed_one = relaxation(tele)
    relaxed_two = relaxation(relaxed_one)

    gathered, _ = spread_columns(relaxed_two, jnp.zeros((vectors,), jnp.float32))
    entries = tile_pass(
        "entries", gathered, tiles, own_rows, kernel_cols, live_mask, block_count,
        row_blocks, vectors,
    )[:, :, 0]
    block_sums = jnp.sum(relaxed_two, axis=2)
    totals_partial = jnp.einsum("bk,ba->ka", block_sums, piece_hot, precision=highest)
    lost_mass_partial = jnp.einsum(
        "bk,ba->ka", block_sums * piece_dangling[:, None], piece_hot, precision=highest
    )
    row_agg = agg_of_block[row_global]
    col_agg = agg_of_block[col_global]
    row_hot = (row_agg[:, None] == agg_range[None, :]).astype(jnp.float32)
    col_hot = (col_agg[:, None] == agg_range[None, :]).astype(jnp.float32)
    inflow_partial = jnp.einsum("tk,ta->ka", entries, row_hot, precision=highest)
    inflow_one, totals, lost_mass, weight = tree_sum(
        jnp.stack([inflow_partial, totals_partial, lost_mass_partial, weight_partial]),
        all_axes,
        all_count,
    )

    def coarse_sweep(inflow, ratios):
        carried = jnp.sum(lost_mass * ratios, axis=1)
        return (
            damping * (inflow + (carried / page_total)[:, None] * weight)
            + (1.0 - damping) * weight
        )

    level_one = coarse_sweep(inflow_one, jnp.ones((vectors, agg_count), jnp.float32))
    ratios_one = level_one / totals
    ratio_at_tile = jnp.einsum("ka,ta->tk", ratios_one, col_hot, precision=highest)
    inflow_two = tree_sum(
        jnp.einsum("tk,ta->ka", entries * ratio_at_tile, row_hot, precision=highest),
        all_axes,
        all_count,
    )
    level_two = coarse_sweep(inflow_two, ratios_one)
    ratios_two = level_two / totals
    rescale = jnp.einsum("ka,ba->bk", ratios_two, piece_hot, precision=highest)
    corrected = relaxed_two * rescale[:, :, None]
    lost_two = jnp.sum(lost_mass * ratios_two, axis=1)

    position = lax.axis_index(all_axes)
    owned_count = agg_count // (src_count * dst_count)
    owned = lax.dynamic_slice_in_dim(owner_list, position * owned_count, owned_count)
    owned_hot = (owned[:, None] == agg_range[None, :]).astype(jnp.float32)
    coarse_out = jnp.einsum("ka,qa->kq", level_two, owned_hot, precision=highest)

    relaxed_three = relaxation(corrected, lost_two)
    relaxed_four = relaxation(relaxed_three)
    fine_out = jnp.transpose(relaxed_four, (1, 0, 2)).reshape(teleport.shape)
    return fine_out, coarse_out


def solution(mesh):
    placed = (
        P(None, "dst", "src"),
        P("dst", "src", None, None, None),
        P("dst", "src", None),
        P("dst", "src", None),
        P("dst", "src"),
        P(),
        P(),
        P(),
    )
    return jax.shard_map(
        per_device,
        mesh=mesh,
        in_specs=placed,
        out_specs=(P(None, "dst", "src"), P(None, ("src", "dst"))),
        check_vma=False,
    )
```

```python
import functools

import jax
import jax.numpy as jnp
from jax import lax
from jax.experimental import pallas as pl
from jax.experimental.pallas import tpu as pltpu
from jax.sharding import PartitionSpec as P

damping = 0.85
group_size = 32
highest = lax.Precision.HIGHEST


def tile_kernel(mode, blocks_piece, rows_ref, cols_ref, live_ref, nb_ref, x_ref, t_ref, o_ref):
    step = pl.program_id(0)
    vectors = o_ref.shape[1]
    if mode == "image":

        @pl.when(step == 0)
        def _():
            o_ref[...] = jnp.zeros_like(o_ref)

    @pl.when(step < nb_ref[0])
    def _():
        for g in range(group_size):
            slot = step * group_size + g
            col = cols_ref[slot]
            start = pl.multiple_of((col % blocks_piece) * vectors, vectors)
            picked = x_ref[col // blocks_piece, pl.ds(start, vectors), :].astype(jnp.bfloat16)
            weight = jnp.where(live_ref[slot] != 0, 1.0, 0.0).astype(jnp.bfloat16)
            product = jnp.dot(picked * weight, t_ref[g], preferred_element_type=jnp.float32)
            if mode == "image":
                row = rows_ref[slot]
                o_ref[row] = o_ref[row] + product
            else:
                o_ref[g] = product[:, :128] + product[:, 128:]

    if mode == "entries":

        @pl.when(step >= nb_ref[0])
        def _():
            o_ref[...] = jnp.zeros_like(o_ref)


def tile_pass(mode, x_cols, tiles, rows, cols, live, block_count, row_blocks, vectors):
    groups, payload_rows, side = x_cols.shape
    slots = tiles.shape[2]
    steps = slots // group_size

    def tile_index(i, rows_ref, cols_ref, live_ref, nb_ref):
        return (0, 0, jnp.minimum(i, nb_ref[0] - 1), 0, 0)

    if mode == "image":
        out_shape = jax.ShapeDtypeStruct((row_blocks, vectors, side), jnp.float32)
        out_spec = pl.BlockSpec((row_blocks, vectors, side), lambda i, *_: (0, 0, 0))
    else:
        out_shape = jax.ShapeDtypeStruct((slots, vectors, 128), jnp.float32)
        out_spec = pl.BlockSpec((group_size, vectors, 128), lambda i, *_: (i, 0, 0))
    grid_spec = pltpu.PrefetchScalarGridSpec(
        num_scalar_prefetch=4,
        grid=(steps,),
        in_specs=[
            pl.BlockSpec((groups, payload_rows, side), lambda i, *_: (0, 0, 0)),
            pl.BlockSpec((None, None, group_size, side, side), tile_index),
        ],
        out_specs=out_spec,
    )
    return pl.pallas_call(
        functools.partial(tile_kernel, mode, payload_rows // vectors),
        grid_spec=grid_spec,
        out_shape=out_shape,
        compiler_params=pltpu.CompilerParams(dimension_semantics=("arbitrary",)),
    )(rows, cols, live, block_count, x_cols, tiles)


def per_device(
    teleport, tiles, tile_rows, tile_cols, tile_counts, dangling, agg_of_block, owner_list
):
    vectors = teleport.shape[0]
    piece_width = teleport.shape[2]
    slots_total = tiles.shape[2]
    tile_side = tiles.shape[4]
    blocks_piece = piece_width // tile_side
    src_count = lax.axis_size("src")
    dst_count = lax.axis_size("dst")
    row_blocks = blocks_piece * src_count
    col_blocks = blocks_piece * dst_count
    page_total = row_blocks * dst_count * tile_side
    agg_count = owner_list.shape[0]
    src_index = lax.axis_index("src")
    dst_index = lax.axis_index("dst")
    own_rows = jnp.clip(tile_rows[0, 0], 0, row_blocks - 1)
    own_cols = jnp.clip(tile_cols[0, 0], 0, col_blocks - 1)
    own_count = tile_counts[0, 0]
    col_global = (
        own_cols // blocks_piece * (blocks_piece * src_count)
        + src_index * blocks_piece
        + own_cols % blocks_piece
    )
    row_global = dst_index * row_blocks + own_rows
    slot_range = jnp.arange(slots_total, dtype=jnp.int32)
    live_mask = ((slot_range < own_count) & (dangling[col_global] == 0)).astype(jnp.int32)
    steps = slots_total // group_size
    block_count = jnp.clip((own_count + group_size - 1) // group_size, 1, steps).reshape(1)
    block_count = block_count.astype(jnp.int32)
    piece_first = dst_index * row_blocks + src_index * blocks_piece
    piece_dangling = lax.dynamic_slice_in_dim(dangling, piece_first, blocks_piece).astype(
        jnp.float32
    )
    piece_agg = lax.dynamic_slice_in_dim(agg_of_block, piece_first, blocks_piece)
    agg_range = jnp.arange(agg_count, dtype=jnp.int32)
    piece_hot = (piece_agg[:, None] == agg_range[None, :]).astype(jnp.float32)
    tele = jnp.transpose(teleport.reshape(vectors, blocks_piece, tile_side), (1, 0, 2))

    all_axes = ("src", "dst")
    all_count = src_count * dst_count

    def tree_sum(value, axis, size):
        if size & (size - 1):
            return lax.psum(value, axis)
        shift = 1
        while shift < size:
            value = value + lax.ppermute(value, axis, [(i, i ^ shift) for i in range(size)])
            shift *= 2
        return value

    exchange = dst_count & (dst_count - 1) == 0
    if exchange:
        kernel_cols = (
            (own_cols // blocks_piece) ^ dst_index
        ) * blocks_piece + own_cols % blocks_piece
    else:
        kernel_cols = own_cols

    payload_rows = blocks_piece * vectors
    pad_rows = 8

    def with_lost_row(body, lost):
        lead = body.shape[:-2]
        extra = jnp.zeros(lead + (pad_rows, tile_side), jnp.float32)
        extra = extra.at[..., 0, :vectors].set(jnp.broadcast_to(lost, lead + (vectors,)))
        return jnp.concatenate([body, extra], axis=-2)

    def spread_columns(blocks, lost):
        payload = with_lost_row(blocks.reshape(payload_rows, tile_side), lost)[None]
        if exchange:
            shift = 1
            while shift < dst_count:
                got = lax.ppermute(payload, "dst", [(i, i ^ shift) for i in range(dst_count)])
                payload = jnp.concatenate([payload, got], axis=0)
                shift *= 2
        else:
            payload = lax.all_gather(payload, "dst", axis=0, tiled=True)
        lost_dst = jnp.sum(payload[:, payload_rows, :vectors], axis=0)
        return payload, lost_dst

    def reduce_rows(accumulated, lost):
        n = src_count
        chunks = with_lost_row(accumulated.reshape(n, payload_rows, tile_side), lost)
        if n & (n - 1) == 0:
            bit = 0
            while chunks.shape[0] > 1:
                mine = (src_index >> bit) & 1
                paired = chunks.reshape(chunks.shape[0] // 2, 2, *chunks.shape[1:])
                keep = lax.dynamic_index_in_dim(paired, mine, 1, keepdims=False)
                give = lax.dynamic_index_in_dim(paired, 1 - mine, 1, keepdims=False)
                partner = [(i, i ^ (1 << bit)) for i in range(n)]
                chunks = keep + lax.ppermute(give, "src", partner)
                bit += 1
            total = chunks[0]
        else:
            total = lax.dynamic_index_in_dim(chunks, src_index, 0, keepdims=False)
            for shift in range(1, n):
                send = lax.dynamic_index_in_dim(chunks, (src_index + shift) % n, 0, keepdims=False)
                total = total + lax.ppermute(send, "src", [(i, (i + shift) % n) for i in range(n)])
        image = total[:payload_rows].reshape(blocks_piece, vectors, tile_side)
        return image, total[payload_rows, :vectors]

    def lost_partial(blocks):
        return jnp.sum(blocks * piece_dangling[:, None, None], axis=(0, 2))

    def relaxation(blocks, lost_sum=None):
        gathered, lost_dst = spread_columns(blocks, lost_partial(blocks))
        accumulated = tile_pass(
            "image", gathered, tiles, own_rows, kernel_cols, live_mask, block_count,
            row_blocks, vectors,
        )
        image, lost_total = reduce_rows(accumulated, lost_dst)
        if lost_sum is None:
            lost_sum = lost_total
        return (
            damping * (image + (lost_sum / page_total)[None, :, None] * tele)
            + (1.0 - damping) * tele
        )

    tele_sums = jnp.sum(tele, axis=2)
    weight_partial = jnp.einsum("bk,ba->ka", tele_sums, piece_hot, precision=highest)

    relaxed_one = relaxation(tele)
    relaxed_two = relaxation(relaxed_one)

    gathered, _ = spread_columns(relaxed_two, jnp.zeros((vectors,), jnp.float32))
    entries = tile_pass(
        "entries", gathered, tiles, own_rows, kernel_cols, live_mask, block_count,
        row_blocks, vectors,
    ).sum(axis=2)
    block_sums = jnp.sum(relaxed_two, axis=2)
    totals_partial = jnp.einsum("bk,ba->ka", block_sums, piece_hot, precision=highest)
    lost_mass_partial = jnp.einsum(
        "bk,ba->ka", block_sums * piece_dangling[:, None], piece_hot, precision=highest
    )
    row_agg = agg_of_block[row_global]
    col_agg = agg_of_block[col_global]
    row_hot = (row_agg[:, None] == agg_range[None, :]).astype(jnp.float32)
    col_hot = (col_agg[:, None] == agg_range[None, :]).astype(jnp.float32)
    inflow_partial = jnp.einsum("tk,ta->ka", entries, row_hot, precision=highest)
    inflow_one, totals, lost_mass, weight = tree_sum(
        jnp.stack([inflow_partial, totals_partial, lost_mass_partial, weight_partial]),
        all_axes,
        all_count,
    )

    def coarse_sweep(inflow, ratios):
        carried = jnp.sum(lost_mass * ratios, axis=1)
        return (
            damping * (inflow + (carried / page_total)[:, None] * weight)
            + (1.0 - damping) * weight
        )

    level_one = coarse_sweep(inflow_one, jnp.ones((vectors, agg_count), jnp.float32))
    ratios_one = level_one / totals
    ratio_at_tile = jnp.einsum("ka,ta->tk", ratios_one, col_hot, precision=highest)
    inflow_two = tree_sum(
        jnp.einsum("tk,ta->ka", entries * ratio_at_tile, row_hot, precision=highest),
        all_axes,
        all_count,
    )
    level_two = coarse_sweep(inflow_two, ratios_one)
    ratios_two = level_two / totals
    rescale = jnp.einsum("ka,ba->bk", ratios_two, piece_hot, precision=highest)
    corrected = relaxed_two * rescale[:, :, None]
    lost_two = jnp.sum(lost_mass * ratios_two, axis=1)

    position = lax.axis_index(all_axes)
    owned_count = agg_count // (src_count * dst_count)
    owned = lax.dynamic_slice_in_dim(owner_list, position * owned_count, owned_count)
    owned_hot = (owned[:, None] == agg_range[None, :]).astype(jnp.float32)
    coarse_out = jnp.einsum("ka,qa->kq", level_two, owned_hot, precision=highest)

    relaxed_three = relaxation(corrected, lost_two)
    relaxed_four = relaxation(relaxed_three)
    fine_out = jnp.transpose(relaxed_four, (1, 0, 2)).reshape(teleport.shape)
    return fine_out, coarse_out


def solution(mesh):
    placed = (
        P(None, "dst", "src"),
        P("dst", "src", None, None, None),
        P("dst", "src", None),
        P("dst", "src", None),
        P("dst", "src"),
        P(),
        P(),
        P(),
    )
    return jax.shard_map(
        per_device,
        mesh=mesh,
        in_specs=placed,
        out_specs=(P(None, "dst", "src"), P(None, ("src", "dst"))),
        check_vma=False,
    )
```

```python
import functools

import jax
import jax.numpy as jnp
from jax import lax
from jax.experimental import pallas as pl
from jax.experimental.pallas import tpu as pltpu
from jax.sharding import PartitionSpec as P

damping = 0.85
group_size = 32
highest = lax.Precision.HIGHEST


def tile_kernel(mode, blocks_piece, rows_ref, cols_ref, live_ref, nb_ref, x_ref, t_ref, o_ref):
    step = pl.program_id(0)
    vectors = o_ref.shape[1]
    if mode == "image":

        @pl.when(step == 0)
        def _():
            o_ref[...] = jnp.zeros_like(o_ref)

    @pl.when(step < nb_ref[0])
    def _():
        for g in range(group_size):
            slot = step * group_size + g
            col = cols_ref[slot]
            start = pl.multiple_of((col % blocks_piece) * vectors, vectors)
            picked = x_ref[col // blocks_piece, pl.ds(start, vectors), :].astype(jnp.bfloat16)
            weight = jnp.where(live_ref[slot] != 0, 1.0, 0.0).astype(jnp.bfloat16)
            product = jnp.dot(picked * weight, t_ref[g], preferred_element_type=jnp.float32)
            if mode == "image":
                row = rows_ref[slot]
                o_ref[row] = o_ref[row] + product
            else:
                o_ref[g] = product[:, :128] + product[:, 128:]

    if mode == "entries":

        @pl.when(step >= nb_ref[0])
        def _():
            o_ref[...] = jnp.zeros_like(o_ref)


def tile_pass(mode, x_cols, tiles, rows, cols, live, block_count, row_blocks, vectors):
    groups, payload_rows, side = x_cols.shape
    slots = tiles.shape[2]
    steps = slots // group_size

    def tile_index(i, rows_ref, cols_ref, live_ref, nb_ref):
        return (0, 0, jnp.minimum(i, nb_ref[0] - 1), 0, 0)

    if mode == "image":
        out_shape = jax.ShapeDtypeStruct((row_blocks, vectors, side), jnp.float32)
        out_spec = pl.BlockSpec((row_blocks, vectors, side), lambda i, *_: (0, 0, 0))
    else:
        out_shape = jax.ShapeDtypeStruct((slots, vectors, 128), jnp.float32)
        out_spec = pl.BlockSpec((group_size, vectors, 128), lambda i, *_: (i, 0, 0))
    grid_spec = pltpu.PrefetchScalarGridSpec(
        num_scalar_prefetch=4,
        grid=(steps,),
        in_specs=[
            pl.BlockSpec((groups, payload_rows, side), lambda i, *_: (0, 0, 0)),
            pl.BlockSpec((None, None, group_size, side, side), tile_index),
        ],
        out_specs=out_spec,
    )
    return pl.pallas_call(
        functools.partial(tile_kernel, mode, payload_rows // vectors),
        grid_spec=grid_spec,
        out_shape=out_shape,
        compiler_params=pltpu.CompilerParams(dimension_semantics=("arbitrary",)),
    )(rows, cols, live, block_count, x_cols, tiles)


def per_device(
    teleport, tiles, tile_rows, tile_cols, tile_counts, dangling, agg_of_block, owner_list
):
    vectors = teleport.shape[0]
    piece_width = teleport.shape[2]
    slots_total = tiles.shape[2]
    tile_side = tiles.shape[4]
    blocks_piece = piece_width // tile_side
    src_count = lax.axis_size("src")
    dst_count = lax.axis_size("dst")
    row_blocks = blocks_piece * src_count
    col_blocks = blocks_piece * dst_count
    page_total = row_blocks * dst_count * tile_side
    agg_count = owner_list.shape[0]
    src_index = lax.axis_index("src")
    dst_index = lax.axis_index("dst")
    own_rows = jnp.clip(tile_rows[0, 0], 0, row_blocks - 1)
    own_cols = jnp.clip(tile_cols[0, 0], 0, col_blocks - 1)
    own_count = tile_counts[0, 0]
    col_global = (
        own_cols // blocks_piece * (blocks_piece * src_count)
        + src_index * blocks_piece
        + own_cols % blocks_piece
    )
    row_global = dst_index * row_blocks + own_rows
    slot_range = jnp.arange(slots_total, dtype=jnp.int32)
    live_mask = ((slot_range < own_count) & (dangling[col_global] == 0)).astype(jnp.int32)
    steps = slots_total // group_size
    block_count = jnp.clip((own_count + group_size - 1) // group_size, 1, steps).reshape(1)
    block_count = block_count.astype(jnp.int32)
    piece_first = dst_index * row_blocks + src_index * blocks_piece
    piece_dangling = lax.dynamic_slice_in_dim(dangling, piece_first, blocks_piece).astype(
        jnp.float32
    )
    piece_agg = lax.dynamic_slice_in_dim(agg_of_block, piece_first, blocks_piece)
    agg_range = jnp.arange(agg_count, dtype=jnp.int32)
    piece_hot = (piece_agg[:, None] == agg_range[None, :]).astype(jnp.float32)
    tele = jnp.transpose(teleport.reshape(vectors, blocks_piece, tile_side), (1, 0, 2))

    all_axes = ("src", "dst")
    all_count = src_count * dst_count

    def tree_sum(value, axis, size):
        if size & (size - 1):
            return lax.psum(value, axis)
        shift = 1
        while shift < size:
            value = value + lax.ppermute(value, axis, [(i, i ^ shift) for i in range(size)])
            shift *= 2
        return value

    exchange = dst_count & (dst_count - 1) == 0
    if exchange:
        kernel_cols = (
            (own_cols // blocks_piece) ^ dst_index
        ) * blocks_piece + own_cols % blocks_piece
    else:
        kernel_cols = own_cols

    payload_rows = blocks_piece * vectors
    pad_rows = 8

    def with_lost_row(body, lost):
        lead = body.shape[:-2]
        extra = jnp.zeros(lead + (pad_rows, tile_side), jnp.float32)
        extra = extra.at[..., 0, :vectors].set(jnp.broadcast_to(lost, lead + (vectors,)))
        return jnp.concatenate([body, extra], axis=-2)

    def spread_columns(blocks, lost):
        payload = with_lost_row(blocks.reshape(payload_rows, tile_side), lost)[None]
        if exchange:
            pieces = [payload] + [
                lax.ppermute(payload, "dst", [(i, i ^ v) for i in range(dst_count)])
                for v in range(1, dst_count)
            ]
            payload = jnp.concatenate(pieces, axis=0)
        else:
            payload = lax.all_gather(payload, "dst", axis=0, tiled=True)
        lost_dst = jnp.sum(payload[:, payload_rows, :vectors], axis=0)
        return payload, lost_dst

    def reduce_rows(accumulated, lost):
        n = src_count
        chunks = with_lost_row(accumulated.reshape(n, payload_rows, tile_side), lost)
        if n % 2 == 0:
            half = n // 2
            paired = chunks.reshape(half, 2, *chunks.shape[1:])
            core = src_index % 2
            keep = lax.dynamic_index_in_dim(paired, core, 1, keepdims=False)
            give = lax.dynamic_index_in_dim(paired, 1 - core, 1, keepdims=False)
            part = keep + lax.ppermute(give, "src", [(i, i ^ 1) for i in range(n)])
            chip = src_index // 2
            total = lax.dynamic_index_in_dim(part, chip, 0, keepdims=False)
            for shift in range(1, half):
                send = lax.dynamic_index_in_dim(part, (chip + shift) % half, 0, keepdims=False)
                pairs = [(i, ((i // 2 + shift) % half) * 2 + i % 2) for i in range(n)]
                total = total + lax.ppermute(send, "src", pairs)
        else:
            total = lax.dynamic_index_in_dim(chunks, src_index, 0, keepdims=False)
            for shift in range(1, n):
                send = lax.dynamic_index_in_dim(chunks, (src_index + shift) % n, 0, keepdims=False)
                total = total + lax.ppermute(send, "src", [(i, (i + shift) % n) for i in range(n)])
        image = total[:payload_rows].reshape(blocks_piece, vectors, tile_side)
        return image, total[payload_rows, :vectors]

    def lost_partial(blocks):
        return jnp.sum(blocks * piece_dangling[:, None, None], axis=(0, 2))

    def relaxation(blocks, lost_sum=None):
        gathered, lost_dst = spread_columns(blocks, lost_partial(blocks))
        accumulated = tile_pass(
            "image", gathered, tiles, own_rows, kernel_cols, live_mask, block_count,
            row_blocks, vectors,
        )
        image, lost_total = reduce_rows(accumulated, lost_dst)
        if lost_sum is None:
            lost_sum = lost_total
        return (
            damping * (image + (lost_sum / page_total)[None, :, None] * tele)
            + (1.0 - damping) * tele
        )

    tele_sums = jnp.sum(tele, axis=2)
    weight_partial = jnp.einsum("bk,ba->ka", tele_sums, piece_hot, precision=highest)

    relaxed_one = relaxation(tele)
    relaxed_two = relaxation(relaxed_one)

    gathered, _ = spread_columns(relaxed_two, jnp.zeros((vectors,), jnp.float32))
    entries = tile_pass(
        "entries", gathered, tiles, own_rows, kernel_cols, live_mask, block_count,
        row_blocks, vectors,
    ).sum(axis=2)
    block_sums = jnp.sum(relaxed_two, axis=2)
    totals_partial = jnp.einsum("bk,ba->ka", block_sums, piece_hot, precision=highest)
    lost_mass_partial = jnp.einsum(
        "bk,ba->ka", block_sums * piece_dangling[:, None], piece_hot, precision=highest
    )
    row_agg = agg_of_block[row_global]
    col_agg = agg_of_block[col_global]
    row_hot = (row_agg[:, None] == agg_range[None, :]).astype(jnp.float32)
    col_hot = (col_agg[:, None] == agg_range[None, :]).astype(jnp.float32)
    inflow_partial = jnp.einsum("tk,ta->ka", entries, row_hot, precision=highest)
    inflow_one, totals, lost_mass, weight = tree_sum(
        jnp.stack([inflow_partial, totals_partial, lost_mass_partial, weight_partial]),
        all_axes,
        all_count,
    )

    def coarse_sweep(inflow, ratios):
        carried = jnp.sum(lost_mass * ratios, axis=1)
        return (
            damping * (inflow + (carried / page_total)[:, None] * weight)
            + (1.0 - damping) * weight
        )

    level_one = coarse_sweep(inflow_one, jnp.ones((vectors, agg_count), jnp.float32))
    ratios_one = level_one / totals
    ratio_at_tile = jnp.einsum("ka,ta->tk", ratios_one, col_hot, precision=highest)
    inflow_two = tree_sum(
        jnp.einsum("tk,ta->ka", entries * ratio_at_tile, row_hot, precision=highest),
        all_axes,
        all_count,
    )
    level_two = coarse_sweep(inflow_two, ratios_one)
    ratios_two = level_two / totals
    rescale = jnp.einsum("ka,ba->bk", ratios_two, piece_hot, precision=highest)
    corrected = relaxed_two * rescale[:, :, None]
    lost_two = jnp.sum(lost_mass * ratios_two, axis=1)

    position = lax.axis_index(all_axes)
    owned_count = agg_count // (src_count * dst_count)
    owned = lax.dynamic_slice_in_dim(owner_list, position * owned_count, owned_count)
    owned_hot = (owned[:, None] == agg_range[None, :]).astype(jnp.float32)
    coarse_out = jnp.einsum("ka,qa->kq", level_two, owned_hot, precision=highest)

    relaxed_three = relaxation(corrected, lost_two)
    relaxed_four = relaxation(relaxed_three)
    fine_out = jnp.transpose(relaxed_four, (1, 0, 2)).reshape(teleport.shape)
    return fine_out, coarse_out


def solution(mesh):
    placed = (
        P(None, "dst", "src"),
        P("dst", "src", None, None, None),
        P("dst", "src", None),
        P("dst", "src", None),
        P("dst", "src"),
        P(),
        P(),
        P(),
    )
    return jax.shard_map(
        per_device,
        mesh=mesh,
        in_specs=placed,
        out_specs=(P(None, "dst", "src"), P(None, ("src", "dst"))),
        check_vma=False,
    )
```

```python
import functools

import jax
import jax.numpy as jnp
from jax import lax
from jax.experimental import pallas as pl
from jax.experimental.pallas import tpu as pltpu
from jax.sharding import PartitionSpec as P

damping = 0.85
group_size = 32
highest = lax.Precision.HIGHEST


def tile_kernel(mode, blocks_piece, rows_ref, cols_ref, live_ref, nb_ref, x_ref, t_ref, o_ref):
    step = pl.program_id(0)
    vectors = o_ref.shape[1]
    if mode == "image":

        @pl.when(step == 0)
        def _():
            o_ref[...] = jnp.zeros_like(o_ref)

    @pl.when(step < nb_ref[0])
    def _():
        for g in range(group_size):
            slot = step * group_size + g
            col = cols_ref[slot]
            start = pl.multiple_of((col % blocks_piece) * vectors, vectors)
            picked = x_ref[col // blocks_piece, pl.ds(start, vectors), :].astype(jnp.bfloat16)
            weight = jnp.where(live_ref[slot] != 0, 1.0, 0.0).astype(jnp.bfloat16)
            product = jnp.dot(picked * weight, t_ref[g], preferred_element_type=jnp.float32)
            if mode == "image":
                row = rows_ref[slot]
                o_ref[row] = o_ref[row] + product
            else:
                o_ref[g] = product[:, :128] + product[:, 128:]

    if mode == "entries":

        @pl.when(step >= nb_ref[0])
        def _():
            o_ref[...] = jnp.zeros_like(o_ref)


def tile_pass(mode, x_cols, tiles, rows, cols, live, block_count, row_blocks, vectors):
    groups, payload_rows, side = x_cols.shape
    slots = tiles.shape[2]
    steps = slots // group_size

    def tile_index(i, rows_ref, cols_ref, live_ref, nb_ref):
        return (0, 0, jnp.minimum(i, nb_ref[0] - 1), 0, 0)

    if mode == "image":
        out_shape = jax.ShapeDtypeStruct((row_blocks, vectors, side), jnp.float32)
        out_spec = pl.BlockSpec((row_blocks, vectors, side), lambda i, *_: (0, 0, 0))
    else:
        out_shape = jax.ShapeDtypeStruct((slots, vectors, 128), jnp.float32)
        out_spec = pl.BlockSpec((group_size, vectors, 128), lambda i, *_: (i, 0, 0))
    grid_spec = pltpu.PrefetchScalarGridSpec(
        num_scalar_prefetch=4,
        grid=(steps,),
        in_specs=[
            pl.BlockSpec((groups, payload_rows, side), lambda i, *_: (0, 0, 0)),
            pl.BlockSpec((None, None, group_size, side, side), tile_index),
        ],
        out_specs=out_spec,
    )
    return pl.pallas_call(
        functools.partial(tile_kernel, mode, payload_rows // vectors),
        grid_spec=grid_spec,
        out_shape=out_shape,
        compiler_params=pltpu.CompilerParams(dimension_semantics=("arbitrary",)),
    )(rows, cols, live, block_count, x_cols, tiles)


def per_device(
    teleport, tiles, tile_rows, tile_cols, tile_counts, dangling, agg_of_block, owner_list
):
    vectors = teleport.shape[0]
    piece_width = teleport.shape[2]
    slots_total = tiles.shape[2]
    tile_side = tiles.shape[4]
    blocks_piece = piece_width // tile_side
    src_count = lax.axis_size("src")
    dst_count = lax.axis_size("dst")
    row_blocks = blocks_piece * src_count
    col_blocks = blocks_piece * dst_count
    page_total = row_blocks * dst_count * tile_side
    agg_count = owner_list.shape[0]
    src_index = lax.axis_index("src")
    dst_index = lax.axis_index("dst")
    own_rows = jnp.clip(tile_rows[0, 0], 0, row_blocks - 1)
    own_cols = jnp.clip(tile_cols[0, 0], 0, col_blocks - 1)
    own_count = tile_counts[0, 0]
    col_global = (
        own_cols // blocks_piece * (blocks_piece * src_count)
        + src_index * blocks_piece
        + own_cols % blocks_piece
    )
    row_global = dst_index * row_blocks + own_rows
    slot_range = jnp.arange(slots_total, dtype=jnp.int32)
    live_mask = ((slot_range < own_count) & (dangling[col_global] == 0)).astype(jnp.int32)
    steps = slots_total // group_size
    block_count = jnp.clip((own_count + group_size - 1) // group_size, 1, steps).reshape(1)
    block_count = block_count.astype(jnp.int32)
    piece_first = dst_index * row_blocks + src_index * blocks_piece
    piece_dangling = lax.dynamic_slice_in_dim(dangling, piece_first, blocks_piece).astype(
        jnp.float32
    )
    piece_agg = lax.dynamic_slice_in_dim(agg_of_block, piece_first, blocks_piece)
    agg_range = jnp.arange(agg_count, dtype=jnp.int32)
    piece_hot = (piece_agg[:, None] == agg_range[None, :]).astype(jnp.float32)
    tele = jnp.transpose(teleport.reshape(vectors, blocks_piece, tile_side), (1, 0, 2))

    all_axes = ("src", "dst")
    all_count = src_count * dst_count

    def tree_sum(value, axis, size):
        if size & (size - 1):
            return lax.psum(value, axis)
        shift = 1
        while shift < size:
            value = value + lax.ppermute(value, axis, [(i, i ^ shift) for i in range(size)])
            shift *= 2
        return value

    exchange = dst_count & (dst_count - 1) == 0
    if exchange:
        kernel_cols = (
            (own_cols // blocks_piece) ^ dst_index
        ) * blocks_piece + own_cols % blocks_piece
    else:
        kernel_cols = own_cols

    payload_rows = blocks_piece * vectors
    pad_rows = 8

    def with_lost_row(body, lost):
        lead = body.shape[:-2]
        extra = jnp.zeros(lead + (pad_rows, tile_side), jnp.float32)
        extra = extra.at[..., 0, :vectors].set(jnp.broadcast_to(lost, lead + (vectors,)))
        return jnp.concatenate([body, extra], axis=-2)

    def spread_columns(blocks, lost):
        payload = with_lost_row(blocks.reshape(payload_rows, tile_side), lost)[None]
        if exchange:
            pieces = [payload] + [
                lax.ppermute(payload, "dst", [(i, i ^ v) for i in range(dst_count)])
                for v in range(1, dst_count)
            ]
            payload = jnp.concatenate(pieces, axis=0)
        else:
            payload = lax.all_gather(payload, "dst", axis=0, tiled=True)
        lost_dst = jnp.sum(payload[:, payload_rows, :vectors], axis=0)
        return payload, lost_dst

    def reduce_rows(accumulated, lost):
        n = src_count
        chunks = with_lost_row(accumulated.reshape(n, payload_rows, tile_side), lost)
        if n % 2 == 0:
            half = n // 2
            paired = chunks.reshape(half, 2, *chunks.shape[1:])
            core = src_index % 2
            keep = lax.dynamic_index_in_dim(paired, core, 1, keepdims=False)
            give = lax.dynamic_index_in_dim(paired, 1 - core, 1, keepdims=False)
            part = keep + lax.ppermute(give, "src", [(i, i ^ 1) for i in range(n)])
            chip = src_index // 2
            total = lax.dynamic_index_in_dim(part, chip, 0, keepdims=False)
            for shift in range(1, half):
                send = lax.dynamic_index_in_dim(part, (chip + shift) % half, 0, keepdims=False)
                pairs = [(i, ((i // 2 + shift) % half) * 2 + i % 2) for i in range(n)]
                total = total + lax.ppermute(send, "src", pairs)
        else:
            total = lax.dynamic_index_in_dim(chunks, src_index, 0, keepdims=False)
            for shift in range(1, n):
                send = lax.dynamic_index_in_dim(chunks, (src_index + shift) % n, 0, keepdims=False)
                total = total + lax.ppermute(send, "src", [(i, (i + shift) % n) for i in range(n)])
        image = total[:payload_rows].reshape(blocks_piece, vectors, tile_side)
        return image, total[payload_rows, :vectors]

    def lost_partial(blocks):
        return jnp.sum(blocks * piece_dangling[:, None, None], axis=(0, 2))

    def relaxation(blocks, lost_sum=None):
        gathered, lost_dst = spread_columns(blocks, lost_partial(blocks))
        accumulated = tile_pass(
            "image", gathered, tiles, own_rows, kernel_cols, live_mask, block_count,
            row_blocks, vectors,
        )
        image, lost_total = reduce_rows(accumulated, lost_dst)
        if lost_sum is None:
            lost_sum = lost_total
        return (
            damping * (image + (lost_sum / page_total)[None, :, None] * tele)
            + (1.0 - damping) * tele
        )

    tele_sums = jnp.sum(tele, axis=2)

    relaxed_one = relaxation(tele)
    relaxed_two = relaxation(relaxed_one)

    gathered, _ = spread_columns(relaxed_two, jnp.zeros((vectors,), jnp.float32))
    entries = tile_pass(
        "entries", gathered, tiles, own_rows, kernel_cols, live_mask, block_count,
        row_blocks, vectors,
    ).sum(axis=2)
    block_sums = jnp.sum(relaxed_two, axis=2)
    row_agg = agg_of_block[row_global]
    col_agg = agg_of_block[col_global]
    fields = [
        entries.reshape(-1),
        row_agg.astype(jnp.float32),
        col_agg.astype(jnp.float32),
        block_sums.reshape(-1),
        tele_sums.reshape(-1),
        piece_agg.astype(jnp.float32),
        piece_dangling,
    ]
    sizes = [f.shape[0] for f in fields]
    shared = jnp.concatenate(fields)[None]
    if all_count & (all_count - 1) == 0:
        shift = 1
        while shift < all_count:
            got = lax.ppermute(shared, all_axes, [(i, i ^ shift) for i in range(all_count)])
            shared = jnp.concatenate([shared, got], axis=0)
            shift *= 2
    else:
        shared = lax.all_gather(shared[0], all_axes, axis=0, tiled=False)
    offsets = [0]
    for size in sizes:
        offsets.append(offsets[-1] + size)
    every = [shared[:, offsets[i]:offsets[i + 1]] for i in range(len(sizes))]
    all_entries = every[0].reshape(-1, vectors)
    all_row_hot = (every[1].reshape(-1)[:, None] == agg_range[None, :].astype(jnp.float32))
    all_col_hot = (every[2].reshape(-1)[:, None] == agg_range[None, :].astype(jnp.float32))
    all_row_hot = all_row_hot.astype(jnp.float32)
    all_col_hot = all_col_hot.astype(jnp.float32)
    all_block_sums = every[3].reshape(-1, vectors)
    all_tele_sums = every[4].reshape(-1, vectors)
    all_block_hot = (every[5].reshape(-1)[:, None] == agg_range[None, :].astype(jnp.float32))
    all_block_hot = all_block_hot.astype(jnp.float32)
    all_dangling = every[6].reshape(-1)
    totals = jnp.einsum("bk,ba->ka", all_block_sums, all_block_hot, precision=highest)
    lost_mass = jnp.einsum(
        "bk,ba->ka", all_block_sums * all_dangling[:, None], all_block_hot, precision=highest
    )
    weight = jnp.einsum("bk,ba->ka", all_tele_sums, all_block_hot, precision=highest)
    inflow_one = jnp.einsum("tk,ta->ka", all_entries, all_row_hot, precision=highest)

    def coarse_sweep(inflow, ratios):
        carried = jnp.sum(lost_mass * ratios, axis=1)
        return (
            damping * (inflow + (carried / page_total)[:, None] * weight)
            + (1.0 - damping) * weight
        )

    level_one = coarse_sweep(inflow_one, jnp.ones((vectors, agg_count), jnp.float32))
    ratios_one = level_one / totals
    ratio_at_tile = jnp.einsum("ka,ta->tk", ratios_one, all_col_hot, precision=highest)
    inflow_two = jnp.einsum(
        "tk,ta->ka", all_entries * ratio_at_tile, all_row_hot, precision=highest
    )
    level_two = coarse_sweep(inflow_two, ratios_one)
    ratios_two = level_two / totals
    rescale = jnp.einsum("ka,ba->bk", ratios_two, piece_hot, precision=highest)
    corrected = relaxed_two * rescale[:, :, None]
    lost_two = jnp.sum(lost_mass * ratios_two, axis=1)

    position = lax.axis_index(all_axes)
    owned_count = agg_count // (src_count * dst_count)
    owned = lax.dynamic_slice_in_dim(owner_list, position * owned_count, owned_count)
    owned_hot = (owned[:, None] == agg_range[None, :]).astype(jnp.float32)
    coarse_out = jnp.einsum("ka,qa->kq", level_two, owned_hot, precision=highest)

    relaxed_three = relaxation(corrected, lost_two)
    relaxed_four = relaxation(relaxed_three)
    fine_out = jnp.transpose(relaxed_four, (1, 0, 2)).reshape(teleport.shape)
    return fine_out, coarse_out


def solution(mesh):
    placed = (
        P(None, "dst", "src"),
        P("dst", "src", None, None, None),
        P("dst", "src", None),
        P("dst", "src", None),
        P("dst", "src"),
        P(),
        P(),
        P(),
    )
    return jax.shard_map(
        per_device,
        mesh=mesh,
        in_specs=placed,
        out_specs=(P(None, "dst", "src"), P(None, ("src", "dst"))),
        check_vma=False,
    )
```

```python
import functools

import jax
import jax.numpy as jnp
from jax import lax
from jax.experimental import pallas as pl
from jax.experimental.pallas import tpu as pltpu
from jax.sharding import PartitionSpec as P

damping = 0.85
group_size = 32
highest = lax.Precision.HIGHEST


def tile_kernel(
    mode, blocks_piece, vectors, rows_ref, cols_ref, live_ref, nb_ref, x_ref, t_ref, o_ref
):
    step = pl.program_id(0)
    if mode == "image":

        @pl.when(step == 0)
        def _():
            o_ref[...] = jnp.zeros_like(o_ref)

    @pl.when(step < nb_ref[0])
    def _():
        for g in range(group_size):
            slot = step * group_size + g
            col = cols_ref[slot]
            start = pl.multiple_of((col % blocks_piece) * vectors, vectors)
            picked = x_ref[col // blocks_piece, pl.ds(start, vectors), :].astype(jnp.bfloat16)
            weight = jnp.where(live_ref[slot] != 0, 1.0, 0.0).astype(jnp.bfloat16)
            product = jnp.dot(picked * weight, t_ref[g], preferred_element_type=jnp.float32)
            if mode == "image":
                row = rows_ref[slot]
                at = pl.multiple_of((row % blocks_piece) * vectors, vectors)
                window = (row // blocks_piece, pl.ds(at, vectors), slice(None))
                o_ref[window] = o_ref[window] + product
            else:
                o_ref[g] = product[:, :128] + product[:, 128:]

    if mode == "entries":

        @pl.when(step >= nb_ref[0])
        def _():
            o_ref[...] = jnp.zeros_like(o_ref)


def tile_pass(mode, x_cols, tiles, rows, cols, live, block_count, row_blocks, vectors):
    groups, padded_rows, side = x_cols.shape
    blocks_piece = padded_rows // vectors
    owners = row_blocks // blocks_piece
    slots = tiles.shape[2]
    steps = slots // group_size

    def tile_index(i, rows_ref, cols_ref, live_ref, nb_ref):
        return (0, 0, jnp.minimum(i, nb_ref[0] - 1), 0, 0)

    if mode == "image":
        out_shape = jax.ShapeDtypeStruct((owners, padded_rows, side), jnp.float32)
        out_spec = pl.BlockSpec((owners, padded_rows, side), lambda i, *_: (0, 0, 0))
    else:
        out_shape = jax.ShapeDtypeStruct((slots, vectors, 128), jnp.float32)
        out_spec = pl.BlockSpec((group_size, vectors, 128), lambda i, *_: (i, 0, 0))
    grid_spec = pltpu.PrefetchScalarGridSpec(
        num_scalar_prefetch=4,
        grid=(steps,),
        in_specs=[
            pl.BlockSpec((groups, padded_rows, side), lambda i, *_: (0, 0, 0)),
            pl.BlockSpec((None, None, group_size, side, side), tile_index),
        ],
        out_specs=out_spec,
    )
    return pl.pallas_call(
        functools.partial(tile_kernel, mode, blocks_piece, vectors),
        grid_spec=grid_spec,
        out_shape=out_shape,
        compiler_params=pltpu.CompilerParams(dimension_semantics=("arbitrary",)),
    )(rows, cols, live, block_count, x_cols, tiles)


def per_device(
    teleport, tiles, tile_rows, tile_cols, tile_counts, dangling, agg_of_block, owner_list
):
    vectors = teleport.shape[0]
    piece_width = teleport.shape[2]
    slots_total = tiles.shape[2]
    tile_side = tiles.shape[4]
    blocks_piece = piece_width // tile_side
    src_count = lax.axis_size("src")
    dst_count = lax.axis_size("dst")
    row_blocks = blocks_piece * src_count
    col_blocks = blocks_piece * dst_count
    page_total = row_blocks * dst_count * tile_side
    agg_count = owner_list.shape[0]
    src_index = lax.axis_index("src")
    dst_index = lax.axis_index("dst")
    own_rows = jnp.clip(tile_rows[0, 0], 0, row_blocks - 1)
    own_cols = jnp.clip(tile_cols[0, 0], 0, col_blocks - 1)
    own_count = tile_counts[0, 0]
    col_global = (
        own_cols // blocks_piece * (blocks_piece * src_count)
        + src_index * blocks_piece
        + own_cols % blocks_piece
    )
    row_global = dst_index * row_blocks + own_rows
    slot_range = jnp.arange(slots_total, dtype=jnp.int32)
    live_mask = ((slot_range < own_count) & (dangling[col_global] == 0)).astype(jnp.int32)
    steps = slots_total // group_size
    block_count = jnp.clip((own_count + group_size - 1) // group_size, 1, steps).reshape(1)
    block_count = block_count.astype(jnp.int32)
    piece_first = dst_index * row_blocks + src_index * blocks_piece
    piece_dangling = lax.dynamic_slice_in_dim(dangling, piece_first, blocks_piece).astype(
        jnp.float32
    )
    piece_agg = lax.dynamic_slice_in_dim(agg_of_block, piece_first, blocks_piece)
    agg_range = jnp.arange(agg_count, dtype=jnp.int32)
    piece_hot = (piece_agg[:, None] == agg_range[None, :]).astype(jnp.float32)
    tele = jnp.transpose(teleport.reshape(vectors, blocks_piece, tile_side), (1, 0, 2))

    all_axes = ("src", "dst")
    all_count = src_count * dst_count

    def tree_sum(value, axis, size):
        if size & (size - 1):
            return lax.psum(value, axis)
        shift = 1
        while shift < size:
            value = value + lax.ppermute(value, axis, [(i, i ^ shift) for i in range(size)])
            shift *= 2
        return value

    exchange = dst_count & (dst_count - 1) == 0
    if exchange:
        kernel_cols = (
            (own_cols // blocks_piece) ^ dst_index
        ) * blocks_piece + own_cols % blocks_piece
    else:
        kernel_cols = own_cols

    payload_rows = blocks_piece * vectors
    pad_rows = 8

    def with_lost_row(body, lost):
        lead = body.shape[:-2]
        extra = jnp.zeros(lead + (pad_rows, tile_side), jnp.float32)
        extra = extra.at[..., 0, :vectors].set(jnp.broadcast_to(lost, lead + (vectors,)))
        return jnp.concatenate([body, extra], axis=-2)

    def spread_columns(blocks, lost):
        payload = with_lost_row(blocks.reshape(payload_rows, tile_side), lost)[None]
        if exchange:
            pieces = [payload] + [
                lax.ppermute(payload, "dst", [(i, i ^ v) for i in range(dst_count)])
                for v in range(1, dst_count)
            ]
            payload = jnp.concatenate(pieces, axis=0)
        else:
            payload = lax.all_gather(payload, "dst", axis=0, tiled=True)
        lost_dst = jnp.sum(payload[:, payload_rows, :vectors], axis=0)
        return payload, lost_dst

    def reduce_rows(accumulated, lost):
        n = src_count
        chunks = accumulated.at[:, payload_rows, :vectors].set(
            jnp.broadcast_to(lost, (n, vectors))
        )
        if n % 2 == 0:
            half = n // 2
            paired = chunks.reshape(half, 2, *chunks.shape[1:])
            core = src_index % 2
            keep = lax.dynamic_index_in_dim(paired, core, 1, keepdims=False)
            give = lax.dynamic_index_in_dim(paired, 1 - core, 1, keepdims=False)
            part = keep + lax.ppermute(give, "src", [(i, i ^ 1) for i in range(n)])
            chip = src_index // 2
            total = lax.dynamic_index_in_dim(part, chip, 0, keepdims=False)
            for shift in range(1, half):
                send = lax.dynamic_index_in_dim(part, (chip + shift) % half, 0, keepdims=False)
                pairs = [(i, ((i // 2 + shift) % half) * 2 + i % 2) for i in range(n)]
                total = total + lax.ppermute(send, "src", pairs)
        else:
            total = lax.dynamic_index_in_dim(chunks, src_index, 0, keepdims=False)
            for shift in range(1, n):
                send = lax.dynamic_index_in_dim(chunks, (src_index + shift) % n, 0, keepdims=False)
                total = total + lax.ppermute(send, "src", [(i, (i + shift) % n) for i in range(n)])
        image = total[:payload_rows].reshape(blocks_piece, vectors, tile_side)
        return image, total[payload_rows, :vectors]

    def lost_partial(blocks):
        return jnp.sum(blocks * piece_dangling[:, None, None], axis=(0, 2))

    def relaxation(blocks, lost_sum=None):
        gathered, lost_dst = spread_columns(blocks, lost_partial(blocks))
        accumulated = tile_pass(
            "image", gathered, tiles, own_rows, kernel_cols, live_mask, block_count,
            row_blocks, vectors,
        )
        image, lost_total = reduce_rows(accumulated, lost_dst)
        if lost_sum is None:
            lost_sum = lost_total
        return (
            damping * (image + (lost_sum / page_total)[None, :, None] * tele)
            + (1.0 - damping) * tele
        )

    tele_sums = jnp.sum(tele, axis=2)

    relaxed_one = relaxation(tele)
    relaxed_two = relaxation(relaxed_one)

    gathered, _ = spread_columns(relaxed_two, jnp.zeros((vectors,), jnp.float32))
    entries = tile_pass(
        "entries", gathered, tiles, own_rows, kernel_cols, live_mask, block_count,
        row_blocks, vectors,
    ).sum(axis=2)
    block_sums = jnp.sum(relaxed_two, axis=2)
    row_agg = agg_of_block[row_global]
    col_agg = agg_of_block[col_global]
    fields = [
        entries.reshape(-1),
        row_agg.astype(jnp.float32),
        col_agg.astype(jnp.float32),
        block_sums.reshape(-1),
        tele_sums.reshape(-1),
        piece_agg.astype(jnp.float32),
        piece_dangling,
    ]
    sizes = [f.shape[0] for f in fields]
    shared = jnp.concatenate(fields)[None]
    if exchange and src_count % 2 == 0:
        shared = jnp.concatenate(
            [shared]
            + [
                lax.ppermute(shared, "dst", [(i, i ^ v) for i in range(dst_count)])
                for v in range(1, dst_count)
            ],
            axis=0,
        )
        shared = jnp.concatenate(
            [shared, lax.ppermute(shared, "src", [(i, i ^ 1) for i in range(src_count)])], axis=0
        )
        half = src_count // 2
        pieces = [shared]
        for shift in range(1, half):
            pairs = [(i, ((i // 2 + shift) % half) * 2 + i % 2) for i in range(src_count)]
            pieces.append(lax.ppermute(shared, "src", pairs))
        shared = jnp.concatenate(pieces, axis=0)
    else:
        shared = lax.all_gather(shared[0], all_axes, axis=0, tiled=False)
    offsets = [0]
    for size in sizes:
        offsets.append(offsets[-1] + size)
    every = [shared[:, offsets[i]:offsets[i + 1]] for i in range(len(sizes))]
    all_entries = every[0].reshape(-1, vectors)
    all_row_hot = (every[1].reshape(-1)[:, None] == agg_range[None, :].astype(jnp.float32))
    all_col_hot = (every[2].reshape(-1)[:, None] == agg_range[None, :].astype(jnp.float32))
    all_row_hot = all_row_hot.astype(jnp.float32)
    all_col_hot = all_col_hot.astype(jnp.float32)
    all_block_sums = every[3].reshape(-1, vectors)
    all_tele_sums = every[4].reshape(-1, vectors)
    all_block_hot = (every[5].reshape(-1)[:, None] == agg_range[None, :].astype(jnp.float32))
    all_block_hot = all_block_hot.astype(jnp.float32)
    all_dangling = every[6].reshape(-1)
    totals = jnp.einsum("bk,ba->ka", all_block_sums, all_block_hot, precision=highest)
    lost_mass = jnp.einsum(
        "bk,ba->ka", all_block_sums * all_dangling[:, None], all_block_hot, precision=highest
    )
    weight = jnp.einsum("bk,ba->ka", all_tele_sums, all_block_hot, precision=highest)
    inflow_one = jnp.einsum("tk,ta->ka", all_entries, all_row_hot, precision=highest)

    def coarse_sweep(inflow, ratios):
        carried = jnp.sum(lost_mass * ratios, axis=1)
        return (
            damping * (inflow + (carried / page_total)[:, None] * weight)
            + (1.0 - damping) * weight
        )

    level_one = coarse_sweep(inflow_one, jnp.ones((vectors, agg_count), jnp.float32))
    ratios_one = level_one / totals
    ratio_at_tile = jnp.einsum("ka,ta->tk", ratios_one, all_col_hot, precision=highest)
    inflow_two = jnp.einsum(
        "tk,ta->ka", all_entries * ratio_at_tile, all_row_hot, precision=highest
    )
    level_two = coarse_sweep(inflow_two, ratios_one)
    ratios_two = level_two / totals
    rescale = jnp.einsum("ka,ba->bk", ratios_two, piece_hot, precision=highest)
    corrected = relaxed_two * rescale[:, :, None]
    lost_two = jnp.sum(lost_mass * ratios_two, axis=1)

    position = lax.axis_index(all_axes)
    owned_count = agg_count // (src_count * dst_count)
    owned = lax.dynamic_slice_in_dim(owner_list, position * owned_count, owned_count)
    owned_hot = (owned[:, None] == agg_range[None, :]).astype(jnp.float32)
    coarse_out = jnp.einsum("ka,qa->kq", level_two, owned_hot, precision=highest)

    relaxed_three = relaxation(corrected, lost_two)
    relaxed_four = relaxation(relaxed_three)
    fine_out = jnp.transpose(relaxed_four, (1, 0, 2)).reshape(teleport.shape)
    return fine_out, coarse_out


def solution(mesh):
    placed = (
        P(None, "dst", "src"),
        P("dst", "src", None, None, None),
        P("dst", "src", None),
        P("dst", "src", None),
        P("dst", "src"),
        P(),
        P(),
        P(),
    )
    return jax.shard_map(
        per_device,
        mesh=mesh,
        in_specs=placed,
        out_specs=(P(None, "dst", "src"), P(None, ("src", "dst"))),
        check_vma=False,
    )
```

```python
import functools

import jax
import jax.numpy as jnp
from jax import lax
from jax.experimental import pallas as pl
from jax.experimental.pallas import tpu as pltpu
from jax.sharding import PartitionSpec as P

damping = 0.85
group_size = 32
highest = lax.Precision.HIGHEST


def tile_kernel(
    mode, blocks_piece, vectors, rows_ref, cols_ref, live_ref, nb_ref, x_ref, t_ref, o_ref
):
    step = pl.program_id(0)
    if mode == "image":

        @pl.when(step == 0)
        def _():
            o_ref[...] = jnp.zeros_like(o_ref)

    @pl.when(step < nb_ref[0])
    def _():
        for g in range(group_size):
            slot = step * group_size + g
            col = cols_ref[slot]
            start = pl.multiple_of((col % blocks_piece) * vectors, vectors)
            picked = x_ref[col // blocks_piece, pl.ds(start, vectors), :].astype(jnp.bfloat16)
            weight = jnp.where(live_ref[slot] != 0, 1.0, 0.0).astype(jnp.bfloat16)
            product = jnp.dot(picked * weight, t_ref[g], preferred_element_type=jnp.float32)
            if mode == "image":
                row = rows_ref[slot]
                at = pl.multiple_of((row % blocks_piece) * vectors, vectors)
                window = (row // blocks_piece, pl.ds(at, vectors), slice(None))
                o_ref[window] = o_ref[window] + product
            else:
                o_ref[g] = product[:, :128] + product[:, 128:]

    if mode == "entries":

        @pl.when(step >= nb_ref[0])
        def _():
            o_ref[...] = jnp.zeros_like(o_ref)


def tile_pass(mode, x_cols, tiles, rows, cols, live, block_count, row_blocks, vectors):
    groups, padded_rows, side = x_cols.shape
    blocks_piece = padded_rows // vectors
    owners = row_blocks // blocks_piece
    slots = tiles.shape[2]
    steps = slots // group_size

    def tile_index(i, rows_ref, cols_ref, live_ref, nb_ref):
        return (0, 0, jnp.minimum(i, nb_ref[0] - 1), 0, 0)

    if mode == "image":
        out_shape = jax.ShapeDtypeStruct((owners, padded_rows, side), jnp.float32)
        out_spec = pl.BlockSpec((owners, padded_rows, side), lambda i, *_: (0, 0, 0))
    else:
        out_shape = jax.ShapeDtypeStruct((slots, vectors, 128), jnp.float32)
        out_spec = pl.BlockSpec((group_size, vectors, 128), lambda i, *_: (i, 0, 0))
    grid_spec = pltpu.PrefetchScalarGridSpec(
        num_scalar_prefetch=4,
        grid=(steps,),
        in_specs=[
            pl.BlockSpec((groups, padded_rows, side), lambda i, *_: (0, 0, 0)),
            pl.BlockSpec((None, None, group_size, side, side), tile_index),
        ],
        out_specs=out_spec,
    )
    return pl.pallas_call(
        functools.partial(tile_kernel, mode, blocks_piece, vectors),
        grid_spec=grid_spec,
        out_shape=out_shape,
        compiler_params=pltpu.CompilerParams(dimension_semantics=("arbitrary",)),
    )(rows, cols, live, block_count, x_cols, tiles)


def per_device(
    teleport, tiles, tile_rows, tile_cols, tile_counts, dangling, agg_of_block, owner_list
):
    vectors = teleport.shape[0]
    piece_width = teleport.shape[2]
    slots_total = tiles.shape[2]
    tile_side = tiles.shape[4]
    blocks_piece = piece_width // tile_side
    src_count = lax.axis_size("src")
    dst_count = lax.axis_size("dst")
    row_blocks = blocks_piece * src_count
    col_blocks = blocks_piece * dst_count
    page_total = row_blocks * dst_count * tile_side
    agg_count = owner_list.shape[0]
    src_index = lax.axis_index("src")
    dst_index = lax.axis_index("dst")
    own_rows = jnp.clip(tile_rows[0, 0], 0, row_blocks - 1)
    own_cols = jnp.clip(tile_cols[0, 0], 0, col_blocks - 1)
    own_count = tile_counts[0, 0]
    col_global = (
        own_cols // blocks_piece * (blocks_piece * src_count)
        + src_index * blocks_piece
        + own_cols % blocks_piece
    )
    row_global = dst_index * row_blocks + own_rows
    slot_range = jnp.arange(slots_total, dtype=jnp.int32)
    live_mask = ((slot_range < own_count) & (dangling[col_global] == 0)).astype(jnp.int32)
    steps = slots_total // group_size
    block_count = jnp.clip((own_count + group_size - 1) // group_size, 1, steps).reshape(1)
    block_count = block_count.astype(jnp.int32)
    piece_first = dst_index * row_blocks + src_index * blocks_piece
    piece_dangling = lax.dynamic_slice_in_dim(dangling, piece_first, blocks_piece).astype(
        jnp.float32
    )
    piece_agg = lax.dynamic_slice_in_dim(agg_of_block, piece_first, blocks_piece)
    agg_range = jnp.arange(agg_count, dtype=jnp.int32)
    piece_hot = (piece_agg[:, None] == agg_range[None, :]).astype(jnp.float32)
    tele = jnp.transpose(teleport.reshape(vectors, blocks_piece, tile_side), (1, 0, 2))

    all_axes = ("src", "dst")
    all_count = src_count * dst_count

    def tree_sum(value, axis, size):
        if size & (size - 1):
            return lax.psum(value, axis)
        shift = 1
        while shift < size:
            value = value + lax.ppermute(value, axis, [(i, i ^ shift) for i in range(size)])
            shift *= 2
        return value

    exchange = dst_count & (dst_count - 1) == 0
    if exchange:
        kernel_cols = (
            (own_cols // blocks_piece) ^ dst_index
        ) * blocks_piece + own_cols % blocks_piece
    else:
        kernel_cols = own_cols

    payload_rows = blocks_piece * vectors
    pad_rows = 8

    def with_lost_row(body, lost):
        lead = body.shape[:-2]
        extra = jnp.zeros(lead + (pad_rows, tile_side), jnp.float32)
        extra = extra.at[..., 0, :vectors].set(jnp.broadcast_to(lost, lead + (vectors,)))
        return jnp.concatenate([body, extra], axis=-2)

    def spread_columns(blocks, lost):
        payload = with_lost_row(blocks.reshape(payload_rows, tile_side), lost)[None]
        if exchange:
            pieces = [payload] + [
                lax.ppermute(payload, "dst", [(i, i ^ v) for i in range(dst_count)])
                for v in range(1, dst_count)
            ]
            payload = jnp.concatenate(pieces, axis=0)
        else:
            payload = lax.all_gather(payload, "dst", axis=0, tiled=True)
        lost_dst = jnp.sum(payload[:, payload_rows, :vectors], axis=0)
        return payload, lost_dst

    def reduce_rows(accumulated, lost):
        n = src_count
        chunks = accumulated.at[:, payload_rows, :vectors].set(
            jnp.broadcast_to(lost, (n, vectors))
        )
        if n % 2 == 0:
            half = n // 2
            paired = chunks.reshape(half, 2, *chunks.shape[1:])
            core = src_index % 2
            keep = lax.dynamic_index_in_dim(paired, core, 1, keepdims=False)
            give = lax.dynamic_index_in_dim(paired, 1 - core, 1, keepdims=False)
            part = keep + lax.ppermute(give, "src", [(i, i ^ 1) for i in range(n)])
            chip = src_index // 2
            total = lax.dynamic_index_in_dim(part, chip, 0, keepdims=False)
            for shift in range(1, half):
                send = lax.dynamic_index_in_dim(part, (chip + shift) % half, 0, keepdims=False)
                pairs = [(i, ((i // 2 + shift) % half) * 2 + i % 2) for i in range(n)]
                total = total + lax.ppermute(send, "src", pairs)
        else:
            total = lax.dynamic_index_in_dim(chunks, src_index, 0, keepdims=False)
            for shift in range(1, n):
                send = lax.dynamic_index_in_dim(chunks, (src_index + shift) % n, 0, keepdims=False)
                total = total + lax.ppermute(send, "src", [(i, (i + shift) % n) for i in range(n)])
        image = total[:payload_rows].reshape(blocks_piece, vectors, tile_side)
        return image, total[payload_rows, :vectors]

    def lost_partial(blocks):
        return jnp.sum(blocks * piece_dangling[:, None, None], axis=(0, 2))

    def relaxation(blocks, lost_sum=None, gathered=None):
        if gathered is None:
            gathered, lost_dst = spread_columns(blocks, lost_partial(blocks))
        else:
            lost_dst = jnp.zeros((vectors,), jnp.float32)
        accumulated = tile_pass(
            "image", gathered, tiles, own_rows, kernel_cols, live_mask, block_count,
            row_blocks, vectors,
        )
        image, lost_total = reduce_rows(accumulated, lost_dst)
        if lost_sum is None:
            lost_sum = lost_total
        return (
            damping * (image + (lost_sum / page_total)[None, :, None] * tele)
            + (1.0 - damping) * tele
        )

    tele_sums = jnp.sum(tele, axis=2)

    relaxed_one = relaxation(tele)
    relaxed_two = relaxation(relaxed_one)

    gathered, _ = spread_columns(relaxed_two, jnp.zeros((vectors,), jnp.float32))
    entries = tile_pass(
        "entries", gathered, tiles, own_rows, kernel_cols, live_mask, block_count,
        row_blocks, vectors,
    ).sum(axis=2)
    block_sums = jnp.sum(relaxed_two, axis=2)
    row_agg = agg_of_block[row_global]
    col_agg = agg_of_block[col_global]
    fields = [
        entries.reshape(-1),
        row_agg.astype(jnp.float32),
        col_agg.astype(jnp.float32),
        block_sums.reshape(-1),
        tele_sums.reshape(-1),
        piece_agg.astype(jnp.float32),
        piece_dangling,
    ]
    sizes = [f.shape[0] for f in fields]
    shared = jnp.concatenate(fields)[None]
    if exchange and src_count % 2 == 0:
        shared = jnp.concatenate(
            [shared]
            + [
                lax.ppermute(shared, "dst", [(i, i ^ v) for i in range(dst_count)])
                for v in range(1, dst_count)
            ],
            axis=0,
        )
        shared = jnp.concatenate(
            [shared, lax.ppermute(shared, "src", [(i, i ^ 1) for i in range(src_count)])], axis=0
        )
        half = src_count // 2
        pieces = [shared]
        for shift in range(1, half):
            pairs = [(i, ((i // 2 + shift) % half) * 2 + i % 2) for i in range(src_count)]
            pieces.append(lax.ppermute(shared, "src", pairs))
        shared = jnp.concatenate(pieces, axis=0)
    else:
        shared = lax.all_gather(shared[0], all_axes, axis=0, tiled=False)
    offsets = [0]
    for size in sizes:
        offsets.append(offsets[-1] + size)
    every = [shared[:, offsets[i]:offsets[i + 1]] for i in range(len(sizes))]
    all_entries = every[0].reshape(-1, vectors)
    all_row_hot = (every[1].reshape(-1)[:, None] == agg_range[None, :].astype(jnp.float32))
    all_col_hot = (every[2].reshape(-1)[:, None] == agg_range[None, :].astype(jnp.float32))
    all_row_hot = all_row_hot.astype(jnp.float32)
    all_col_hot = all_col_hot.astype(jnp.float32)
    all_block_sums = every[3].reshape(-1, vectors)
    all_tele_sums = every[4].reshape(-1, vectors)
    all_block_hot = (every[5].reshape(-1)[:, None] == agg_range[None, :].astype(jnp.float32))
    all_block_hot = all_block_hot.astype(jnp.float32)
    all_dangling = every[6].reshape(-1)
    totals = jnp.einsum("bk,ba->ka", all_block_sums, all_block_hot, precision=highest)
    lost_mass = jnp.einsum(
        "bk,ba->ka", all_block_sums * all_dangling[:, None], all_block_hot, precision=highest
    )
    weight = jnp.einsum("bk,ba->ka", all_tele_sums, all_block_hot, precision=highest)
    inflow_one = jnp.einsum("tk,ta->ka", all_entries, all_row_hot, precision=highest)

    def coarse_sweep(inflow, ratios):
        carried = jnp.sum(lost_mass * ratios, axis=1)
        return (
            damping * (inflow + (carried / page_total)[:, None] * weight)
            + (1.0 - damping) * weight
        )

    level_one = coarse_sweep(inflow_one, jnp.ones((vectors, agg_count), jnp.float32))
    ratios_one = level_one / totals
    ratio_at_tile = jnp.einsum("ka,ta->tk", ratios_one, all_col_hot, precision=highest)
    inflow_two = jnp.einsum(
        "tk,ta->ka", all_entries * ratio_at_tile, all_row_hot, precision=highest
    )
    level_two = coarse_sweep(inflow_two, ratios_one)
    ratios_two = level_two / totals
    groups = gathered.shape[0]
    group_ids = jnp.arange(groups, dtype=jnp.int32)
    if exchange:
        group_ids = group_ids ^ dst_index
    block_ids = (
        group_ids[:, None] * row_blocks
        + src_index * blocks_piece
        + jnp.arange(blocks_piece, dtype=jnp.int32)[None, :]
    )
    block_scale = jnp.take(ratios_two, agg_of_block[block_ids.reshape(-1)], axis=1)
    block_scale = block_scale.T.reshape(groups, payload_rows, 1)
    corrected_cols = jnp.concatenate(
        [
            gathered[:, :payload_rows, :] * block_scale,
            jnp.zeros((groups, pad_rows, tile_side), jnp.float32),
        ],
        axis=1,
    )
    lost_two = jnp.sum(lost_mass * ratios_two, axis=1)

    position = lax.axis_index(all_axes)
    owned_count = agg_count // (src_count * dst_count)
    owned = lax.dynamic_slice_in_dim(owner_list, position * owned_count, owned_count)
    owned_hot = (owned[:, None] == agg_range[None, :]).astype(jnp.float32)
    coarse_out = jnp.einsum("ka,qa->kq", level_two, owned_hot, precision=highest)

    relaxed_three = relaxation(None, lost_two, corrected_cols)
    relaxed_four = relaxation(relaxed_three)
    fine_out = jnp.transpose(relaxed_four, (1, 0, 2)).reshape(teleport.shape)
    return fine_out, coarse_out


def solution(mesh):
    placed = (
        P(None, "dst", "src"),
        P("dst", "src", None, None, None),
        P("dst", "src", None),
        P("dst", "src", None),
        P("dst", "src"),
        P(),
        P(),
        P(),
    )
    return jax.shard_map(
        per_device,
        mesh=mesh,
        in_specs=placed,
        out_specs=(P(None, "dst", "src"), P(None, ("src", "dst"))),
        check_vma=False,
    )
```

```python
import functools

import jax
import jax.numpy as jnp
from jax import lax
from jax.experimental import pallas as pl
from jax.experimental.pallas import tpu as pltpu
from jax.sharding import PartitionSpec as P

damping = 0.85
group_size = 32
highest = lax.Precision.HIGHEST


def tile_kernel(
    mode, blocks_piece, vectors, rows_ref, cols_ref, live_ref, nb_ref, x_ref, t_ref, *refs
):
    step = pl.program_id(0)
    if mode == "image":
        lost_ref, o_ref = refs
        body_rows = blocks_piece * vectors

        @pl.when(step == 0)
        def _():
            o_ref[:, :body_rows, :] = jnp.zeros((o_ref.shape[0], body_rows, o_ref.shape[2]), o_ref.dtype)
            o_ref[:, body_rows:, :] = jnp.broadcast_to(
                lost_ref[...][None], (o_ref.shape[0],) + lost_ref.shape
            )
    else:
        (o_ref,) = refs

    @pl.when(step < nb_ref[0])
    def _():
        for g in range(group_size):
            slot = step * group_size + g
            col = cols_ref[slot]
            start = pl.multiple_of((col % blocks_piece) * vectors, vectors)
            picked = x_ref[col // blocks_piece, pl.ds(start, vectors), :].astype(jnp.bfloat16)
            weight = jnp.where(live_ref[slot] != 0, 1.0, 0.0).astype(jnp.bfloat16)
            product = jnp.dot(picked * weight, t_ref[g], preferred_element_type=jnp.float32)
            if mode == "image":
                row = rows_ref[slot]
                at = pl.multiple_of((row % blocks_piece) * vectors, vectors)
                window = (row // blocks_piece, pl.ds(at, vectors), slice(None))
                o_ref[window] = o_ref[window] + product
            else:
                o_ref[g] = product[:, :128] + product[:, 128:]

    if mode == "entries":

        @pl.when(step >= nb_ref[0])
        def _():
            o_ref[...] = jnp.zeros_like(o_ref)


def tile_pass(mode, x_cols, tiles, rows, cols, live, block_count, row_blocks, vectors, lost=None):
    groups, padded_rows, side = x_cols.shape
    blocks_piece = padded_rows // vectors
    owners = row_blocks // blocks_piece
    slots = tiles.shape[2]
    steps = slots // group_size

    def tile_index(i, rows_ref, cols_ref, live_ref, nb_ref):
        return (0, 0, jnp.minimum(i, nb_ref[0] - 1), 0, 0)

    if mode == "image":
        out_shape = jax.ShapeDtypeStruct((owners, padded_rows, side), jnp.float32)
        out_spec = pl.BlockSpec((owners, padded_rows, side), lambda i, *_: (0, 0, 0))
    else:
        out_shape = jax.ShapeDtypeStruct((slots, vectors, 128), jnp.float32)
        out_spec = pl.BlockSpec((group_size, vectors, 128), lambda i, *_: (i, 0, 0))
    in_specs = [
        pl.BlockSpec((groups, padded_rows, side), lambda i, *_: (0, 0, 0)),
        pl.BlockSpec((None, None, group_size, side, side), tile_index),
    ]
    operands = [x_cols, tiles]
    if mode == "image":
        pad = padded_rows - blocks_piece * vectors
        lost_block = jnp.zeros((pad, side), jnp.float32).at[0, :vectors].set(lost)
        in_specs.append(pl.BlockSpec((pad, side), lambda i, *_: (0, 0)))
        operands.append(lost_block)
    grid_spec = pltpu.PrefetchScalarGridSpec(
        num_scalar_prefetch=4,
        grid=(steps,),
        in_specs=in_specs,
        out_specs=out_spec,
    )
    return pl.pallas_call(
        functools.partial(tile_kernel, mode, blocks_piece, vectors),
        grid_spec=grid_spec,
        out_shape=out_shape,
        compiler_params=pltpu.CompilerParams(dimension_semantics=("arbitrary",)),
    )(rows, cols, live, block_count, *operands)


def per_device(
    teleport, tiles, tile_rows, tile_cols, tile_counts, dangling, agg_of_block, owner_list
):
    vectors = teleport.shape[0]
    piece_width = teleport.shape[2]
    slots_total = tiles.shape[2]
    tile_side = tiles.shape[4]
    blocks_piece = piece_width // tile_side
    src_count = lax.axis_size("src")
    dst_count = lax.axis_size("dst")
    row_blocks = blocks_piece * src_count
    col_blocks = blocks_piece * dst_count
    page_total = row_blocks * dst_count * tile_side
    agg_count = owner_list.shape[0]
    src_index = lax.axis_index("src")
    dst_index = lax.axis_index("dst")
    own_rows = jnp.clip(tile_rows[0, 0], 0, row_blocks - 1)
    own_cols = jnp.clip(tile_cols[0, 0], 0, col_blocks - 1)
    own_count = tile_counts[0, 0]
    col_global = (
        own_cols // blocks_piece * (blocks_piece * src_count)
        + src_index * blocks_piece
        + own_cols % blocks_piece
    )
    row_global = dst_index * row_blocks + own_rows
    slot_range = jnp.arange(slots_total, dtype=jnp.int32)
    live_mask = ((slot_range < own_count) & (dangling[col_global] == 0)).astype(jnp.int32)
    steps = slots_total // group_size
    block_count = jnp.clip((own_count + group_size - 1) // group_size, 1, steps).reshape(1)
    block_count = block_count.astype(jnp.int32)
    piece_first = dst_index * row_blocks + src_index * blocks_piece
    piece_dangling = lax.dynamic_slice_in_dim(dangling, piece_first, blocks_piece).astype(
        jnp.float32
    )
    piece_agg = lax.dynamic_slice_in_dim(agg_of_block, piece_first, blocks_piece)
    agg_range = jnp.arange(agg_count, dtype=jnp.int32)
    piece_hot = (piece_agg[:, None] == agg_range[None, :]).astype(jnp.float32)
    tele = jnp.transpose(teleport.reshape(vectors, blocks_piece, tile_side), (1, 0, 2))

    all_axes = ("src", "dst")
    all_count = src_count * dst_count

    def tree_sum(value, axis, size):
        if size & (size - 1):
            return lax.psum(value, axis)
        shift = 1
        while shift < size:
            value = value + lax.ppermute(value, axis, [(i, i ^ shift) for i in range(size)])
            shift *= 2
        return value

    exchange = dst_count & (dst_count - 1) == 0
    if exchange:
        kernel_cols = (
            (own_cols // blocks_piece) ^ dst_index
        ) * blocks_piece + own_cols % blocks_piece
    else:
        kernel_cols = own_cols

    payload_rows = blocks_piece * vectors
    pad_rows = 8

    def with_lost_row(body, lost):
        lead = body.shape[:-2]
        extra = jnp.zeros(lead + (pad_rows, tile_side), jnp.float32)
        extra = extra.at[..., 0, :vectors].set(jnp.broadcast_to(lost, lead + (vectors,)))
        return jnp.concatenate([body, extra], axis=-2)

    row_owner = own_rows // blocks_piece
    if src_count % 2 == 0:
        half = src_count // 2
        chip = src_index // 2
        position = ((row_owner % 2) ^ (src_index % 2)) * half + (row_owner // 2 - chip) % half
    else:
        position = (row_owner - src_index) % src_count
    kernel_rows = position * blocks_piece + own_rows % blocks_piece

    def spread_columns(blocks, lost):
        payload = with_lost_row(blocks.reshape(payload_rows, tile_side), lost)[None]
        if exchange:
            pieces = [payload] + [
                lax.ppermute(payload, "dst", [(i, i ^ v) for i in range(dst_count)])
                for v in range(1, dst_count)
            ]
            payload = jnp.concatenate(pieces, axis=0)
        else:
            payload = lax.all_gather(payload, "dst", axis=0, tiled=True)
        lost_dst = jnp.sum(payload[:, payload_rows, :vectors], axis=0)
        return payload, lost_dst

    def reduce_rows(chunks):
        n = src_count
        if n % 2 == 0:
            half = n // 2
            part = chunks[:half] + lax.ppermute(chunks[half:], "src", [(i, i ^ 1) for i in range(n)])
            total = part[0]
            for shift in range(1, half):
                pairs = [(i, ((i // 2 + shift) % half) * 2 + i % 2) for i in range(n)]
                total = total + lax.ppermute(part[shift], "src", pairs)
        else:
            total = chunks[0]
            for shift in range(1, n):
                pairs = [(i, (i + shift) % n) for i in range(n)]
                total = total + lax.ppermute(chunks[shift], "src", pairs)
        image = total[:payload_rows].reshape(blocks_piece, vectors, tile_side)
        return image, total[payload_rows, :vectors]

    def lost_partial(blocks):
        return jnp.sum(blocks * piece_dangling[:, None, None], axis=(0, 2))

    def relaxation(blocks, lost_sum=None, gathered=None):
        if gathered is None:
            gathered, lost_dst = spread_columns(blocks, lost_partial(blocks))
        else:
            lost_dst = jnp.zeros((vectors,), jnp.float32)
        accumulated = tile_pass(
            "image", gathered, tiles, kernel_rows, kernel_cols, live_mask, block_count,
            row_blocks, vectors, lost_dst,
        )
        image, lost_total = reduce_rows(accumulated)
        if lost_sum is None:
            lost_sum = lost_total
        return (
            damping * (image + (lost_sum / page_total)[None, :, None] * tele)
            + (1.0 - damping) * tele
        )

    tele_sums = jnp.sum(tele, axis=2)

    relaxed_one = relaxation(tele)
    relaxed_two = relaxation(relaxed_one)

    gathered, _ = spread_columns(relaxed_two, jnp.zeros((vectors,), jnp.float32))
    entries = tile_pass(
        "entries", gathered, tiles, own_rows, kernel_cols, live_mask, block_count,
        row_blocks, vectors,
    ).sum(axis=2)
    block_sums = jnp.sum(relaxed_two, axis=2)
    row_agg = agg_of_block[row_global]
    col_agg = agg_of_block[col_global]
    fields = [
        entries.reshape(-1),
        row_agg.astype(jnp.float32),
        col_agg.astype(jnp.float32),
        block_sums.reshape(-1),
        tele_sums.reshape(-1),
        piece_agg.astype(jnp.float32),
        piece_dangling,
    ]
    sizes = [f.shape[0] for f in fields]
    shared = jnp.concatenate(fields)[None]
    if exchange and src_count % 2 == 0:
        shared = jnp.concatenate(
            [shared]
            + [
                lax.ppermute(shared, "dst", [(i, i ^ v) for i in range(dst_count)])
                for v in range(1, dst_count)
            ],
            axis=0,
        )
        shared = jnp.concatenate(
            [shared, lax.ppermute(shared, "src", [(i, i ^ 1) for i in range(src_count)])], axis=0
        )
        half = src_count // 2
        pieces = [shared]
        for shift in range(1, half):
            pairs = [(i, ((i // 2 + shift) % half) * 2 + i % 2) for i in range(src_count)]
            pieces.append(lax.ppermute(shared, "src", pairs))
        shared = jnp.concatenate(pieces, axis=0)
    else:
        shared = lax.all_gather(shared[0], all_axes, axis=0, tiled=False)
    offsets = [0]
    for size in sizes:
        offsets.append(offsets[-1] + size)
    every = [shared[:, offsets[i]:offsets[i + 1]] for i in range(len(sizes))]
    all_entries = every[0].reshape(-1, vectors)
    all_row_hot = (every[1].reshape(-1)[:, None] == agg_range[None, :].astype(jnp.float32))
    all_col_hot = (every[2].reshape(-1)[:, None] == agg_range[None, :].astype(jnp.float32))
    all_row_hot = all_row_hot.astype(jnp.float32)
    all_col_hot = all_col_hot.astype(jnp.float32)
    all_block_sums = every[3].reshape(-1, vectors)
    all_tele_sums = every[4].reshape(-1, vectors)
    all_block_hot = (every[5].reshape(-1)[:, None] == agg_range[None, :].astype(jnp.float32))
    all_block_hot = all_block_hot.astype(jnp.float32)
    all_dangling = every[6].reshape(-1)
    totals = jnp.einsum("bk,ba->ka", all_block_sums, all_block_hot, precision=highest)
    lost_mass = jnp.einsum(
        "bk,ba->ka", all_block_sums * all_dangling[:, None], all_block_hot, precision=highest
    )
    weight = jnp.einsum("bk,ba->ka", all_tele_sums, all_block_hot, precision=highest)
    inflow_one = jnp.einsum("tk,ta->ka", all_entries, all_row_hot, precision=highest)

    def coarse_sweep(inflow, ratios):
        carried = jnp.sum(lost_mass * ratios, axis=1)
        return (
            damping * (inflow + (carried / page_total)[:, None] * weight)
            + (1.0 - damping) * weight
        )

    level_one = coarse_sweep(inflow_one, jnp.ones((vectors, agg_count), jnp.float32))
    ratios_one = level_one / totals
    ratio_at_tile = jnp.einsum("ka,ta->tk", ratios_one, all_col_hot, precision=highest)
    inflow_two = jnp.einsum(
        "tk,ta->ka", all_entries * ratio_at_tile, all_row_hot, precision=highest
    )
    level_two = coarse_sweep(inflow_two, ratios_one)
    ratios_two = level_two / totals
    groups = gathered.shape[0]
    group_ids = jnp.arange(groups, dtype=jnp.int32)
    if exchange:
        group_ids = group_ids ^ dst_index
    block_ids = (
        group_ids[:, None] * row_blocks
        + src_index * blocks_piece
        + jnp.arange(blocks_piece, dtype=jnp.int32)[None, :]
    )
    block_scale = jnp.take(ratios_two, agg_of_block[block_ids.reshape(-1)], axis=1)
    block_scale = block_scale.T.reshape(groups, payload_rows, 1)
    corrected_cols = jnp.concatenate(
        [
            gathered[:, :payload_rows, :] * block_scale,
            jnp.zeros((groups, pad_rows, tile_side), jnp.float32),
        ],
        axis=1,
    )
    lost_two = jnp.sum(lost_mass * ratios_two, axis=1)

    position = lax.axis_index(all_axes)
    owned_count = agg_count // (src_count * dst_count)
    owned = lax.dynamic_slice_in_dim(owner_list, position * owned_count, owned_count)
    owned_hot = (owned[:, None] == agg_range[None, :]).astype(jnp.float32)
    coarse_out = jnp.einsum("ka,qa->kq", level_two, owned_hot, precision=highest)

    relaxed_three = relaxation(None, lost_two, corrected_cols)
    relaxed_four = relaxation(relaxed_three)
    fine_out = jnp.transpose(relaxed_four, (1, 0, 2)).reshape(teleport.shape)
    return fine_out, coarse_out


def solution(mesh):
    placed = (
        P(None, "dst", "src"),
        P("dst", "src", None, None, None),
        P("dst", "src", None),
        P("dst", "src", None),
        P("dst", "src"),
        P(),
        P(),
        P(),
    )
    return jax.shard_map(
        per_device,
        mesh=mesh,
        in_specs=placed,
        out_specs=(P(None, "dst", "src"), P(None, ("src", "dst"))),
        check_vma=False,
    )
```

```python
import functools

import jax
import jax.numpy as jnp
from jax import lax
from jax.experimental import pallas as pl
from jax.experimental.pallas import tpu as pltpu
from jax.sharding import PartitionSpec as P

damping = 0.85
group_size = 32
highest = lax.Precision.HIGHEST


def tile_kernel(
    mode, blocks_piece, vectors, rows_ref, cols_ref, live_ref, nb_ref, x_ref, t_ref, *refs
):
    step = pl.program_id(0)
    if mode == "image":
        lost_ref, o_ref = refs
        body_rows = blocks_piece * vectors

        @pl.when(step == 0)
        def _():
            o_ref[:, :body_rows, :] = jnp.zeros((o_ref.shape[0], body_rows, o_ref.shape[2]), o_ref.dtype)
            o_ref[:, body_rows:, :] = jnp.broadcast_to(
                lost_ref[...][None], (o_ref.shape[0],) + lost_ref.shape
            )
    else:
        (o_ref,) = refs

    @pl.when(step < nb_ref[0])
    def _():
        for g in range(group_size):
            slot = step * group_size + g
            col = cols_ref[slot]
            start = pl.multiple_of((col % blocks_piece) * vectors, vectors)
            picked = x_ref[col // blocks_piece, pl.ds(start, vectors), :].astype(jnp.bfloat16)
            weight = jnp.where(live_ref[slot] != 0, 1.0, 0.0).astype(jnp.bfloat16)
            product = jnp.dot(picked * weight, t_ref[g], preferred_element_type=jnp.float32)
            if mode == "image":
                row = rows_ref[slot]
                at = pl.multiple_of((row % blocks_piece) * vectors, vectors)
                window = (row // blocks_piece, pl.ds(at, vectors), slice(None))
                o_ref[window] = o_ref[window] + product
            else:
                o_ref[g] = product[:, :128] + product[:, 128:]

    if mode == "entries":

        @pl.when(step >= nb_ref[0])
        def _():
            o_ref[...] = jnp.zeros_like(o_ref)


def tile_pass(mode, x_cols, tiles, rows, cols, live, block_count, row_blocks, vectors, lost=None):
    groups, padded_rows, side = x_cols.shape
    blocks_piece = padded_rows // vectors
    owners = row_blocks // blocks_piece
    slots = tiles.shape[2]
    steps = slots // group_size

    def tile_index(i, rows_ref, cols_ref, live_ref, nb_ref):
        return (0, 0, jnp.minimum(i, nb_ref[0] - 1), 0, 0)

    if mode == "image":
        out_shape = jax.ShapeDtypeStruct((owners, padded_rows, side), jnp.float32)
        out_spec = pl.BlockSpec((owners, padded_rows, side), lambda i, *_: (0, 0, 0))
    else:
        out_shape = jax.ShapeDtypeStruct((slots, vectors, 128), jnp.float32)
        out_spec = pl.BlockSpec((group_size, vectors, 128), lambda i, *_: (i, 0, 0))
    in_specs = [
        pl.BlockSpec((groups, padded_rows, side), lambda i, *_: (0, 0, 0)),
        pl.BlockSpec((None, None, group_size, side, side), tile_index),
    ]
    operands = [x_cols, tiles]
    if mode == "image":
        pad = padded_rows - blocks_piece * vectors
        lost_block = jnp.zeros((pad, side), jnp.float32).at[0, :vectors].set(lost)
        in_specs.append(pl.BlockSpec((pad, side), lambda i, *_: (0, 0)))
        operands.append(lost_block)
    grid_spec = pltpu.PrefetchScalarGridSpec(
        num_scalar_prefetch=4,
        grid=(steps,),
        in_specs=in_specs,
        out_specs=out_spec,
    )
    return pl.pallas_call(
        functools.partial(tile_kernel, mode, blocks_piece, vectors),
        grid_spec=grid_spec,
        out_shape=out_shape,
        compiler_params=pltpu.CompilerParams(dimension_semantics=("arbitrary",)),
    )(rows, cols, live, block_count, *operands)


def split_three(value):
    high = lax.reduce_precision(value, exponent_bits=8, mantissa_bits=7)
    rest = value - high
    middle = lax.reduce_precision(rest, exponent_bits=8, mantissa_bits=7)
    low = lax.reduce_precision(rest - middle, exponent_bits=8, mantissa_bits=7)
    return jnp.stack([high, middle, low]).astype(jnp.bfloat16)


def select_dot(spec, value, one_hot):
    parts = jnp.einsum(
        "p" + spec.split(",")[0] + "," + spec.split(",")[1].split("->")[0] + "->p"
        + spec.split("->")[1],
        split_three(value),
        one_hot,
        preferred_element_type=jnp.float32,
    )
    return jnp.sum(parts, axis=0)


def per_device(
    teleport, tiles, tile_rows, tile_cols, tile_counts, dangling, agg_of_block, owner_list
):
    vectors = teleport.shape[0]
    piece_width = teleport.shape[2]
    slots_total = tiles.shape[2]
    tile_side = tiles.shape[4]
    blocks_piece = piece_width // tile_side
    src_count = lax.axis_size("src")
    dst_count = lax.axis_size("dst")
    row_blocks = blocks_piece * src_count
    col_blocks = blocks_piece * dst_count
    page_total = row_blocks * dst_count * tile_side
    agg_count = owner_list.shape[0]
    src_index = lax.axis_index("src")
    dst_index = lax.axis_index("dst")
    own_rows = jnp.clip(tile_rows[0, 0], 0, row_blocks - 1)
    own_cols = jnp.clip(tile_cols[0, 0], 0, col_blocks - 1)
    own_count = tile_counts[0, 0]
    col_global = (
        own_cols // blocks_piece * (blocks_piece * src_count)
        + src_index * blocks_piece
        + own_cols % blocks_piece
    )
    row_global = dst_index * row_blocks + own_rows
    slot_range = jnp.arange(slots_total, dtype=jnp.int32)
    live_mask = ((slot_range < own_count) & (dangling[col_global] == 0)).astype(jnp.int32)
    steps = slots_total // group_size
    block_count = jnp.clip((own_count + group_size - 1) // group_size, 1, steps).reshape(1)
    block_count = block_count.astype(jnp.int32)
    piece_first = dst_index * row_blocks + src_index * blocks_piece
    piece_dangling = lax.dynamic_slice_in_dim(dangling, piece_first, blocks_piece).astype(
        jnp.float32
    )
    piece_agg = lax.dynamic_slice_in_dim(agg_of_block, piece_first, blocks_piece)
    agg_range = jnp.arange(agg_count, dtype=jnp.int32)
    piece_hot = (piece_agg[:, None] == agg_range[None, :]).astype(jnp.float32)
    tele = jnp.transpose(teleport.reshape(vectors, blocks_piece, tile_side), (1, 0, 2))

    all_axes = ("src", "dst")
    all_count = src_count * dst_count

    def tree_sum(value, axis, size):
        if size & (size - 1):
            return lax.psum(value, axis)
        shift = 1
        while shift < size:
            value = value + lax.ppermute(value, axis, [(i, i ^ shift) for i in range(size)])
            shift *= 2
        return value

    exchange = dst_count & (dst_count - 1) == 0
    if exchange:
        kernel_cols = (
            (own_cols // blocks_piece) ^ dst_index
        ) * blocks_piece + own_cols % blocks_piece
    else:
        kernel_cols = own_cols

    payload_rows = blocks_piece * vectors
    pad_rows = 8

    def with_lost_row(body, lost):
        lead = body.shape[:-2]
        extra = jnp.zeros(lead + (pad_rows, tile_side), jnp.float32)
        extra = extra.at[..., 0, :vectors].set(jnp.broadcast_to(lost, lead + (vectors,)))
        return jnp.concatenate([body, extra], axis=-2)

    row_owner = own_rows // blocks_piece
    if src_count % 2 == 0:
        half = src_count // 2
        chip = src_index // 2
        position = ((row_owner % 2) ^ (src_index % 2)) * half + (row_owner // 2 - chip) % half
    else:
        position = (row_owner - src_index) % src_count
    kernel_rows = position * blocks_piece + own_rows % blocks_piece

    def spread_columns(blocks, lost):
        payload = with_lost_row(blocks.reshape(payload_rows, tile_side), lost)[None]
        if exchange:
            pieces = [payload] + [
                lax.ppermute(payload, "dst", [(i, i ^ v) for i in range(dst_count)])
                for v in range(1, dst_count)
            ]
            payload = jnp.concatenate(pieces, axis=0)
        else:
            payload = lax.all_gather(payload, "dst", axis=0, tiled=True)
        lost_dst = jnp.sum(payload[:, payload_rows, :vectors], axis=0)
        return payload, lost_dst

    def reduce_rows(chunks):
        n = src_count
        if n % 2 == 0:
            half = n // 2
            part = chunks[:half] + lax.ppermute(chunks[half:], "src", [(i, i ^ 1) for i in range(n)])
            total = part[0]
            for shift in range(1, half):
                pairs = [(i, ((i // 2 + shift) % half) * 2 + i % 2) for i in range(n)]
                total = total + lax.ppermute(part[shift], "src", pairs)
        else:
            total = chunks[0]
            for shift in range(1, n):
                pairs = [(i, (i + shift) % n) for i in range(n)]
                total = total + lax.ppermute(chunks[shift], "src", pairs)
        image = total[:payload_rows].reshape(blocks_piece, vectors, tile_side)
        return image, total[payload_rows, :vectors]

    def lost_partial(blocks):
        return jnp.sum(blocks * piece_dangling[:, None, None], axis=(0, 2))

    def relaxation(blocks, lost_sum=None, gathered=None):
        if gathered is None:
            gathered, lost_dst = spread_columns(blocks, lost_partial(blocks))
        else:
            lost_dst = jnp.zeros((vectors,), jnp.float32)
        accumulated = tile_pass(
            "image", gathered, tiles, kernel_rows, kernel_cols, live_mask, block_count,
            row_blocks, vectors, lost_dst,
        )
        image, lost_total = reduce_rows(accumulated)
        if lost_sum is None:
            lost_sum = lost_total
        return (
            damping * (image + (lost_sum / page_total)[None, :, None] * tele)
            + (1.0 - damping) * tele
        )

    tele_sums = jnp.sum(tele, axis=2)

    relaxed_one = relaxation(tele)
    relaxed_two = relaxation(relaxed_one)

    gathered, _ = spread_columns(relaxed_two, jnp.zeros((vectors,), jnp.float32))
    entries = tile_pass(
        "entries", gathered, tiles, own_rows, kernel_cols, live_mask, block_count,
        row_blocks, vectors,
    ).sum(axis=2)
    block_sums = jnp.sum(relaxed_two, axis=2)
    row_agg = agg_of_block[row_global]
    col_agg = agg_of_block[col_global]
    fields = [
        entries.reshape(-1),
        row_agg.astype(jnp.float32),
        col_agg.astype(jnp.float32),
        block_sums.reshape(-1),
        tele_sums.reshape(-1),
        piece_agg.astype(jnp.float32),
        piece_dangling,
    ]
    sizes = [f.shape[0] for f in fields]
    shared = jnp.concatenate(fields)[None]
    if exchange and src_count % 2 == 0:
        shared = jnp.concatenate(
            [shared]
            + [
                lax.ppermute(shared, "dst", [(i, i ^ v) for i in range(dst_count)])
                for v in range(1, dst_count)
            ],
            axis=0,
        )
        shared = jnp.concatenate(
            [shared, lax.ppermute(shared, "src", [(i, i ^ 1) for i in range(src_count)])], axis=0
        )
        half = src_count // 2
        pieces = [shared]
        for shift in range(1, half):
            pairs = [(i, ((i // 2 + shift) % half) * 2 + i % 2) for i in range(src_count)]
            pieces.append(lax.ppermute(shared, "src", pairs))
        shared = jnp.concatenate(pieces, axis=0)
    else:
        shared = lax.all_gather(shared[0], all_axes, axis=0, tiled=False)
    offsets = [0]
    for size in sizes:
        offsets.append(offsets[-1] + size)
    every = [shared[:, offsets[i]:offsets[i + 1]] for i in range(len(sizes))]
    all_entries = every[0].reshape(-1, vectors)
    all_row_hot = every[1].reshape(-1)[:, None] == agg_range[None, :].astype(jnp.float32)
    all_col_hot = every[2].reshape(-1)[:, None] == agg_range[None, :].astype(jnp.float32)
    all_row_hot = all_row_hot.astype(jnp.bfloat16)
    all_col_hot = all_col_hot.astype(jnp.bfloat16)
    all_block_sums = every[3].reshape(-1, vectors)
    all_tele_sums = every[4].reshape(-1, vectors)
    all_block_hot = (every[5].reshape(-1)[:, None] == agg_range[None, :].astype(jnp.float32))
    all_block_hot = all_block_hot.astype(jnp.float32)
    all_dangling = every[6].reshape(-1)
    totals = jnp.einsum("bk,ba->ka", all_block_sums, all_block_hot, precision=highest)
    lost_mass = jnp.einsum(
        "bk,ba->ka", all_block_sums * all_dangling[:, None], all_block_hot, precision=highest
    )
    weight = jnp.einsum("bk,ba->ka", all_tele_sums, all_block_hot, precision=highest)
    inflow_one = select_dot("tk,ta->ka", all_entries, all_row_hot)

    def coarse_sweep(inflow, ratios):
        carried = jnp.sum(lost_mass * ratios, axis=1)
        return (
            damping * (inflow + (carried / page_total)[:, None] * weight)
            + (1.0 - damping) * weight
        )

    level_one = coarse_sweep(inflow_one, jnp.ones((vectors, agg_count), jnp.float32))
    ratios_one = level_one / totals
    ratio_at_tile = select_dot("ka,ta->tk", ratios_one, all_col_hot)
    inflow_two = select_dot("tk,ta->ka", all_entries * ratio_at_tile, all_row_hot)
    level_two = coarse_sweep(inflow_two, ratios_one)
    ratios_two = level_two / totals
    groups = gathered.shape[0]
    group_ids = jnp.arange(groups, dtype=jnp.int32)
    if exchange:
        group_ids = group_ids ^ dst_index
    block_ids = (
        group_ids[:, None] * row_blocks
        + src_index * blocks_piece
        + jnp.arange(blocks_piece, dtype=jnp.int32)[None, :]
    )
    block_scale = jnp.take(ratios_two, agg_of_block[block_ids.reshape(-1)], axis=1)
    block_scale = block_scale.T.reshape(groups, payload_rows, 1)
    corrected_cols = jnp.concatenate(
        [
            gathered[:, :payload_rows, :] * block_scale,
            jnp.zeros((groups, pad_rows, tile_side), jnp.float32),
        ],
        axis=1,
    )
    lost_two = jnp.sum(lost_mass * ratios_two, axis=1)

    position = lax.axis_index(all_axes)
    owned_count = agg_count // (src_count * dst_count)
    owned = lax.dynamic_slice_in_dim(owner_list, position * owned_count, owned_count)
    owned_hot = (owned[:, None] == agg_range[None, :]).astype(jnp.float32)
    coarse_out = jnp.einsum("ka,qa->kq", level_two, owned_hot, precision=highest)

    relaxed_three = relaxation(None, lost_two, corrected_cols)
    relaxed_four = relaxation(relaxed_three)
    fine_out = jnp.transpose(relaxed_four, (1, 0, 2)).reshape(teleport.shape)
    return fine_out, coarse_out


def solution(mesh):
    placed = (
        P(None, "dst", "src"),
        P("dst", "src", None, None, None),
        P("dst", "src", None),
        P("dst", "src", None),
        P("dst", "src"),
        P(),
        P(),
        P(),
    )
    return jax.shard_map(
        per_device,
        mesh=mesh,
        in_specs=placed,
        out_specs=(P(None, "dst", "src"), P(None, ("src", "dst"))),
        check_vma=False,
    )
```

```python
import functools

import jax
import jax.numpy as jnp
from jax import lax
from jax.experimental import pallas as pl
from jax.experimental.pallas import tpu as pltpu
from jax.sharding import PartitionSpec as P

damping = 0.85
group_size = 32
highest = lax.Precision.HIGHEST


def tile_kernel(
    mode, blocks_piece, vectors, rows_ref, cols_ref, live_ref, nb_ref, x_ref, t_ref, *refs
):
    step = pl.program_id(0)
    if mode == "image":
        lost_ref = refs[0]
        outs = refs[1:]
        body_rows = blocks_piece * vectors

        @pl.when(step == 0)
        def _():
            for out_ref in outs:
                count = out_ref.shape[0]
                out_ref[:, :body_rows, :] = jnp.zeros((count, body_rows, out_ref.shape[2]), jnp.float32)
                out_ref[:, body_rows:, :] = jnp.broadcast_to(
                    lost_ref[...][None], (count,) + lost_ref.shape
                )
    else:
        (o_ref,) = refs

    @pl.when(step < nb_ref[0])
    def _():
        for g in range(group_size):
            slot = step * group_size + g
            col = cols_ref[slot]
            start = pl.multiple_of((col % blocks_piece) * vectors, vectors)
            picked = x_ref[col // blocks_piece, pl.ds(start, vectors), :].astype(jnp.bfloat16)
            weight = jnp.where(live_ref[slot] != 0, 1.0, 0.0).astype(jnp.bfloat16)
            product = jnp.dot(picked * weight, t_ref[g], preferred_element_type=jnp.float32)
            if mode == "image":
                row = rows_ref[slot]
                at = pl.multiple_of((row % blocks_piece) * vectors, vectors)
                spot = row // blocks_piece
                part_size = outs[0].shape[0]
                for q, out_ref in enumerate(outs):
                    window = (spot % part_size, pl.ds(at, vectors), slice(None))
                    if len(outs) == 1:
                        out_ref[window] = out_ref[window] + product
                    else:
                        mask = jnp.where(spot // part_size == q, 1.0, 0.0)
                        out_ref[window] = out_ref[window] + product * mask
            else:
                o_ref[g] = product[:, :128] + product[:, 128:]

    if mode == "entries":

        @pl.when(step >= nb_ref[0])
        def _():
            o_ref[...] = jnp.zeros_like(o_ref)


def tile_pass(mode, x_cols, tiles, rows, cols, live, block_count, row_blocks, vectors, lost=None):
    groups, padded_rows, side = x_cols.shape
    blocks_piece = padded_rows // vectors
    owners = row_blocks // blocks_piece
    slots = tiles.shape[2]
    steps = slots // group_size

    def tile_index(i, rows_ref, cols_ref, live_ref, nb_ref):
        return (0, 0, jnp.minimum(i, nb_ref[0] - 1), 0, 0)

    if mode == "image":
        parts = 2 if owners % 2 == 0 else 1
        part_shape = (owners // parts, padded_rows, side)
        out_shape = [jax.ShapeDtypeStruct(part_shape, jnp.float32)] * parts
        out_spec = [pl.BlockSpec(part_shape, lambda i, *_: (0, 0, 0))] * parts
    else:
        out_shape = jax.ShapeDtypeStruct((slots, vectors, 128), jnp.float32)
        out_spec = pl.BlockSpec((group_size, vectors, 128), lambda i, *_: (i, 0, 0))
    in_specs = [
        pl.BlockSpec((groups, padded_rows, side), lambda i, *_: (0, 0, 0)),
        pl.BlockSpec((None, None, group_size, side, side), tile_index),
    ]
    operands = [x_cols, tiles]
    if mode == "image":
        pad = padded_rows - blocks_piece * vectors
        lost_block = jnp.zeros((pad, side), jnp.float32).at[0, :vectors].set(lost)
        in_specs.append(pl.BlockSpec((pad, side), lambda i, *_: (0, 0)))
        operands.append(lost_block)
    grid_spec = pltpu.PrefetchScalarGridSpec(
        num_scalar_prefetch=4,
        grid=(steps,),
        in_specs=in_specs,
        out_specs=out_spec,
    )
    return pl.pallas_call(
        functools.partial(tile_kernel, mode, blocks_piece, vectors),
        grid_spec=grid_spec,
        out_shape=out_shape,
        compiler_params=pltpu.CompilerParams(dimension_semantics=("arbitrary",)),
    )(rows, cols, live, block_count, *operands)


def split_three(value):
    high = lax.reduce_precision(value, exponent_bits=8, mantissa_bits=7)
    rest = value - high
    middle = lax.reduce_precision(rest, exponent_bits=8, mantissa_bits=7)
    low = lax.reduce_precision(rest - middle, exponent_bits=8, mantissa_bits=7)
    return jnp.stack([high, middle, low]).astype(jnp.bfloat16)


def select_dot(spec, value, one_hot):
    parts = jnp.einsum(
        "p" + spec.split(",")[0] + "," + spec.split(",")[1].split("->")[0] + "->p"
        + spec.split("->")[1],
        split_three(value),
        one_hot,
        preferred_element_type=jnp.float32,
    )
    return jnp.sum(parts, axis=0)


def per_device(
    teleport, tiles, tile_rows, tile_cols, tile_counts, dangling, agg_of_block, owner_list
):
    vectors = teleport.shape[0]
    piece_width = teleport.shape[2]
    slots_total = tiles.shape[2]
    tile_side = tiles.shape[4]
    blocks_piece = piece_width // tile_side
    src_count = lax.axis_size("src")
    dst_count = lax.axis_size("dst")
    row_blocks = blocks_piece * src_count
    col_blocks = blocks_piece * dst_count
    page_total = row_blocks * dst_count * tile_side
    agg_count = owner_list.shape[0]
    src_index = lax.axis_index("src")
    dst_index = lax.axis_index("dst")
    own_rows = jnp.clip(tile_rows[0, 0], 0, row_blocks - 1)
    own_cols = jnp.clip(tile_cols[0, 0], 0, col_blocks - 1)
    own_count = tile_counts[0, 0]
    col_global = (
        own_cols // blocks_piece * (blocks_piece * src_count)
        + src_index * blocks_piece
        + own_cols % blocks_piece
    )
    row_global = dst_index * row_blocks + own_rows
    slot_range = jnp.arange(slots_total, dtype=jnp.int32)
    live_mask = ((slot_range < own_count) & (dangling[col_global] == 0)).astype(jnp.int32)
    steps = slots_total // group_size
    block_count = jnp.clip((own_count + group_size - 1) // group_size, 1, steps).reshape(1)
    block_count = block_count.astype(jnp.int32)
    piece_first = dst_index * row_blocks + src_index * blocks_piece
    piece_dangling = lax.dynamic_slice_in_dim(dangling, piece_first, blocks_piece).astype(
        jnp.float32
    )
    piece_agg = lax.dynamic_slice_in_dim(agg_of_block, piece_first, blocks_piece)
    agg_range = jnp.arange(agg_count, dtype=jnp.int32)
    piece_hot = (piece_agg[:, None] == agg_range[None, :]).astype(jnp.float32)
    tele = jnp.transpose(teleport.reshape(vectors, blocks_piece, tile_side), (1, 0, 2))

    all_axes = ("src", "dst")
    all_count = src_count * dst_count

    def tree_sum(value, axis, size):
        if size & (size - 1):
            return lax.psum(value, axis)
        shift = 1
        while shift < size:
            value = value + lax.ppermute(value, axis, [(i, i ^ shift) for i in range(size)])
            shift *= 2
        return value

    exchange = dst_count & (dst_count - 1) == 0
    if exchange:
        kernel_cols = (
            (own_cols // blocks_piece) ^ dst_index
        ) * blocks_piece + own_cols % blocks_piece
    else:
        kernel_cols = own_cols

    payload_rows = blocks_piece * vectors
    pad_rows = 8

    def with_lost_row(body, lost):
        lead = body.shape[:-2]
        extra = jnp.zeros(lead + (pad_rows, tile_side), jnp.float32)
        extra = extra.at[..., 0, :vectors].set(jnp.broadcast_to(lost, lead + (vectors,)))
        return jnp.concatenate([body, extra], axis=-2)

    row_owner = own_rows // blocks_piece
    if src_count % 2 == 0:
        half = src_count // 2
        chip = src_index // 2
        position = ((row_owner % 2) ^ (src_index % 2)) * half + (row_owner // 2 - chip) % half
    else:
        position = (row_owner - src_index) % src_count
    kernel_rows = position * blocks_piece + own_rows % blocks_piece

    def spread_columns(blocks, lost):
        payload = with_lost_row(blocks.reshape(payload_rows, tile_side), lost)[None]
        if exchange:
            pieces = [payload] + [
                lax.ppermute(payload, "dst", [(i, i ^ v) for i in range(dst_count)])
                for v in range(1, dst_count)
            ]
            payload = jnp.concatenate(pieces, axis=0)
        else:
            payload = lax.all_gather(payload, "dst", axis=0, tiled=True)
        lost_dst = jnp.sum(payload[:, payload_rows, :vectors], axis=0)
        return payload, lost_dst

    def reduce_rows(outputs):
        n = src_count
        if n % 2 == 0:
            half = n // 2
            keep, give = outputs
            part = keep + lax.ppermute(give, "src", [(i, i ^ 1) for i in range(n)])
            total = part[0]
            for shift in range(1, half):
                pairs = [(i, ((i // 2 + shift) % half) * 2 + i % 2) for i in range(n)]
                total = total + lax.ppermute(part[shift], "src", pairs)
        else:
            (chunks,) = outputs
            total = chunks[0]
            for shift in range(1, n):
                pairs = [(i, (i + shift) % n) for i in range(n)]
                total = total + lax.ppermute(chunks[shift], "src", pairs)
        image = total[:payload_rows].reshape(blocks_piece, vectors, tile_side)
        return image, total[payload_rows, :vectors]

    def lost_partial(blocks):
        return jnp.sum(blocks * piece_dangling[:, None, None], axis=(0, 2))

    def relaxation(blocks, lost_sum=None, gathered=None):
        if gathered is None:
            gathered, lost_dst = spread_columns(blocks, lost_partial(blocks))
        else:
            lost_dst = jnp.zeros((vectors,), jnp.float32)
        accumulated = tile_pass(
            "image", gathered, tiles, kernel_rows, kernel_cols, live_mask, block_count,
            row_blocks, vectors, lost_dst,
        )
        image, lost_total = reduce_rows(accumulated)
        if lost_sum is None:
            lost_sum = lost_total
        return (
            damping * (image + (lost_sum / page_total)[None, :, None] * tele)
            + (1.0 - damping) * tele
        )

    tele_sums = jnp.sum(tele, axis=2)

    relaxed_one = relaxation(tele)
    relaxed_two = relaxation(relaxed_one)

    gathered, _ = spread_columns(relaxed_two, jnp.zeros((vectors,), jnp.float32))
    entries = tile_pass(
        "entries", gathered, tiles, own_rows, kernel_cols, live_mask, block_count,
        row_blocks, vectors,
    ).sum(axis=2)
    block_sums = jnp.sum(relaxed_two, axis=2)
    row_agg = agg_of_block[row_global]
    col_agg = agg_of_block[col_global]
    fields = [
        entries.reshape(-1),
        row_agg.astype(jnp.float32),
        col_agg.astype(jnp.float32),
        block_sums.reshape(-1),
        tele_sums.reshape(-1),
        piece_agg.astype(jnp.float32),
        piece_dangling,
    ]
    sizes = [f.shape[0] for f in fields]
    shared = jnp.concatenate(fields)[None]
    if exchange and src_count % 2 == 0:
        shared = jnp.concatenate(
            [shared]
            + [
                lax.ppermute(shared, "dst", [(i, i ^ v) for i in range(dst_count)])
                for v in range(1, dst_count)
            ],
            axis=0,
        )
        shared = jnp.concatenate(
            [shared, lax.ppermute(shared, "src", [(i, i ^ 1) for i in range(src_count)])], axis=0
        )
        half = src_count // 2
        pieces = [shared]
        for shift in range(1, half):
            pairs = [(i, ((i // 2 + shift) % half) * 2 + i % 2) for i in range(src_count)]
            pieces.append(lax.ppermute(shared, "src", pairs))
        shared = jnp.concatenate(pieces, axis=0)
    else:
        shared = lax.all_gather(shared[0], all_axes, axis=0, tiled=False)
    offsets = [0]
    for size in sizes:
        offsets.append(offsets[-1] + size)
    every = [shared[:, offsets[i]:offsets[i + 1]] for i in range(len(sizes))]
    all_entries = every[0].reshape(-1, vectors)
    all_row_hot = every[1].reshape(-1)[:, None] == agg_range[None, :].astype(jnp.float32)
    all_col_hot = every[2].reshape(-1)[:, None] == agg_range[None, :].astype(jnp.float32)
    all_row_hot = all_row_hot.astype(jnp.bfloat16)
    all_col_hot = all_col_hot.astype(jnp.bfloat16)
    all_block_sums = every[3].reshape(-1, vectors)
    all_tele_sums = every[4].reshape(-1, vectors)
    all_block_hot = (every[5].reshape(-1)[:, None] == agg_range[None, :].astype(jnp.float32))
    all_block_hot = all_block_hot.astype(jnp.float32)
    all_dangling = every[6].reshape(-1)
    totals = jnp.einsum("bk,ba->ka", all_block_sums, all_block_hot, precision=highest)
    lost_mass = jnp.einsum(
        "bk,ba->ka", all_block_sums * all_dangling[:, None], all_block_hot, precision=highest
    )
    weight = jnp.einsum("bk,ba->ka", all_tele_sums, all_block_hot, precision=highest)
    inflow_one = select_dot("tk,ta->ka", all_entries, all_row_hot)

    def coarse_sweep(inflow, ratios):
        carried = jnp.sum(lost_mass * ratios, axis=1)
        return (
            damping * (inflow + (carried / page_total)[:, None] * weight)
            + (1.0 - damping) * weight
        )

    level_one = coarse_sweep(inflow_one, jnp.ones((vectors, agg_count), jnp.float32))
    ratios_one = level_one / totals
    ratio_at_tile = select_dot("ka,ta->tk", ratios_one, all_col_hot)
    inflow_two = select_dot("tk,ta->ka", all_entries * ratio_at_tile, all_row_hot)
    level_two = coarse_sweep(inflow_two, ratios_one)
    ratios_two = level_two / totals
    groups = gathered.shape[0]
    group_ids = jnp.arange(groups, dtype=jnp.int32)
    if exchange:
        group_ids = group_ids ^ dst_index
    block_ids = (
        group_ids[:, None] * row_blocks
        + src_index * blocks_piece
        + jnp.arange(blocks_piece, dtype=jnp.int32)[None, :]
    )
    block_scale = jnp.take(ratios_two, agg_of_block[block_ids.reshape(-1)], axis=1)
    block_scale = block_scale.T.reshape(groups, payload_rows, 1)
    block_scale = jnp.concatenate(
        [block_scale, jnp.zeros((groups, pad_rows, 1), jnp.float32)], axis=1
    )
    corrected_cols = gathered * block_scale
    lost_two = jnp.sum(lost_mass * ratios_two, axis=1)

    position = lax.axis_index(all_axes)
    owned_count = agg_count // (src_count * dst_count)
    owned = lax.dynamic_slice_in_dim(owner_list, position * owned_count, owned_count)
    owned_hot = (owned[:, None] == agg_range[None, :]).astype(jnp.float32)
    coarse_out = jnp.einsum("ka,qa->kq", level_two, owned_hot, precision=highest)

    relaxed_three = relaxation(None, lost_two, corrected_cols)
    relaxed_four = relaxation(relaxed_three)
    fine_out = jnp.transpose(relaxed_four, (1, 0, 2)).reshape(teleport.shape)
    return fine_out, coarse_out


def solution(mesh):
    placed = (
        P(None, "dst", "src"),
        P("dst", "src", None, None, None),
        P("dst", "src", None),
        P("dst", "src", None),
        P("dst", "src"),
        P(),
        P(),
        P(),
    )
    return jax.shard_map(
        per_device,
        mesh=mesh,
        in_specs=placed,
        out_specs=(P(None, "dst", "src"), P(None, ("src", "dst"))),
        check_vma=False,
    )
```

```python
import functools

import jax
import jax.numpy as jnp
from jax import lax
from jax.experimental import pallas as pl
from jax.experimental.pallas import tpu as pltpu
from jax.sharding import PartitionSpec as P

damping = 0.85
group_size = 32
highest = lax.Precision.HIGHEST


def tile_kernel(
    mode, blocks_piece, vectors, rows_ref, cols_ref, live_ref, nb_ref, x_ref, t_ref, *refs
):
    step = pl.program_id(0)
    if mode == "image":
        lost_ref = refs[0]
        outs = refs[1:]
        body_rows = blocks_piece * vectors

        @pl.when(step == 0)
        def _():
            for out_ref in outs:
                count = out_ref.shape[0]
                out_ref[:, :body_rows, :] = jnp.zeros((count, body_rows, out_ref.shape[2]), jnp.float32)
                out_ref[:, body_rows:, :] = jnp.broadcast_to(
                    lost_ref[...][None], (count,) + lost_ref.shape
                )
    else:
        (o_ref,) = refs

        @pl.when(step == 0)
        def _():
            o_ref[...] = jnp.zeros_like(o_ref)

    @pl.when(step < nb_ref[0])
    def _():
        for g in range(group_size):
            slot = step * group_size + g
            col = cols_ref[slot]
            start = pl.multiple_of((col % blocks_piece) * vectors, vectors)
            picked = x_ref[col // blocks_piece, pl.ds(start, vectors), :].astype(jnp.bfloat16)
            weight = jnp.where(live_ref[slot] != 0, 1.0, 0.0).astype(jnp.bfloat16)
            product = jnp.dot(picked * weight, t_ref[g], preferred_element_type=jnp.float32)
            if mode == "image":
                row = rows_ref[slot]
                at = pl.multiple_of((row % blocks_piece) * vectors, vectors)
                spot = row // blocks_piece
                part_size = outs[0].shape[0]
                for q, out_ref in enumerate(outs):
                    window = (spot % part_size, pl.ds(at, vectors), slice(None))
                    if len(outs) == 1:
                        out_ref[window] = out_ref[window] + product
                    else:
                        mask = jnp.where(spot // part_size == q, 1.0, 0.0)
                        out_ref[window] = out_ref[window] + product * mask
            else:
                row_sum = jnp.sum(product, axis=1, keepdims=True)
                lane = lax.broadcasted_iota(jnp.int32, o_ref.shape, 1)
                o_ref[...] = o_ref[...] + jnp.where(lane == slot, row_sum, 0.0)


def tile_pass(mode, x_cols, tiles, rows, cols, live, block_count, row_blocks, vectors, lost=None):
    groups, padded_rows, side = x_cols.shape
    blocks_piece = padded_rows // vectors
    owners = row_blocks // blocks_piece
    slots = tiles.shape[2]
    steps = slots // group_size

    def tile_index(i, rows_ref, cols_ref, live_ref, nb_ref):
        return (0, 0, jnp.minimum(i, nb_ref[0] - 1), 0, 0)

    if mode == "image":
        parts = 2 if owners % 2 == 0 else 1
        part_shape = (owners // parts, padded_rows, side)
        out_shape = [jax.ShapeDtypeStruct(part_shape, jnp.float32)] * parts
        out_spec = [pl.BlockSpec(part_shape, lambda i, *_: (0, 0, 0))] * parts
    else:
        out_shape = jax.ShapeDtypeStruct((vectors, slots), jnp.float32)
        out_spec = pl.BlockSpec((vectors, slots), lambda i, *_: (0, 0))
    in_specs = [
        pl.BlockSpec((groups, padded_rows, side), lambda i, *_: (0, 0, 0)),
        pl.BlockSpec((None, None, group_size, side, side), tile_index),
    ]
    operands = [x_cols, tiles]
    if mode == "image":
        pad = padded_rows - blocks_piece * vectors
        lost_block = jnp.zeros((pad, side), jnp.float32).at[0, :vectors].set(lost)
        in_specs.append(pl.BlockSpec((pad, side), lambda i, *_: (0, 0)))
        operands.append(lost_block)
    grid_spec = pltpu.PrefetchScalarGridSpec(
        num_scalar_prefetch=4,
        grid=(steps,),
        in_specs=in_specs,
        out_specs=out_spec,
    )
    return pl.pallas_call(
        functools.partial(tile_kernel, mode, blocks_piece, vectors),
        grid_spec=grid_spec,
        out_shape=out_shape,
        compiler_params=pltpu.CompilerParams(dimension_semantics=("arbitrary",)),
    )(rows, cols, live, block_count, *operands)


def split_three(value):
    high = lax.reduce_precision(value, exponent_bits=8, mantissa_bits=7)
    rest = value - high
    middle = lax.reduce_precision(rest, exponent_bits=8, mantissa_bits=7)
    low = lax.reduce_precision(rest - middle, exponent_bits=8, mantissa_bits=7)
    return jnp.stack([high, middle, low]).astype(jnp.bfloat16)


def select_dot(spec, value, one_hot):
    parts = jnp.einsum(
        "p" + spec.split(",")[0] + "," + spec.split(",")[1].split("->")[0] + "->p"
        + spec.split("->")[1],
        split_three(value),
        one_hot,
        preferred_element_type=jnp.float32,
    )
    return jnp.sum(parts, axis=0)


def per_device(
    teleport, tiles, tile_rows, tile_cols, tile_counts, dangling, agg_of_block, owner_list
):
    vectors = teleport.shape[0]
    piece_width = teleport.shape[2]
    slots_total = tiles.shape[2]
    tile_side = tiles.shape[4]
    blocks_piece = piece_width // tile_side
    src_count = lax.axis_size("src")
    dst_count = lax.axis_size("dst")
    row_blocks = blocks_piece * src_count
    col_blocks = blocks_piece * dst_count
    page_total = row_blocks * dst_count * tile_side
    agg_count = owner_list.shape[0]
    src_index = lax.axis_index("src")
    dst_index = lax.axis_index("dst")
    own_rows = jnp.clip(tile_rows[0, 0], 0, row_blocks - 1)
    own_cols = jnp.clip(tile_cols[0, 0], 0, col_blocks - 1)
    own_count = tile_counts[0, 0]
    col_global = (
        own_cols // blocks_piece * (blocks_piece * src_count)
        + src_index * blocks_piece
        + own_cols % blocks_piece
    )
    row_global = dst_index * row_blocks + own_rows
    slot_range = jnp.arange(slots_total, dtype=jnp.int32)
    live_mask = ((slot_range < own_count) & (dangling[col_global] == 0)).astype(jnp.int32)
    steps = slots_total // group_size
    block_count = jnp.clip((own_count + group_size - 1) // group_size, 1, steps).reshape(1)
    block_count = block_count.astype(jnp.int32)
    piece_first = dst_index * row_blocks + src_index * blocks_piece
    piece_dangling = lax.dynamic_slice_in_dim(dangling, piece_first, blocks_piece).astype(
        jnp.float32
    )
    piece_agg = lax.dynamic_slice_in_dim(agg_of_block, piece_first, blocks_piece)
    agg_range = jnp.arange(agg_count, dtype=jnp.int32)
    piece_hot = (piece_agg[:, None] == agg_range[None, :]).astype(jnp.float32)
    tele = jnp.transpose(teleport.reshape(vectors, blocks_piece, tile_side), (1, 0, 2))

    all_axes = ("src", "dst")
    all_count = src_count * dst_count

    def tree_sum(value, axis, size):
        if size & (size - 1):
            return lax.psum(value, axis)
        shift = 1
        while shift < size:
            value = value + lax.ppermute(value, axis, [(i, i ^ shift) for i in range(size)])
            shift *= 2
        return value

    exchange = dst_count & (dst_count - 1) == 0
    if exchange:
        kernel_cols = (
            (own_cols // blocks_piece) ^ dst_index
        ) * blocks_piece + own_cols % blocks_piece
    else:
        kernel_cols = own_cols

    payload_rows = blocks_piece * vectors
    pad_rows = 8

    def with_lost_row(body, lost):
        lead = body.shape[:-2]
        extra = jnp.zeros(lead + (pad_rows, tile_side), jnp.float32)
        extra = extra.at[..., 0, :vectors].set(jnp.broadcast_to(lost, lead + (vectors,)))
        return jnp.concatenate([body, extra], axis=-2)

    row_owner = own_rows // blocks_piece
    if src_count % 2 == 0:
        half = src_count // 2
        chip = src_index // 2
        position = ((row_owner % 2) ^ (src_index % 2)) * half + (row_owner // 2 - chip) % half
    else:
        position = (row_owner - src_index) % src_count
    kernel_rows = position * blocks_piece + own_rows % blocks_piece

    def spread_columns(blocks, lost):
        payload = with_lost_row(blocks.reshape(payload_rows, tile_side), lost)[None]
        if exchange:
            pieces = [payload] + [
                lax.ppermute(payload, "dst", [(i, i ^ v) for i in range(dst_count)])
                for v in range(1, dst_count)
            ]
            payload = jnp.concatenate(pieces, axis=0)
        else:
            payload = lax.all_gather(payload, "dst", axis=0, tiled=True)
        lost_dst = jnp.sum(payload[:, payload_rows, :vectors], axis=0)
        return payload, lost_dst

    def reduce_rows(outputs):
        n = src_count
        if n % 2 == 0:
            half = n // 2
            keep, give = outputs
            part = keep + lax.ppermute(give, "src", [(i, i ^ 1) for i in range(n)])
            total = part[0]
            for shift in range(1, half):
                pairs = [(i, ((i // 2 + shift) % half) * 2 + i % 2) for i in range(n)]
                total = total + lax.ppermute(part[shift], "src", pairs)
        else:
            (chunks,) = outputs
            total = chunks[0]
            for shift in range(1, n):
                pairs = [(i, (i + shift) % n) for i in range(n)]
                total = total + lax.ppermute(chunks[shift], "src", pairs)
        image = total[:payload_rows].reshape(blocks_piece, vectors, tile_side)
        return image, total[payload_rows, :vectors]

    def lost_partial(blocks):
        return jnp.sum(blocks * piece_dangling[:, None, None], axis=(0, 2))

    def relaxation(blocks, lost_sum=None, gathered=None):
        if gathered is None:
            gathered, lost_dst = spread_columns(blocks, lost_partial(blocks))
        else:
            lost_dst = jnp.zeros((vectors,), jnp.float32)
        accumulated = tile_pass(
            "image", gathered, tiles, kernel_rows, kernel_cols, live_mask, block_count,
            row_blocks, vectors, lost_dst,
        )
        image, lost_total = reduce_rows(accumulated)
        if lost_sum is None:
            lost_sum = lost_total
        return (
            damping * (image + (lost_sum / page_total)[None, :, None] * tele)
            + (1.0 - damping) * tele
        )

    tele_sums = jnp.sum(tele, axis=2)

    relaxed_one = relaxation(tele)
    relaxed_two = relaxation(relaxed_one)

    gathered, _ = spread_columns(relaxed_two, jnp.zeros((vectors,), jnp.float32))
    entries = tile_pass(
        "entries", gathered, tiles, own_rows, kernel_cols, live_mask, block_count,
        row_blocks, vectors,
    ).T
    block_sums = jnp.sum(relaxed_two, axis=2)
    row_agg = agg_of_block[row_global]
    col_agg = agg_of_block[col_global]
    fields = [
        entries.reshape(-1),
        row_agg.astype(jnp.float32),
        col_agg.astype(jnp.float32),
        block_sums.reshape(-1),
        tele_sums.reshape(-1),
        piece_agg.astype(jnp.float32),
        piece_dangling,
    ]
    sizes = [f.shape[0] for f in fields]
    shared = jnp.concatenate(fields)[None]
    if exchange and src_count % 2 == 0:
        shared = jnp.concatenate(
            [shared]
            + [
                lax.ppermute(shared, "dst", [(i, i ^ v) for i in range(dst_count)])
                for v in range(1, dst_count)
            ],
            axis=0,
        )
        shared = jnp.concatenate(
            [shared, lax.ppermute(shared, "src", [(i, i ^ 1) for i in range(src_count)])], axis=0
        )
        half = src_count // 2
        pieces = [shared]
        for shift in range(1, half):
            pairs = [(i, ((i // 2 + shift) % half) * 2 + i % 2) for i in range(src_count)]
            pieces.append(lax.ppermute(shared, "src", pairs))
        shared = jnp.concatenate(pieces, axis=0)
    else:
        shared = lax.all_gather(shared[0], all_axes, axis=0, tiled=False)
    offsets = [0]
    for size in sizes:
        offsets.append(offsets[-1] + size)
    every = [shared[:, offsets[i]:offsets[i + 1]] for i in range(len(sizes))]
    all_entries = every[0].reshape(-1, vectors)
    all_row_hot = every[1].reshape(-1)[:, None] == agg_range[None, :].astype(jnp.float32)
    all_col_hot = every[2].reshape(-1)[:, None] == agg_range[None, :].astype(jnp.float32)
    all_row_hot = all_row_hot.astype(jnp.bfloat16)
    all_col_hot = all_col_hot.astype(jnp.bfloat16)
    all_block_sums = every[3].reshape(-1, vectors)
    all_tele_sums = every[4].reshape(-1, vectors)
    all_block_hot = (every[5].reshape(-1)[:, None] == agg_range[None, :].astype(jnp.float32))
    all_block_hot = all_block_hot.astype(jnp.float32)
    all_dangling = every[6].reshape(-1)
    totals = jnp.einsum("bk,ba->ka", all_block_sums, all_block_hot, precision=highest)
    lost_mass = jnp.einsum(
        "bk,ba->ka", all_block_sums * all_dangling[:, None], all_block_hot, precision=highest
    )
    weight = jnp.einsum("bk,ba->ka", all_tele_sums, all_block_hot, precision=highest)
    inflow_one = select_dot("tk,ta->ka", all_entries, all_row_hot)

    def coarse_sweep(inflow, ratios):
        carried = jnp.sum(lost_mass * ratios, axis=1)
        return (
            damping * (inflow + (carried / page_total)[:, None] * weight)
            + (1.0 - damping) * weight
        )

    level_one = coarse_sweep(inflow_one, jnp.ones((vectors, agg_count), jnp.float32))
    ratios_one = level_one / totals
    ratio_at_tile = select_dot("ka,ta->tk", ratios_one, all_col_hot)
    inflow_two = select_dot("tk,ta->ka", all_entries * ratio_at_tile, all_row_hot)
    level_two = coarse_sweep(inflow_two, ratios_one)
    ratios_two = level_two / totals
    groups = gathered.shape[0]
    group_ids = jnp.arange(groups, dtype=jnp.int32)
    if exchange:
        group_ids = group_ids ^ dst_index
    block_ids = (
        group_ids[:, None] * row_blocks
        + src_index * blocks_piece
        + jnp.arange(blocks_piece, dtype=jnp.int32)[None, :]
    )
    block_scale = jnp.take(ratios_two, agg_of_block[block_ids.reshape(-1)], axis=1)
    block_scale = block_scale.T.reshape(groups, payload_rows, 1)
    block_scale = jnp.concatenate(
        [block_scale, jnp.zeros((groups, pad_rows, 1), jnp.float32)], axis=1
    )
    corrected_cols = gathered * block_scale
    lost_two = jnp.sum(lost_mass * ratios_two, axis=1)

    position = lax.axis_index(all_axes)
    owned_count = agg_count // (src_count * dst_count)
    owned = lax.dynamic_slice_in_dim(owner_list, position * owned_count, owned_count)
    owned_hot = (owned[:, None] == agg_range[None, :]).astype(jnp.float32)
    coarse_out = jnp.einsum("ka,qa->kq", level_two, owned_hot, precision=highest)

    relaxed_three = relaxation(None, lost_two, corrected_cols)
    relaxed_four = relaxation(relaxed_three)
    fine_out = jnp.transpose(relaxed_four, (1, 0, 2)).reshape(teleport.shape)
    return fine_out, coarse_out


def solution(mesh):
    placed = (
        P(None, "dst", "src"),
        P("dst", "src", None, None, None),
        P("dst", "src", None),
        P("dst", "src", None),
        P("dst", "src"),
        P(),
        P(),
        P(),
    )
    return jax.shard_map(
        per_device,
        mesh=mesh,
        in_specs=placed,
        out_specs=(P(None, "dst", "src"), P(None, ("src", "dst"))),
        check_vma=False,
    )
```

```python
import functools

import jax
import jax.numpy as jnp
from jax import lax
from jax.experimental import pallas as pl
from jax.experimental.pallas import tpu as pltpu
from jax.sharding import PartitionSpec as P

damping = 0.85
group_size = 32
highest = lax.Precision.HIGHEST


def tile_kernel(
    mode, blocks_piece, vectors, rows_ref, cols_ref, live_ref, nb_ref, x_ref, t_ref, *refs
):
    step = pl.program_id(0)
    if mode == "image":
        lost_ref = refs[0]
        outs = refs[1:]
        body_rows = blocks_piece * vectors

        @pl.when(step == 0)
        def _():
            for out_ref in outs:
                count = out_ref.shape[0]
                out_ref[:, :body_rows, :] = jnp.zeros((count, body_rows, out_ref.shape[2]), jnp.float32)
                out_ref[:, body_rows:, :] = jnp.broadcast_to(
                    lost_ref[...][None], (count,) + lost_ref.shape
                )
    else:
        (o_ref,) = refs

        @pl.when(step == 0)
        def _():
            o_ref[...] = jnp.zeros_like(o_ref)

    @pl.when(step < nb_ref[0])
    def _():
        for g in range(group_size):
            slot = step * group_size + g
            col = cols_ref[slot]
            start = pl.multiple_of((col % blocks_piece) * vectors, vectors)
            picked = x_ref[col // blocks_piece, pl.ds(start, vectors), :].astype(jnp.bfloat16)
            weight = jnp.where(live_ref[slot] != 0, 1.0, 0.0).astype(jnp.bfloat16)
            product = jnp.dot(picked * weight, t_ref[g], preferred_element_type=jnp.float32)
            if mode == "image":
                row = rows_ref[slot]
                at = pl.multiple_of((row % blocks_piece) * vectors, vectors)
                spot = row // blocks_piece
                part_size = outs[0].shape[0]
                for q, out_ref in enumerate(outs):
                    window = (spot % part_size, pl.ds(at, vectors), slice(None))
                    if len(outs) == 1:
                        out_ref[window] = out_ref[window] + product
                    else:
                        mask = jnp.where(spot // part_size == q, 1.0, 0.0)
                        out_ref[window] = out_ref[window] + product * mask
            else:
                row_sum = jnp.sum(product, axis=1, keepdims=True)
                lane = lax.broadcasted_iota(jnp.int32, o_ref.shape, 1)
                o_ref[...] = o_ref[...] + jnp.where(lane == slot, row_sum, 0.0)


def tile_pass(mode, x_cols, tiles, rows, cols, live, block_count, row_blocks, vectors, lost=None):
    groups, padded_rows, side = x_cols.shape
    blocks_piece = padded_rows // vectors
    owners = row_blocks // blocks_piece
    slots = tiles.shape[2]
    steps = slots // group_size

    def tile_index(i, rows_ref, cols_ref, live_ref, nb_ref):
        return (0, 0, jnp.minimum(i, nb_ref[0] - 1), 0, 0)

    if mode == "image":
        parts = 2 if owners % 2 == 0 else 1
        part_shape = (owners // parts, padded_rows, side)
        out_shape = [jax.ShapeDtypeStruct(part_shape, jnp.float32)] * parts
        out_spec = [pl.BlockSpec(part_shape, lambda i, *_: (0, 0, 0))] * parts
    else:
        out_shape = jax.ShapeDtypeStruct((vectors, slots), jnp.float32)
        out_spec = pl.BlockSpec((vectors, slots), lambda i, *_: (0, 0))
    in_specs = [
        pl.BlockSpec((groups, padded_rows, side), lambda i, *_: (0, 0, 0)),
        pl.BlockSpec((None, None, group_size, side, side), tile_index),
    ]
    operands = [x_cols, tiles]
    if mode == "image":
        pad = padded_rows - blocks_piece * vectors
        lost_block = jnp.zeros((pad, side), jnp.float32).at[0, :vectors].set(lost)
        in_specs.append(pl.BlockSpec((pad, side), lambda i, *_: (0, 0)))
        operands.append(lost_block)
    grid_spec = pltpu.PrefetchScalarGridSpec(
        num_scalar_prefetch=4,
        grid=(steps,),
        in_specs=in_specs,
        out_specs=out_spec,
    )
    return pl.pallas_call(
        functools.partial(tile_kernel, mode, blocks_piece, vectors),
        grid_spec=grid_spec,
        out_shape=out_shape,
        compiler_params=pltpu.CompilerParams(dimension_semantics=("arbitrary",)),
    )(rows, cols, live, block_count, *operands)


def split_three(value):
    high = lax.reduce_precision(value, exponent_bits=8, mantissa_bits=7)
    rest = value - high
    middle = lax.reduce_precision(rest, exponent_bits=8, mantissa_bits=7)
    low = lax.reduce_precision(rest - middle, exponent_bits=8, mantissa_bits=7)
    return jnp.stack([high, middle, low]).astype(jnp.bfloat16)


def select_dot(spec, value, one_hot):
    parts = jnp.einsum(
        "p" + spec.split(",")[0] + "," + spec.split(",")[1].split("->")[0] + "->p"
        + spec.split("->")[1],
        split_three(value),
        one_hot,
        preferred_element_type=jnp.float32,
    )
    return jnp.sum(parts, axis=0)


def per_device(
    teleport, tiles, tile_rows, tile_cols, tile_counts, dangling, agg_of_block, owner_list
):
    vectors = teleport.shape[0]
    piece_width = teleport.shape[2]
    slots_total = tiles.shape[2]
    tile_side = tiles.shape[4]
    blocks_piece = piece_width // tile_side
    src_count = lax.axis_size("src")
    dst_count = lax.axis_size("dst")
    row_blocks = blocks_piece * src_count
    col_blocks = blocks_piece * dst_count
    page_total = row_blocks * dst_count * tile_side
    agg_count = owner_list.shape[0]
    src_index = lax.axis_index("src")
    dst_index = lax.axis_index("dst")
    own_rows = jnp.clip(tile_rows[0, 0], 0, row_blocks - 1)
    own_cols = jnp.clip(tile_cols[0, 0], 0, col_blocks - 1)
    own_count = tile_counts[0, 0]
    col_global = (
        own_cols // blocks_piece * (blocks_piece * src_count)
        + src_index * blocks_piece
        + own_cols % blocks_piece
    )
    row_global = dst_index * row_blocks + own_rows
    slot_range = jnp.arange(slots_total, dtype=jnp.int32)
    live_mask = ((slot_range < own_count) & (dangling[col_global] == 0)).astype(jnp.int32)
    steps = slots_total // group_size
    block_count = jnp.clip((own_count + group_size - 1) // group_size, 1, steps).reshape(1)
    block_count = block_count.astype(jnp.int32)
    piece_first = dst_index * row_blocks + src_index * blocks_piece
    piece_dangling = lax.dynamic_slice_in_dim(dangling, piece_first, blocks_piece).astype(
        jnp.float32
    )
    piece_agg = lax.dynamic_slice_in_dim(agg_of_block, piece_first, blocks_piece)
    agg_range = jnp.arange(agg_count, dtype=jnp.int32)
    piece_hot = (piece_agg[:, None] == agg_range[None, :]).astype(jnp.float32)
    tele = jnp.transpose(teleport.reshape(vectors, blocks_piece, tile_side), (1, 0, 2))

    all_axes = ("src", "dst")
    all_count = src_count * dst_count

    def tree_sum(value, axis, size):
        if size & (size - 1):
            return lax.psum(value, axis)
        shift = 1
        while shift < size:
            value = value + lax.ppermute(value, axis, [(i, i ^ shift) for i in range(size)])
            shift *= 2
        return value

    exchange = dst_count & (dst_count - 1) == 0
    if exchange:
        kernel_cols = (
            (own_cols // blocks_piece) ^ dst_index
        ) * blocks_piece + own_cols % blocks_piece
    else:
        kernel_cols = own_cols

    payload_rows = blocks_piece * vectors
    pad_rows = 8

    def with_lost_row(body, lost):
        lead = body.shape[:-2]
        extra = jnp.zeros(lead + (pad_rows, tile_side), jnp.float32)
        extra = extra.at[..., 0, :vectors].set(jnp.broadcast_to(lost, lead + (vectors,)))
        return jnp.concatenate([body, extra], axis=-2)

    row_owner = own_rows // blocks_piece
    if src_count % 2 == 0:
        half = src_count // 2
        chip = src_index // 2
        position = ((row_owner % 2) ^ (src_index % 2)) * half + (row_owner // 2 - chip) % half
    else:
        position = (row_owner - src_index) % src_count
    kernel_rows = position * blocks_piece + own_rows % blocks_piece

    def spread_columns(blocks, lost):
        payload = with_lost_row(blocks.reshape(payload_rows, tile_side), lost)[None]
        if exchange:
            pieces = [payload] + [
                lax.ppermute(payload, "dst", [(i, i ^ v) for i in range(dst_count)])
                for v in range(1, dst_count)
            ]
            payload = jnp.concatenate(pieces, axis=0)
        else:
            payload = lax.all_gather(payload, "dst", axis=0, tiled=True)
        lost_dst = jnp.sum(payload[:, payload_rows, :vectors], axis=0)
        return payload, lost_dst

    def reduce_rows(outputs):
        n = src_count
        if n % 2 == 0:
            half = n // 2
            keep, give = outputs
            part = keep + lax.ppermute(give, "src", [(i, i ^ 1) for i in range(n)])
            total = part[0]
            for shift in range(1, half):
                pairs = [(i, ((i // 2 + shift) % half) * 2 + i % 2) for i in range(n)]
                total = total + lax.ppermute(part[shift], "src", pairs)
        else:
            (chunks,) = outputs
            total = chunks[0]
            for shift in range(1, n):
                pairs = [(i, (i + shift) % n) for i in range(n)]
                total = total + lax.ppermute(chunks[shift], "src", pairs)
        image = total[:payload_rows].reshape(blocks_piece, vectors, tile_side)
        return image, total[payload_rows, :vectors]

    def lost_partial(blocks):
        return jnp.sum(blocks * piece_dangling[:, None, None], axis=(0, 2))

    def relaxation(blocks, lost_sum=None, gathered=None):
        if gathered is None:
            gathered, lost_dst = spread_columns(blocks, lost_partial(blocks))
        else:
            lost_dst = jnp.zeros((vectors,), jnp.float32)
        accumulated = tile_pass(
            "image", gathered, tiles, kernel_rows, kernel_cols, live_mask, block_count,
            row_blocks, vectors, lost_dst,
        )
        image, lost_total = reduce_rows(accumulated)
        if lost_sum is None:
            lost_sum = lost_total
        return (
            damping * (image + (lost_sum / page_total)[None, :, None] * tele)
            + (1.0 - damping) * tele
        )

    tele_sums = jnp.sum(tele, axis=2)

    relaxed_one = relaxation(tele)
    relaxed_two = relaxation(relaxed_one)

    gathered, _ = spread_columns(relaxed_two, jnp.zeros((vectors,), jnp.float32))
    entries = tile_pass(
        "entries", gathered, tiles, own_rows, kernel_cols, live_mask, block_count,
        row_blocks, vectors,
    )
    block_sums = jnp.sum(relaxed_two, axis=2)
    row_agg = agg_of_block[row_global]
    col_agg = agg_of_block[col_global]

    def as_rows(values):
        extra = -values.shape[0] % slots_total
        return jnp.pad(values, (0, extra)).reshape(-1, slots_total)

    small = [
        block_sums.reshape(-1),
        tele_sums.reshape(-1),
        piece_agg.astype(jnp.float32),
        piece_dangling,
    ]
    small_rows = [as_rows(f) for f in small]
    fields = [entries, row_agg.astype(jnp.float32)[None], col_agg.astype(jnp.float32)[None]]
    shared = jnp.concatenate(fields + small_rows, axis=0)[None]
    if exchange and src_count % 2 == 0:
        shared = jnp.concatenate(
            [shared]
            + [
                lax.ppermute(shared, "dst", [(i, i ^ v) for i in range(dst_count)])
                for v in range(1, dst_count)
            ],
            axis=0,
        )
        shared = jnp.concatenate(
            [shared, lax.ppermute(shared, "src", [(i, i ^ 1) for i in range(src_count)])], axis=0
        )
        half = src_count // 2
        pieces = [shared]
        for shift in range(1, half):
            pairs = [(i, ((i // 2 + shift) % half) * 2 + i % 2) for i in range(src_count)]
            pieces.append(lax.ppermute(shared, "src", pairs))
        shared = jnp.concatenate(pieces, axis=0)
    else:
        shared = lax.all_gather(shared[0], all_axes, axis=0, tiled=False)
    all_entries = shared[:, :vectors, :]
    agg_float = agg_range.astype(jnp.float32)
    all_row_hot = (shared[:, vectors, :, None] == agg_float).astype(jnp.bfloat16)
    all_col_hot = (shared[:, vectors + 1, :, None] == agg_float).astype(jnp.bfloat16)
    every = []
    at = vectors + 2
    for field, rows in zip(small, small_rows):
        count = rows.shape[0]
        every.append(shared[:, at:at + count, :].reshape(shared.shape[0], -1)[:, :field.shape[0]])
        at += count
    all_block_sums = every[0].reshape(-1, vectors)
    all_tele_sums = every[1].reshape(-1, vectors)
    all_block_hot = (every[2].reshape(-1)[:, None] == agg_float[None, :]).astype(jnp.float32)
    all_dangling = every[3].reshape(-1)
    totals = jnp.einsum("bk,ba->ka", all_block_sums, all_block_hot, precision=highest)
    lost_mass = jnp.einsum(
        "bk,ba->ka", all_block_sums * all_dangling[:, None], all_block_hot, precision=highest
    )
    weight = jnp.einsum("bk,ba->ka", all_tele_sums, all_block_hot, precision=highest)
    inflow_one = select_dot("dkt,dta->ka", all_entries, all_row_hot)

    def coarse_sweep(inflow, ratios):
        carried = jnp.sum(lost_mass * ratios, axis=1)
        return (
            damping * (inflow + (carried / page_total)[:, None] * weight)
            + (1.0 - damping) * weight
        )

    level_one = coarse_sweep(inflow_one, jnp.ones((vectors, agg_count), jnp.float32))
    ratios_one = level_one / totals
    ratio_at_tile = select_dot("ka,dta->dkt", ratios_one, all_col_hot)
    inflow_two = select_dot("dkt,dta->ka", all_entries * ratio_at_tile, all_row_hot)
    level_two = coarse_sweep(inflow_two, ratios_one)
    ratios_two = level_two / totals
    groups = gathered.shape[0]
    group_ids = jnp.arange(groups, dtype=jnp.int32)
    if exchange:
        group_ids = group_ids ^ dst_index
    block_ids = (
        group_ids[:, None] * row_blocks
        + src_index * blocks_piece
        + jnp.arange(blocks_piece, dtype=jnp.int32)[None, :]
    )
    block_scale = jnp.take(ratios_two, agg_of_block[block_ids.reshape(-1)], axis=1)
    block_scale = block_scale.T.reshape(groups, payload_rows, 1)
    block_scale = jnp.concatenate(
        [block_scale, jnp.zeros((groups, pad_rows, 1), jnp.float32)], axis=1
    )
    corrected_cols = gathered * block_scale
    lost_two = jnp.sum(lost_mass * ratios_two, axis=1)

    position = lax.axis_index(all_axes)
    owned_count = agg_count // (src_count * dst_count)
    owned = lax.dynamic_slice_in_dim(owner_list, position * owned_count, owned_count)
    owned_hot = (owned[:, None] == agg_range[None, :]).astype(jnp.float32)
    coarse_out = jnp.einsum("ka,qa->kq", level_two, owned_hot, precision=highest)

    relaxed_three = relaxation(None, lost_two, corrected_cols)
    relaxed_four = relaxation(relaxed_three)
    fine_out = jnp.transpose(relaxed_four, (1, 0, 2)).reshape(teleport.shape)
    return fine_out, coarse_out


def solution(mesh):
    placed = (
        P(None, "dst", "src"),
        P("dst", "src", None, None, None),
        P("dst", "src", None),
        P("dst", "src", None),
        P("dst", "src"),
        P(),
        P(),
        P(),
    )
    return jax.shard_map(
        per_device,
        mesh=mesh,
        in_specs=placed,
        out_specs=(P(None, "dst", "src"), P(None, ("src", "dst"))),
        check_vma=False,
    )
```

```python
import functools

import jax
import jax.numpy as jnp
from jax import lax
from jax.experimental import pallas as pl
from jax.experimental.pallas import tpu as pltpu
from jax.sharding import PartitionSpec as P

damping = 0.85
group_size = 32
highest = lax.Precision.HIGHEST


def tile_kernel(
    mode, blocks_piece, vectors, rows_ref, cols_ref, live_ref, nb_ref, x_ref, t_ref, *refs
):
    step = pl.program_id(0)
    if mode == "image":
        outs = refs
        body_rows = blocks_piece * vectors

        @pl.when(step == 0)
        def _():
            lost_rows = x_ref[0, body_rows:, :]
            for v in range(1, x_ref.shape[0]):
                lost_rows = lost_rows + x_ref[v, body_rows:, :]
            for out_ref in outs:
                count = out_ref.shape[0]
                out_ref[:, :body_rows, :] = jnp.zeros((count, body_rows, out_ref.shape[2]), jnp.float32)
                out_ref[:, body_rows:, :] = jnp.broadcast_to(
                    lost_rows[None], (count,) + lost_rows.shape
                )
    else:
        (o_ref,) = refs

        @pl.when(step == 0)
        def _():
            o_ref[...] = jnp.zeros_like(o_ref)

    @pl.when(step < nb_ref[0])
    def _():
        for g in range(group_size):
            slot = step * group_size + g
            col = cols_ref[slot]
            start = pl.multiple_of((col % blocks_piece) * vectors, vectors)
            picked = x_ref[col // blocks_piece, pl.ds(start, vectors), :].astype(jnp.bfloat16)
            weight = jnp.where(live_ref[slot] != 0, 1.0, 0.0).astype(jnp.bfloat16)
            product = jnp.dot(picked * weight, t_ref[g], preferred_element_type=jnp.float32)
            if mode == "image":
                row = rows_ref[slot]
                at = pl.multiple_of((row % blocks_piece) * vectors, vectors)
                spot = row // blocks_piece
                part_size = outs[0].shape[0]
                for q, out_ref in enumerate(outs):
                    window = (spot % part_size, pl.ds(at, vectors), slice(None))
                    if len(outs) == 1:
                        out_ref[window] = out_ref[window] + product
                    else:
                        mask = jnp.where(spot // part_size == q, 1.0, 0.0)
                        out_ref[window] = out_ref[window] + product * mask
            else:
                row_sum = jnp.sum(product, axis=1, keepdims=True)
                lane = lax.broadcasted_iota(jnp.int32, o_ref.shape, 1)
                o_ref[...] = o_ref[...] + jnp.where(lane == slot, row_sum, 0.0)


def tile_pass(mode, x_cols, tiles, rows, cols, live, block_count, row_blocks, vectors, lost=None):
    groups, padded_rows, side = x_cols.shape
    blocks_piece = padded_rows // vectors
    owners = row_blocks // blocks_piece
    slots = tiles.shape[2]
    steps = slots // group_size

    def tile_index(i, rows_ref, cols_ref, live_ref, nb_ref):
        return (0, 0, jnp.minimum(i, nb_ref[0] - 1), 0, 0)

    if mode == "image":
        parts = 2 if owners % 2 == 0 else 1
        part_shape = (owners // parts, padded_rows, side)
        out_shape = [jax.ShapeDtypeStruct(part_shape, jnp.float32)] * parts
        out_spec = [pl.BlockSpec(part_shape, lambda i, *_: (0, 0, 0))] * parts
    else:
        out_shape = jax.ShapeDtypeStruct((vectors, slots), jnp.float32)
        out_spec = pl.BlockSpec((vectors, slots), lambda i, *_: (0, 0))
    in_specs = [
        pl.BlockSpec((groups, padded_rows, side), lambda i, *_: (0, 0, 0)),
        pl.BlockSpec((None, None, group_size, side, side), tile_index),
    ]
    operands = [x_cols, tiles]
    grid_spec = pltpu.PrefetchScalarGridSpec(
        num_scalar_prefetch=4,
        grid=(steps,),
        in_specs=in_specs,
        out_specs=out_spec,
    )
    return pl.pallas_call(
        functools.partial(tile_kernel, mode, blocks_piece, vectors),
        grid_spec=grid_spec,
        out_shape=out_shape,
        compiler_params=pltpu.CompilerParams(dimension_semantics=("arbitrary",)),
    )(rows, cols, live, block_count, *operands)


def split_three(value):
    high = lax.reduce_precision(value, exponent_bits=8, mantissa_bits=7)
    rest = value - high
    middle = lax.reduce_precision(rest, exponent_bits=8, mantissa_bits=7)
    low = lax.reduce_precision(rest - middle, exponent_bits=8, mantissa_bits=7)
    return jnp.stack([high, middle, low]).astype(jnp.bfloat16)


def select_dot(spec, value, one_hot):
    parts = jnp.einsum(
        "p" + spec.split(",")[0] + "," + spec.split(",")[1].split("->")[0] + "->p"
        + spec.split("->")[1],
        split_three(value),
        one_hot,
        preferred_element_type=jnp.float32,
    )
    return jnp.sum(parts, axis=0)


def per_device(
    teleport, tiles, tile_rows, tile_cols, tile_counts, dangling, agg_of_block, owner_list
):
    vectors = teleport.shape[0]
    piece_width = teleport.shape[2]
    slots_total = tiles.shape[2]
    tile_side = tiles.shape[4]
    blocks_piece = piece_width // tile_side
    src_count = lax.axis_size("src")
    dst_count = lax.axis_size("dst")
    row_blocks = blocks_piece * src_count
    col_blocks = blocks_piece * dst_count
    page_total = row_blocks * dst_count * tile_side
    agg_count = owner_list.shape[0]
    src_index = lax.axis_index("src")
    dst_index = lax.axis_index("dst")
    own_rows = jnp.clip(tile_rows[0, 0], 0, row_blocks - 1)
    own_cols = jnp.clip(tile_cols[0, 0], 0, col_blocks - 1)
    own_count = tile_counts[0, 0]
    col_global = (
        own_cols // blocks_piece * (blocks_piece * src_count)
        + src_index * blocks_piece
        + own_cols % blocks_piece
    )
    row_global = dst_index * row_blocks + own_rows
    slot_range = jnp.arange(slots_total, dtype=jnp.int32)
    live_mask = ((slot_range < own_count) & (dangling[col_global] == 0)).astype(jnp.int32)
    steps = slots_total // group_size
    block_count = jnp.clip((own_count + group_size - 1) // group_size, 1, steps).reshape(1)
    block_count = block_count.astype(jnp.int32)
    piece_first = dst_index * row_blocks + src_index * blocks_piece
    piece_dangling = lax.dynamic_slice_in_dim(dangling, piece_first, blocks_piece).astype(
        jnp.float32
    )
    piece_agg = lax.dynamic_slice_in_dim(agg_of_block, piece_first, blocks_piece)
    agg_range = jnp.arange(agg_count, dtype=jnp.int32)
    piece_hot = (piece_agg[:, None] == agg_range[None, :]).astype(jnp.float32)
    tele = jnp.transpose(teleport.reshape(vectors, blocks_piece, tile_side), (1, 0, 2))

    all_axes = ("src", "dst")
    all_count = src_count * dst_count

    def tree_sum(value, axis, size):
        if size & (size - 1):
            return lax.psum(value, axis)
        shift = 1
        while shift < size:
            value = value + lax.ppermute(value, axis, [(i, i ^ shift) for i in range(size)])
            shift *= 2
        return value

    exchange = dst_count & (dst_count - 1) == 0
    if exchange:
        kernel_cols = (
            (own_cols // blocks_piece) ^ dst_index
        ) * blocks_piece + own_cols % blocks_piece
    else:
        kernel_cols = own_cols

    payload_rows = blocks_piece * vectors
    pad_rows = 8

    def with_lost_row(body, lost):
        lead = body.shape[:-2]
        extra = jnp.zeros(lead + (pad_rows, tile_side), jnp.float32)
        extra = extra.at[..., 0, :vectors].set(jnp.broadcast_to(lost, lead + (vectors,)))
        return jnp.concatenate([body, extra], axis=-2)

    row_owner = own_rows // blocks_piece
    if src_count % 2 == 0:
        half = src_count // 2
        chip = src_index // 2
        position = ((row_owner % 2) ^ (src_index % 2)) * half + (row_owner // 2 - chip) % half
    else:
        position = (row_owner - src_index) % src_count
    kernel_rows = position * blocks_piece + own_rows % blocks_piece

    def spread_columns(blocks, lost):
        payload = with_lost_row(blocks.reshape(payload_rows, tile_side), lost)[None]
        if exchange:
            pieces = [payload] + [
                lax.ppermute(payload, "dst", [(i, i ^ v) for i in range(dst_count)])
                for v in range(1, dst_count)
            ]
            payload = jnp.concatenate(pieces, axis=0)
        else:
            payload = lax.all_gather(payload, "dst", axis=0, tiled=True)
        lost_dst = jnp.sum(payload[:, payload_rows, :vectors], axis=0)
        return payload, lost_dst

    def reduce_rows(outputs):
        n = src_count
        if n % 2 == 0:
            half = n // 2
            keep, give = outputs
            part = keep + lax.ppermute(give, "src", [(i, i ^ 1) for i in range(n)])
            total = part[0]
            for shift in range(1, half):
                pairs = [(i, ((i // 2 + shift) % half) * 2 + i % 2) for i in range(n)]
                total = total + lax.ppermute(part[shift], "src", pairs)
        else:
            (chunks,) = outputs
            total = chunks[0]
            for shift in range(1, n):
                pairs = [(i, (i + shift) % n) for i in range(n)]
                total = total + lax.ppermute(chunks[shift], "src", pairs)
        image = total[:payload_rows].reshape(blocks_piece, vectors, tile_side)
        return image, total[payload_rows, :vectors]

    def lost_partial(blocks):
        return jnp.sum(blocks * piece_dangling[:, None, None], axis=(0, 2))

    def relaxation(blocks, lost_sum=None, gathered=None):
        if gathered is None:
            gathered, _ = spread_columns(blocks, lost_partial(blocks))
        accumulated = tile_pass(
            "image", gathered, tiles, kernel_rows, kernel_cols, live_mask, block_count,
            row_blocks, vectors,
        )
        image, lost_total = reduce_rows(accumulated)
        if lost_sum is None:
            lost_sum = lost_total
        return (
            damping * (image + (lost_sum / page_total)[None, :, None] * tele)
            + (1.0 - damping) * tele
        )

    tele_sums = jnp.sum(tele, axis=2)

    relaxed_one = relaxation(tele)
    relaxed_two = relaxation(relaxed_one)

    gathered, _ = spread_columns(relaxed_two, jnp.zeros((vectors,), jnp.float32))
    entries = tile_pass(
        "entries", gathered, tiles, own_rows, kernel_cols, live_mask, block_count,
        row_blocks, vectors,
    ).T
    block_sums = jnp.sum(relaxed_two, axis=2)
    row_agg = agg_of_block[row_global]
    col_agg = agg_of_block[col_global]
    fields = [
        entries.reshape(-1),
        row_agg.astype(jnp.float32),
        col_agg.astype(jnp.float32),
        block_sums.reshape(-1),
        tele_sums.reshape(-1),
        piece_agg.astype(jnp.float32),
        piece_dangling,
    ]
    sizes = [f.shape[0] for f in fields]
    shared = jnp.concatenate(fields)[None]
    if exchange and src_count % 2 == 0:
        shared = jnp.concatenate(
            [shared]
            + [
                lax.ppermute(shared, "dst", [(i, i ^ v) for i in range(dst_count)])
                for v in range(1, dst_count)
            ],
            axis=0,
        )
        shared = jnp.concatenate(
            [shared, lax.ppermute(shared, "src", [(i, i ^ 1) for i in range(src_count)])], axis=0
        )
        half = src_count // 2
        pieces = [shared]
        for shift in range(1, half):
            pairs = [(i, ((i // 2 + shift) % half) * 2 + i % 2) for i in range(src_count)]
            pieces.append(lax.ppermute(shared, "src", pairs))
        shared = jnp.concatenate(pieces, axis=0)
    else:
        shared = lax.all_gather(shared[0], all_axes, axis=0, tiled=False)
    offsets = [0]
    for size in sizes:
        offsets.append(offsets[-1] + size)
    every = [shared[:, offsets[i]:offsets[i + 1]] for i in range(len(sizes))]
    all_entries = every[0].reshape(-1, vectors)
    all_row_hot = every[1].reshape(-1)[:, None] == agg_range[None, :].astype(jnp.float32)
    all_col_hot = every[2].reshape(-1)[:, None] == agg_range[None, :].astype(jnp.float32)
    all_row_hot = all_row_hot.astype(jnp.bfloat16)
    all_col_hot = all_col_hot.astype(jnp.bfloat16)
    all_block_sums = every[3].reshape(-1, vectors)
    all_tele_sums = every[4].reshape(-1, vectors)
    all_block_hot = (every[5].reshape(-1)[:, None] == agg_range[None, :].astype(jnp.float32))
    all_block_hot = all_block_hot.astype(jnp.float32)
    all_dangling = every[6].reshape(-1)
    totals = jnp.einsum("bk,ba->ka", all_block_sums, all_block_hot, precision=highest)
    lost_mass = jnp.einsum(
        "bk,ba->ka", all_block_sums * all_dangling[:, None], all_block_hot, precision=highest
    )
    weight = jnp.einsum("bk,ba->ka", all_tele_sums, all_block_hot, precision=highest)
    inflow_one = select_dot("tk,ta->ka", all_entries, all_row_hot)

    def coarse_sweep(inflow, ratios):
        carried = jnp.sum(lost_mass * ratios, axis=1)
        return (
            damping * (inflow + (carried / page_total)[:, None] * weight)
            + (1.0 - damping) * weight
        )

    level_one = coarse_sweep(inflow_one, jnp.ones((vectors, agg_count), jnp.float32))
    ratios_one = level_one / totals
    ratio_at_tile = select_dot("ka,ta->tk", ratios_one, all_col_hot)
    inflow_two = select_dot("tk,ta->ka", all_entries * ratio_at_tile, all_row_hot)
    level_two = coarse_sweep(inflow_two, ratios_one)
    ratios_two = level_two / totals
    groups = gathered.shape[0]
    group_ids = jnp.arange(groups, dtype=jnp.int32)
    if exchange:
        group_ids = group_ids ^ dst_index
    block_ids = (
        group_ids[:, None] * row_blocks
        + src_index * blocks_piece
        + jnp.arange(blocks_piece, dtype=jnp.int32)[None, :]
    )
    block_scale = jnp.take(ratios_two, agg_of_block[block_ids.reshape(-1)], axis=1)
    block_scale = block_scale.T.reshape(groups, payload_rows, 1)
    block_scale = jnp.concatenate(
        [block_scale, jnp.zeros((groups, pad_rows, 1), jnp.float32)], axis=1
    )
    corrected_cols = gathered * block_scale
    lost_two = jnp.sum(lost_mass * ratios_two, axis=1)

    position = lax.axis_index(all_axes)
    owned_count = agg_count // (src_count * dst_count)
    owned = lax.dynamic_slice_in_dim(owner_list, position * owned_count, owned_count)
    owned_hot = (owned[:, None] == agg_range[None, :]).astype(jnp.float32)
    coarse_out = jnp.einsum("ka,qa->kq", level_two, owned_hot, precision=highest)

    relaxed_three = relaxation(None, lost_two, corrected_cols)
    relaxed_four = relaxation(relaxed_three)
    fine_out = jnp.transpose(relaxed_four, (1, 0, 2)).reshape(teleport.shape)
    return fine_out, coarse_out


def solution(mesh):
    placed = (
        P(None, "dst", "src"),
        P("dst", "src", None, None, None),
        P("dst", "src", None),
        P("dst", "src", None),
        P("dst", "src"),
        P(),
        P(),
        P(),
    )
    return jax.shard_map(
        per_device,
        mesh=mesh,
        in_specs=placed,
        out_specs=(P(None, "dst", "src"), P(None, ("src", "dst"))),
        check_vma=False,
    )
```

```python
import functools

import jax
import jax.numpy as jnp
from jax import lax
from jax.experimental import pallas as pl
from jax.experimental.pallas import tpu as pltpu
from jax.sharding import PartitionSpec as P

damping = 0.85
group_size = 64
highest = lax.Precision.HIGHEST


def tile_kernel(
    mode, blocks_piece, vectors, rows_ref, cols_ref, live_ref, nb_ref, x_ref, t_ref, *refs
):
    step = pl.program_id(0)
    if mode == "image":
        outs = refs
        body_rows = blocks_piece * vectors

        @pl.when(step == 0)
        def _():
            lost_rows = x_ref[0, body_rows:, :]
            for v in range(1, x_ref.shape[0]):
                lost_rows = lost_rows + x_ref[v, body_rows:, :]
            for out_ref in outs:
                count = out_ref.shape[0]
                out_ref[:, :body_rows, :] = jnp.zeros((count, body_rows, out_ref.shape[2]), jnp.float32)
                out_ref[:, body_rows:, :] = jnp.broadcast_to(
                    lost_rows[None], (count,) + lost_rows.shape
                )
    else:
        (o_ref,) = refs

        @pl.when(step == 0)
        def _():
            o_ref[...] = jnp.zeros_like(o_ref)

    @pl.when(step < nb_ref[0])
    def _():
        for g in range(group_size):
            slot = step * group_size + g
            col = cols_ref[slot]
            start = pl.multiple_of((col % blocks_piece) * vectors, vectors)
            picked = x_ref[col // blocks_piece, pl.ds(start, vectors), :].astype(jnp.bfloat16)
            weight = jnp.where(live_ref[slot] != 0, 1.0, 0.0).astype(jnp.bfloat16)
            product = jnp.dot(picked * weight, t_ref[g], preferred_element_type=jnp.float32)
            if mode == "image":
                row = rows_ref[slot]
                at = pl.multiple_of((row % blocks_piece) * vectors, vectors)
                spot = row // blocks_piece
                part_size = outs[0].shape[0]
                for q, out_ref in enumerate(outs):
                    window = (spot % part_size, pl.ds(at, vectors), slice(None))
                    if len(outs) == 1:
                        out_ref[window] = out_ref[window] + product
                    else:
                        mask = jnp.where(spot // part_size == q, 1.0, 0.0)
                        out_ref[window] = out_ref[window] + product * mask
            else:
                row_sum = jnp.sum(product, axis=1, keepdims=True)
                lane = lax.broadcasted_iota(jnp.int32, o_ref.shape, 1)
                o_ref[...] = o_ref[...] + jnp.where(lane == slot, row_sum, 0.0)


def tile_pass(mode, x_cols, tiles, rows, cols, live, block_count, row_blocks, vectors, lost=None):
    groups, padded_rows, side = x_cols.shape
    blocks_piece = padded_rows // vectors
    owners = row_blocks // blocks_piece
    slots = tiles.shape[2]
    steps = slots // group_size

    def tile_index(i, rows_ref, cols_ref, live_ref, nb_ref):
        return (0, 0, jnp.minimum(i, nb_ref[0] - 1), 0, 0)

    if mode == "image":
        parts = 2 if owners % 2 == 0 else 1
        part_shape = (owners // parts, padded_rows, side)
        out_shape = [jax.ShapeDtypeStruct(part_shape, jnp.float32)] * parts
        out_spec = [pl.BlockSpec(part_shape, lambda i, *_: (0, 0, 0))] * parts
    else:
        out_shape = jax.ShapeDtypeStruct((vectors, slots), jnp.float32)
        out_spec = pl.BlockSpec((vectors, slots), lambda i, *_: (0, 0))
    in_specs = [
        pl.BlockSpec((groups, padded_rows, side), lambda i, *_: (0, 0, 0)),
        pl.BlockSpec((None, None, group_size, side, side), tile_index),
    ]
    operands = [x_cols, tiles]
    grid_spec = pltpu.PrefetchScalarGridSpec(
        num_scalar_prefetch=4,
        grid=(steps,),
        in_specs=in_specs,
        out_specs=out_spec,
    )
    return pl.pallas_call(
        functools.partial(tile_kernel, mode, blocks_piece, vectors),
        grid_spec=grid_spec,
        out_shape=out_shape,
        compiler_params=pltpu.CompilerParams(dimension_semantics=("arbitrary",)),
    )(rows, cols, live, block_count, *operands)


def split_three(value):
    high = lax.reduce_precision(value, exponent_bits=8, mantissa_bits=7)
    rest = value - high
    middle = lax.reduce_precision(rest, exponent_bits=8, mantissa_bits=7)
    low = lax.reduce_precision(rest - middle, exponent_bits=8, mantissa_bits=7)
    return jnp.stack([high, middle, low]).astype(jnp.bfloat16)


def select_dot(spec, value, one_hot):
    parts = jnp.einsum(
        "p" + spec.split(",")[0] + "," + spec.split(",")[1].split("->")[0] + "->p"
        + spec.split("->")[1],
        split_three(value),
        one_hot,
        preferred_element_type=jnp.float32,
    )
    return jnp.sum(parts, axis=0)


def per_device(
    teleport, tiles, tile_rows, tile_cols, tile_counts, dangling, agg_of_block, owner_list
):
    vectors = teleport.shape[0]
    piece_width = teleport.shape[2]
    slots_total = tiles.shape[2]
    tile_side = tiles.shape[4]
    blocks_piece = piece_width // tile_side
    src_count = lax.axis_size("src")
    dst_count = lax.axis_size("dst")
    row_blocks = blocks_piece * src_count
    col_blocks = blocks_piece * dst_count
    page_total = row_blocks * dst_count * tile_side
    agg_count = owner_list.shape[0]
    src_index = lax.axis_index("src")
    dst_index = lax.axis_index("dst")
    own_rows = jnp.clip(tile_rows[0, 0], 0, row_blocks - 1)
    own_cols = jnp.clip(tile_cols[0, 0], 0, col_blocks - 1)
    own_count = tile_counts[0, 0]
    col_global = (
        own_cols // blocks_piece * (blocks_piece * src_count)
        + src_index * blocks_piece
        + own_cols % blocks_piece
    )
    row_global = dst_index * row_blocks + own_rows
    slot_range = jnp.arange(slots_total, dtype=jnp.int32)
    live_mask = ((slot_range < own_count) & (dangling[col_global] == 0)).astype(jnp.int32)
    steps = slots_total // group_size
    block_count = jnp.clip((own_count + group_size - 1) // group_size, 1, steps).reshape(1)
    block_count = block_count.astype(jnp.int32)
    piece_first = dst_index * row_blocks + src_index * blocks_piece
    piece_dangling = lax.dynamic_slice_in_dim(dangling, piece_first, blocks_piece).astype(
        jnp.float32
    )
    piece_agg = lax.dynamic_slice_in_dim(agg_of_block, piece_first, blocks_piece)
    agg_range = jnp.arange(agg_count, dtype=jnp.int32)
    piece_hot = (piece_agg[:, None] == agg_range[None, :]).astype(jnp.float32)
    tele = jnp.transpose(teleport.reshape(vectors, blocks_piece, tile_side), (1, 0, 2))

    all_axes = ("src", "dst")
    all_count = src_count * dst_count

    def tree_sum(value, axis, size):
        if size & (size - 1):
            return lax.psum(value, axis)
        shift = 1
        while shift < size:
            value = value + lax.ppermute(value, axis, [(i, i ^ shift) for i in range(size)])
            shift *= 2
        return value

    exchange = dst_count & (dst_count - 1) == 0
    if exchange:
        kernel_cols = (
            (own_cols // blocks_piece) ^ dst_index
        ) * blocks_piece + own_cols % blocks_piece
    else:
        kernel_cols = own_cols

    payload_rows = blocks_piece * vectors
    pad_rows = 8

    def with_lost_row(body, lost):
        lead = body.shape[:-2]
        extra = jnp.zeros(lead + (pad_rows, tile_side), jnp.float32)
        extra = extra.at[..., 0, :vectors].set(jnp.broadcast_to(lost, lead + (vectors,)))
        return jnp.concatenate([body, extra], axis=-2)

    row_owner = own_rows // blocks_piece
    if src_count % 2 == 0:
        half = src_count // 2
        chip = src_index // 2
        position = ((row_owner % 2) ^ (src_index % 2)) * half + (row_owner // 2 - chip) % half
    else:
        position = (row_owner - src_index) % src_count
    kernel_rows = position * blocks_piece + own_rows % blocks_piece

    def spread_columns(blocks, lost):
        payload = with_lost_row(blocks.reshape(payload_rows, tile_side), lost)[None]
        if exchange:
            pieces = [payload] + [
                lax.ppermute(payload, "dst", [(i, i ^ v) for i in range(dst_count)])
                for v in range(1, dst_count)
            ]
            payload = jnp.concatenate(pieces, axis=0)
        else:
            payload = lax.all_gather(payload, "dst", axis=0, tiled=True)
        lost_dst = jnp.sum(payload[:, payload_rows, :vectors], axis=0)
        return payload, lost_dst

    def reduce_rows(outputs):
        n = src_count
        if n % 2 == 0:
            half = n // 2
            keep, give = outputs
            part = keep + lax.ppermute(give, "src", [(i, i ^ 1) for i in range(n)])
            total = part[0]
            for shift in range(1, half):
                pairs = [(i, ((i // 2 + shift) % half) * 2 + i % 2) for i in range(n)]
                total = total + lax.ppermute(part[shift], "src", pairs)
        else:
            (chunks,) = outputs
            total = chunks[0]
            for shift in range(1, n):
                pairs = [(i, (i + shift) % n) for i in range(n)]
                total = total + lax.ppermute(chunks[shift], "src", pairs)
        image = total[:payload_rows].reshape(blocks_piece, vectors, tile_side)
        return image, total[payload_rows, :vectors]

    def lost_partial(blocks):
        return jnp.sum(blocks * piece_dangling[:, None, None], axis=(0, 2))

    def relaxation(blocks, lost_sum=None, gathered=None):
        if gathered is None:
            gathered, _ = spread_columns(blocks, lost_partial(blocks))
        accumulated = tile_pass(
            "image", gathered, tiles, kernel_rows, kernel_cols, live_mask, block_count,
            row_blocks, vectors,
        )
        image, lost_total = reduce_rows(accumulated)
        if lost_sum is None:
            lost_sum = lost_total
        return (
            damping * (image + (lost_sum / page_total)[None, :, None] * tele)
            + (1.0 - damping) * tele
        )

    tele_sums = jnp.sum(tele, axis=2)

    relaxed_one = relaxation(tele)
    relaxed_two = relaxation(relaxed_one)

    gathered, _ = spread_columns(relaxed_two, jnp.zeros((vectors,), jnp.float32))
    entries = tile_pass(
        "entries", gathered, tiles, own_rows, kernel_cols, live_mask, block_count,
        row_blocks, vectors,
    ).T
    block_sums = jnp.sum(relaxed_two, axis=2)
    row_agg = agg_of_block[row_global]
    col_agg = agg_of_block[col_global]
    fields = [
        entries.reshape(-1),
        row_agg.astype(jnp.float32),
        col_agg.astype(jnp.float32),
        block_sums.reshape(-1),
        tele_sums.reshape(-1),
        piece_agg.astype(jnp.float32),
        piece_dangling,
    ]
    sizes = [f.shape[0] for f in fields]
    shared = jnp.concatenate(fields)[None]
    if exchange and src_count % 2 == 0:
        shared = jnp.concatenate(
            [shared]
            + [
                lax.ppermute(shared, "dst", [(i, i ^ v) for i in range(dst_count)])
                for v in range(1, dst_count)
            ],
            axis=0,
        )
        shared = jnp.concatenate(
            [shared, lax.ppermute(shared, "src", [(i, i ^ 1) for i in range(src_count)])], axis=0
        )
        half = src_count // 2
        pieces = [shared]
        for shift in range(1, half):
            pairs = [(i, ((i // 2 + shift) % half) * 2 + i % 2) for i in range(src_count)]
            pieces.append(lax.ppermute(shared, "src", pairs))
        shared = jnp.concatenate(pieces, axis=0)
    else:
        shared = lax.all_gather(shared[0], all_axes, axis=0, tiled=False)
    offsets = [0]
    for size in sizes:
        offsets.append(offsets[-1] + size)
    every = [shared[:, offsets[i]:offsets[i + 1]] for i in range(len(sizes))]
    all_entries = every[0].reshape(-1, vectors)
    all_row_hot = every[1].reshape(-1)[:, None] == agg_range[None, :].astype(jnp.float32)
    all_col_hot = every[2].reshape(-1)[:, None] == agg_range[None, :].astype(jnp.float32)
    all_row_hot = all_row_hot.astype(jnp.bfloat16)
    all_col_hot = all_col_hot.astype(jnp.bfloat16)
    all_block_sums = every[3].reshape(-1, vectors)
    all_tele_sums = every[4].reshape(-1, vectors)
    all_block_hot = (every[5].reshape(-1)[:, None] == agg_range[None, :].astype(jnp.float32))
    all_block_hot = all_block_hot.astype(jnp.float32)
    all_dangling = every[6].reshape(-1)
    totals = jnp.einsum("bk,ba->ka", all_block_sums, all_block_hot, precision=highest)
    lost_mass = jnp.einsum(
        "bk,ba->ka", all_block_sums * all_dangling[:, None], all_block_hot, precision=highest
    )
    weight = jnp.einsum("bk,ba->ka", all_tele_sums, all_block_hot, precision=highest)
    inflow_one = select_dot("tk,ta->ka", all_entries, all_row_hot)

    def coarse_sweep(inflow, ratios):
        carried = jnp.sum(lost_mass * ratios, axis=1)
        return (
            damping * (inflow + (carried / page_total)[:, None] * weight)
            + (1.0 - damping) * weight
        )

    level_one = coarse_sweep(inflow_one, jnp.ones((vectors, agg_count), jnp.float32))
    ratios_one = level_one / totals
    ratio_at_tile = select_dot("ka,ta->tk", ratios_one, all_col_hot)
    inflow_two = select_dot("tk,ta->ka", all_entries * ratio_at_tile, all_row_hot)
    level_two = coarse_sweep(inflow_two, ratios_one)
    ratios_two = level_two / totals
    groups = gathered.shape[0]
    group_ids = jnp.arange(groups, dtype=jnp.int32)
    if exchange:
        group_ids = group_ids ^ dst_index
    block_ids = (
        group_ids[:, None] * row_blocks
        + src_index * blocks_piece
        + jnp.arange(blocks_piece, dtype=jnp.int32)[None, :]
    )
    block_scale = jnp.take(ratios_two, agg_of_block[block_ids.reshape(-1)], axis=1)
    block_scale = block_scale.T.reshape(groups, payload_rows, 1)
    block_scale = jnp.concatenate(
        [block_scale, jnp.zeros((groups, pad_rows, 1), jnp.float32)], axis=1
    )
    corrected_cols = gathered * block_scale
    lost_two = jnp.sum(lost_mass * ratios_two, axis=1)

    position = lax.axis_index(all_axes)
    owned_count = agg_count // (src_count * dst_count)
    owned = lax.dynamic_slice_in_dim(owner_list, position * owned_count, owned_count)
    owned_hot = (owned[:, None] == agg_range[None, :]).astype(jnp.float32)
    coarse_out = jnp.einsum("ka,qa->kq", level_two, owned_hot, precision=highest)

    relaxed_three = relaxation(None, lost_two, corrected_cols)
    relaxed_four = relaxation(relaxed_three)
    fine_out = jnp.transpose(relaxed_four, (1, 0, 2)).reshape(teleport.shape)
    return fine_out, coarse_out


def solution(mesh):
    placed = (
        P(None, "dst", "src"),
        P("dst", "src", None, None, None),
        P("dst", "src", None),
        P("dst", "src", None),
        P("dst", "src"),
        P(),
        P(),
        P(),
    )
    return jax.shard_map(
        per_device,
        mesh=mesh,
        in_specs=placed,
        out_specs=(P(None, "dst", "src"), P(None, ("src", "dst"))),
        check_vma=False,
    )
```

```python
import functools

import jax
import jax.numpy as jnp
from jax import lax
from jax.experimental import pallas as pl
from jax.experimental.pallas import tpu as pltpu
from jax.sharding import PartitionSpec as P

damping = 0.85
group_size = 32
highest = lax.Precision.HIGHEST


def tile_kernel(
    mode, blocks_piece, vectors, rows_ref, cols_ref, live_ref, nb_ref, x_ref, t_ref, *refs
):
    step = pl.program_id(0)
    if mode == "image":
        outs = refs
        body_rows = blocks_piece * vectors

        @pl.when(step == 0)
        def _():
            lost_rows = x_ref[0, body_rows:, :]
            for v in range(1, x_ref.shape[0]):
                lost_rows = lost_rows + x_ref[v, body_rows:, :]
            for out_ref in outs:
                count = out_ref.shape[0]
                out_ref[:, :body_rows, :] = jnp.zeros((count, body_rows, out_ref.shape[2]), jnp.float32)
                out_ref[:, body_rows:, :] = jnp.broadcast_to(
                    lost_rows[None], (count,) + lost_rows.shape
                )
    else:
        (o_ref,) = refs

        @pl.when(step == 0)
        def _():
            o_ref[...] = jnp.zeros_like(o_ref)

    @pl.when(step < nb_ref[0])
    def _():
        for g in range(group_size):
            slot = step * group_size + g
            col = cols_ref[slot]
            start = pl.multiple_of((col % blocks_piece) * vectors, vectors)
            picked = x_ref[col // blocks_piece, pl.ds(start, vectors), :].astype(jnp.bfloat16)
            weight = jnp.where(live_ref[slot] != 0, 1.0, 0.0).astype(jnp.bfloat16)
            product = jnp.dot(picked * weight, t_ref[g], preferred_element_type=jnp.float32)
            if mode == "image":
                row = rows_ref[slot]
                at = pl.multiple_of((row % blocks_piece) * vectors, vectors)
                spot = row // blocks_piece
                part_size = outs[0].shape[0]
                for q, out_ref in enumerate(outs):
                    window = (spot % part_size, pl.ds(at, vectors), slice(None))
                    if len(outs) == 1:
                        out_ref[window] = out_ref[window] + product
                    else:
                        mask = jnp.where(spot // part_size == q, 1.0, 0.0)
                        out_ref[window] = out_ref[window] + product * mask
            else:
                row_sum = jnp.sum(product, axis=1, keepdims=True)
                lane = lax.broadcasted_iota(jnp.int32, o_ref.shape, 1)
                o_ref[...] = o_ref[...] + jnp.where(lane == slot, row_sum, 0.0)


def tile_pass(mode, x_cols, tiles, rows, cols, live, block_count, row_blocks, vectors, lost=None):
    groups, padded_rows, side = x_cols.shape
    blocks_piece = padded_rows // vectors
    owners = row_blocks // blocks_piece
    slots = tiles.shape[2]
    steps = slots // group_size

    def tile_index(i, rows_ref, cols_ref, live_ref, nb_ref):
        return (0, 0, jnp.minimum(i, nb_ref[0] - 1), 0, 0)

    if mode == "image":
        parts = 2 if owners % 2 == 0 else 1
        part_shape = (owners // parts, padded_rows, side)
        out_shape = [jax.ShapeDtypeStruct(part_shape, jnp.float32)] * parts
        out_spec = [pl.BlockSpec(part_shape, lambda i, *_: (0, 0, 0))] * parts
    else:
        out_shape = jax.ShapeDtypeStruct((vectors, slots), jnp.float32)
        out_spec = pl.BlockSpec((vectors, slots), lambda i, *_: (0, 0))
    in_specs = [
        pl.BlockSpec((groups, padded_rows, side), lambda i, *_: (0, 0, 0)),
        pl.BlockSpec((None, None, group_size, side, side), tile_index),
    ]
    operands = [x_cols, tiles]
    grid_spec = pltpu.PrefetchScalarGridSpec(
        num_scalar_prefetch=4,
        grid=(steps,),
        in_specs=in_specs,
        out_specs=out_spec,
    )
    return pl.pallas_call(
        functools.partial(tile_kernel, mode, blocks_piece, vectors),
        grid_spec=grid_spec,
        out_shape=out_shape,
        compiler_params=pltpu.CompilerParams(dimension_semantics=("arbitrary",)),
    )(rows, cols, live, block_count, *operands)


def split_three(value):
    high = lax.reduce_precision(value, exponent_bits=8, mantissa_bits=7)
    rest = value - high
    middle = lax.reduce_precision(rest, exponent_bits=8, mantissa_bits=7)
    low = lax.reduce_precision(rest - middle, exponent_bits=8, mantissa_bits=7)
    return jnp.stack([high, middle, low]).astype(jnp.bfloat16)


def select_dot(spec, value, one_hot):
    parts = jnp.einsum(
        "p" + spec.split(",")[0] + "," + spec.split(",")[1].split("->")[0] + "->p"
        + spec.split("->")[1],
        split_three(value),
        one_hot,
        preferred_element_type=jnp.float32,
    )
    return jnp.sum(parts, axis=0)


def per_device(
    teleport, tiles, tile_rows, tile_cols, tile_counts, dangling, agg_of_block, owner_list
):
    vectors = teleport.shape[0]
    piece_width = teleport.shape[2]
    slots_total = tiles.shape[2]
    tile_side = tiles.shape[4]
    blocks_piece = piece_width // tile_side
    src_count = lax.axis_size("src")
    dst_count = lax.axis_size("dst")
    row_blocks = blocks_piece * src_count
    col_blocks = blocks_piece * dst_count
    page_total = row_blocks * dst_count * tile_side
    agg_count = owner_list.shape[0]
    src_index = lax.axis_index("src")
    dst_index = lax.axis_index("dst")
    own_rows = jnp.clip(tile_rows[0, 0], 0, row_blocks - 1)
    own_cols = jnp.clip(tile_cols[0, 0], 0, col_blocks - 1)
    own_count = tile_counts[0, 0]
    col_global = (
        own_cols // blocks_piece * (blocks_piece * src_count)
        + src_index * blocks_piece
        + own_cols % blocks_piece
    )
    row_global = dst_index * row_blocks + own_rows
    slot_range = jnp.arange(slots_total, dtype=jnp.int32)
    live_mask = ((slot_range < own_count) & (dangling[col_global] == 0)).astype(jnp.int32)
    steps = slots_total // group_size
    block_count = jnp.clip((own_count + group_size - 1) // group_size, 1, steps).reshape(1)
    block_count = block_count.astype(jnp.int32)
    piece_first = dst_index * row_blocks + src_index * blocks_piece
    piece_dangling = lax.dynamic_slice_in_dim(dangling, piece_first, blocks_piece).astype(
        jnp.float32
    )
    piece_agg = lax.dynamic_slice_in_dim(agg_of_block, piece_first, blocks_piece)
    agg_range = jnp.arange(agg_count, dtype=jnp.int32)
    piece_hot = (piece_agg[:, None] == agg_range[None, :]).astype(jnp.float32)
    tele = jnp.transpose(teleport.reshape(vectors, blocks_piece, tile_side), (1, 0, 2))

    all_axes = ("src", "dst")
    all_count = src_count * dst_count

    def tree_sum(value, axis, size):
        if size & (size - 1):
            return lax.psum(value, axis)
        shift = 1
        while shift < size:
            value = value + lax.ppermute(value, axis, [(i, i ^ shift) for i in range(size)])
            shift *= 2
        return value

    exchange = dst_count & (dst_count - 1) == 0
    if exchange:
        kernel_cols = (
            (own_cols // blocks_piece) ^ dst_index
        ) * blocks_piece + own_cols % blocks_piece
    else:
        kernel_cols = own_cols

    payload_rows = blocks_piece * vectors
    pad_rows = 8

    def with_lost_row(body, lost):
        lead = body.shape[:-2]
        shape = lead + (pad_rows, tile_side)
        row = lax.broadcasted_iota(jnp.int32, shape, len(shape) - 2)
        lane = lax.broadcasted_iota(jnp.int32, shape, len(shape) - 1)
        spread = jnp.pad(lost, (0, tile_side - vectors))
        extra = jnp.where((row == 0) & (lane < vectors), jnp.broadcast_to(spread, shape), 0.0)
        return jnp.concatenate([body, extra], axis=-2)

    row_owner = own_rows // blocks_piece
    if src_count % 2 == 0:
        half = src_count // 2
        chip = src_index // 2
        position = ((row_owner % 2) ^ (src_index % 2)) * half + (row_owner // 2 - chip) % half
    else:
        position = (row_owner - src_index) % src_count
    kernel_rows = position * blocks_piece + own_rows % blocks_piece

    def spread_columns(blocks, lost):
        payload = with_lost_row(blocks.reshape(payload_rows, tile_side), lost)[None]
        if exchange:
            pieces = [payload] + [
                lax.ppermute(payload, "dst", [(i, i ^ v) for i in range(dst_count)])
                for v in range(1, dst_count)
            ]
            payload = jnp.concatenate(pieces, axis=0)
        else:
            payload = lax.all_gather(payload, "dst", axis=0, tiled=True)
        lost_dst = jnp.sum(payload[:, payload_rows, :vectors], axis=0)
        return payload, lost_dst

    def reduce_rows(outputs):
        n = src_count
        if n % 2 == 0:
            half = n // 2
            keep, give = outputs
            part = keep + lax.ppermute(give, "src", [(i, i ^ 1) for i in range(n)])
            total = part[0]
            for shift in range(1, half):
                pairs = [(i, ((i // 2 + shift) % half) * 2 + i % 2) for i in range(n)]
                total = total + lax.ppermute(part[shift], "src", pairs)
        else:
            (chunks,) = outputs
            total = chunks[0]
            for shift in range(1, n):
                pairs = [(i, (i + shift) % n) for i in range(n)]
                total = total + lax.ppermute(chunks[shift], "src", pairs)
        image = total[:payload_rows].reshape(blocks_piece, vectors, tile_side)
        return image, total[payload_rows, :vectors]

    def lost_partial(blocks):
        return jnp.sum(blocks * piece_dangling[:, None, None], axis=(0, 2))

    def relaxation(blocks, lost_sum=None, gathered=None):
        if gathered is None:
            gathered, _ = spread_columns(blocks, lost_partial(blocks))
        accumulated = tile_pass(
            "image", gathered, tiles, kernel_rows, kernel_cols, live_mask, block_count,
            row_blocks, vectors,
        )
        image, lost_total = reduce_rows(accumulated)
        if lost_sum is None:
            lost_sum = lost_total
        return (
            damping * (image + (lost_sum / page_total)[None, :, None] * tele)
            + (1.0 - damping) * tele
        )

    tele_sums = jnp.sum(tele, axis=2)

    relaxed_one = relaxation(tele)
    relaxed_two = relaxation(relaxed_one)

    gathered, _ = spread_columns(relaxed_two, jnp.zeros((vectors,), jnp.float32))
    entries = tile_pass(
        "entries", gathered, tiles, own_rows, kernel_cols, live_mask, block_count,
        row_blocks, vectors,
    ).T
    block_sums = jnp.sum(relaxed_two, axis=2)
    row_agg = agg_of_block[row_global]
    col_agg = agg_of_block[col_global]
    fields = [
        entries.reshape(-1),
        row_agg.astype(jnp.float32),
        col_agg.astype(jnp.float32),
        block_sums.reshape(-1),
        tele_sums.reshape(-1),
        piece_agg.astype(jnp.float32),
        piece_dangling,
    ]
    sizes = [f.shape[0] for f in fields]
    shared = jnp.concatenate(fields)[None]
    if exchange and src_count % 2 == 0:
        shared = jnp.concatenate(
            [shared]
            + [
                lax.ppermute(shared, "dst", [(i, i ^ v) for i in range(dst_count)])
                for v in range(1, dst_count)
            ],
            axis=0,
        )
        shared = jnp.concatenate(
            [shared, lax.ppermute(shared, "src", [(i, i ^ 1) for i in range(src_count)])], axis=0
        )
        half = src_count // 2
        pieces = [shared]
        for shift in range(1, half):
            pairs = [(i, ((i // 2 + shift) % half) * 2 + i % 2) for i in range(src_count)]
            pieces.append(lax.ppermute(shared, "src", pairs))
        shared = jnp.concatenate(pieces, axis=0)
    else:
        shared = lax.all_gather(shared[0], all_axes, axis=0, tiled=False)
    offsets = [0]
    for size in sizes:
        offsets.append(offsets[-1] + size)
    every = [shared[:, offsets[i]:offsets[i + 1]] for i in range(len(sizes))]
    all_entries = every[0].reshape(-1, vectors)
    all_row_hot = every[1].reshape(-1)[:, None] == agg_range[None, :].astype(jnp.float32)
    all_col_hot = every[2].reshape(-1)[:, None] == agg_range[None, :].astype(jnp.float32)
    all_row_hot = all_row_hot.astype(jnp.bfloat16)
    all_col_hot = all_col_hot.astype(jnp.bfloat16)
    all_block_sums = every[3].reshape(-1, vectors)
    all_tele_sums = every[4].reshape(-1, vectors)
    all_block_hot = (every[5].reshape(-1)[:, None] == agg_range[None, :].astype(jnp.float32))
    all_block_hot = all_block_hot.astype(jnp.float32)
    all_dangling = every[6].reshape(-1)
    totals = jnp.einsum("bk,ba->ka", all_block_sums, all_block_hot, precision=highest)
    lost_mass = jnp.einsum(
        "bk,ba->ka", all_block_sums * all_dangling[:, None], all_block_hot, precision=highest
    )
    weight = jnp.einsum("bk,ba->ka", all_tele_sums, all_block_hot, precision=highest)
    inflow_one = select_dot("tk,ta->ka", all_entries, all_row_hot)

    def coarse_sweep(inflow, ratios):
        carried = jnp.sum(lost_mass * ratios, axis=1)
        return (
            damping * (inflow + (carried / page_total)[:, None] * weight)
            + (1.0 - damping) * weight
        )

    level_one = coarse_sweep(inflow_one, jnp.ones((vectors, agg_count), jnp.float32))
    ratios_one = level_one / totals
    ratio_at_tile = select_dot("ka,ta->tk", ratios_one, all_col_hot)
    inflow_two = select_dot("tk,ta->ka", all_entries * ratio_at_tile, all_row_hot)
    level_two = coarse_sweep(inflow_two, ratios_one)
    ratios_two = level_two / totals
    groups = gathered.shape[0]
    group_ids = jnp.arange(groups, dtype=jnp.int32)
    if exchange:
        group_ids = group_ids ^ dst_index
    block_ids = (
        group_ids[:, None] * row_blocks
        + src_index * blocks_piece
        + jnp.arange(blocks_piece, dtype=jnp.int32)[None, :]
    )
    block_scale = jnp.take(ratios_two, agg_of_block[block_ids.reshape(-1)], axis=1)
    block_scale = block_scale.T.reshape(groups, payload_rows, 1)
    block_scale = jnp.concatenate(
        [block_scale, jnp.zeros((groups, pad_rows, 1), jnp.float32)], axis=1
    )
    corrected_cols = gathered * block_scale
    lost_two = jnp.sum(lost_mass * ratios_two, axis=1)

    position = lax.axis_index(all_axes)
    owned_count = agg_count // (src_count * dst_count)
    owned = lax.dynamic_slice_in_dim(owner_list, position * owned_count, owned_count)
    owned_hot = (owned[:, None] == agg_range[None, :]).astype(jnp.float32)
    coarse_out = jnp.einsum("ka,qa->kq", level_two, owned_hot, precision=highest)

    relaxed_three = relaxation(None, lost_two, corrected_cols)
    relaxed_four = relaxation(relaxed_three)
    fine_out = jnp.transpose(relaxed_four, (1, 0, 2)).reshape(teleport.shape)
    return fine_out, coarse_out


def solution(mesh):
    placed = (
        P(None, "dst", "src"),
        P("dst", "src", None, None, None),
        P("dst", "src", None),
        P("dst", "src", None),
        P("dst", "src"),
        P(),
        P(),
        P(),
    )
    return jax.shard_map(
        per_device,
        mesh=mesh,
        in_specs=placed,
        out_specs=(P(None, "dst", "src"), P(None, ("src", "dst"))),
        check_vma=False,
    )
```
